32 devices in a mesh: view: 4 (over y, x), tile: 8 (over z, core).
Axes of the slice: x: 2, y: 2, z: 4, core: 2. Of those that a mesh axis runs over, the one named last changes fastest.
Arguments:
- initial_estimate: float32 [4, 256, 2048], P('view', 'tile'), may hold values from 0.5 to 1.5
- raw_views: bfloat16 [4, 4, 256, 2048], P('view', None, 'tile'), may hold values from 1 to 3
- route_tile: int32 [4, 512, 1], replicated, may hold values from 0 to 7; in each aligned block of 64 rows (0 to 63, 64 to 127, ..., all dimensions but the last counted through in order) at most 16 rows name the same one
- route_block: int32 [4, 512], replicated, may hold values from 0 to 63
- interp: bfloat16 [4, 128, 128], replicated, may hold values from 0 to 1, as said below
- row_kernel: float32 [4, 4, 17], replicated, may hold values from 0.05 to 1
- col_kernel: float32 [4, 4, 17], replicated, may hold values from 0.05 to 1
- psf_band: int32 [4], replicated, may hold values from 0 to 3
- background: float32 [4], replicated, may hold values from 0.2 to 1
Outputs:
- final_estimate: float32 [4, 256, 2048], P('view', 'tile')
The draws below stay inside these ranges and needn't reach their ends.
Inputs may be any that keep to these rules, and one draw needn't show every extreme that they name: `route_tile`: entry [v, t * 64 + b, 0] is the tile on which block b of tile t lands in view v; in each view the 64 blocks of one tile name any one tile at most 16 times. `route_block`: entry [v, t * 64 + b] is the block of the receiving tile on which that block lands; several may land on one block and some blocks receive none. `interp`: entries are positive.
All inputs are finite; a program needn't handle non-finite values.
Results may differ from the reference program's by a relative error of at most 0.0091.
Values may be sent and summed in bfloat16 or wider, within the bound.
No kernel may reach another device: no remote copies, remote signals or barrier semaphores. Data moves between devices by JAX's collectives and lax.ppermute only.
A program may use at most 64 MiB of HBM per device.

```python
import math
import jax
import jax.numpy as jnp
import numpy as np
from jax import lax

W = 2048
TR = 32
PL = 1
BR = 8
BW = 128
TAPS = 17
BANDS = 4
VIEWS = 4
TILES = 8
PLANES = 4
ROWS = 256
BLK = 64
TILE_BLOCKS = 512
CAP = 16
RADIUS = 8
N_TILE = 8


def draw_interp(key, part):
    spread_values = jax.random.uniform(key, (VIEWS, BW, BW), jnp.float32, 0.0, 2.0)
    diagonal_mask = (jnp.arange(BW)[:, None] == jnp.arange(BW)[None, :]).astype(jnp.float32)
    return (0.5 * diagonal_mask[None, :, :] + 0.5 / BW * spread_values).astype(jnp.bfloat16)


def with_ends(values, key, smallest, high):
    longest = values.shape.index(max(values.shape))
    spots = []
    for shift in (0, 1):
        where = [jax.random.randint(jax.random.fold_in(key, axis), (), 0, length) for axis, length in enumerate(values.shape)]
        where[longest] = (where[longest] + shift) % values.shape[longest]
        spots.append(tuple(where))
    return values.at[spots[0]].set(smallest).at[spots[1]].set(high)


def block_scale(key, dims, cuts, least, largest):
    gain = 1.0
    for position, shards_of in cuts:
        heights = jax.random.uniform(jax.random.fold_in(jax.random.fold_in(key, 6), position), (shards_of,), jnp.float32, least / len(cuts), largest / len(cuts))
        gain = gain * jnp.repeat(jnp.exp(heights), dims[position] // shards_of).reshape((-1,) + (1,) * (len(dims) - 1 - position))
    return gain


def routed_block(rng, own, number, rows, amount, top, reach, skew):
    order = jax.random.permutation(rng, amount)
    crowded, usual = load_shares(amount, rows * top, reach, skew, True), load_shares(amount, rows * top, reach, skew, False)
    places = jnp.arange(amount)

    def named(lengths, rotation):
        used = int((lengths > 0).sum())
        fixed = max(1, used // 4)
        passed = fixed + (places - fixed + rotation * (used - fixed)) % max(1, amount - fixed)
        return jnp.zeros((amount,), jnp.int32).at[order[jnp.where(places < fixed, places, passed)]].set(jnp.asarray(lengths, jnp.int32))

    lengths = jnp.where(number % 4 == 0, named(crowded, number // 4), named(usual, number - number // 4 - 1))
    mixed = jax.random.permutation(jax.random.fold_in(own, 3), amount)
    source_of, receiver = mixed[0:amount // 2 * 2:2], mixed[1:amount // 2 * 2:2]
    slack = jnp.minimum(lengths[source_of] - 1, reach - lengths[receiver]) // 2
    slack = jnp.where((source_of == order[0]) | (receiver == order[0]) | (lengths[receiver] == 0), 0, jnp.maximum(slack, 0))
    passed = jax.random.randint(jax.random.fold_in(own, 4), (amount // 2,), 0, 1 << 20) % (slack + 1)
    lengths = lengths.at[source_of].add(-passed).at[receiver].add(passed)
    labels = jnp.searchsorted(jnp.cumsum(lengths), jnp.arange(rows * top), side="right").astype(jnp.int32)
    grid = labels.reshape(top, rows).T
    grid = grid[jax.random.permutation(jax.random.fold_in(own, 1), rows)]
    rotation = jax.random.randint(jax.random.fold_in(own, 2), (rows, 1), 0, top)
    return jnp.take_along_axis(grid, (jnp.arange(top)[None, :] + rotation) % top, axis=1)


def load_shares(count, total, reach, lean, full):
    portions = [(1 << 20) // math.isqrt(rank ** lean) + 1 for rank in range(1, count + 1)]
    largest = reach if full else min(reach, max(-(-total // count), total * portions[0] // sum(portions)))
    least = 1 if total - largest >= count - 1 else 0
    counts, rest = [largest] + [least] * (count - 1), total - largest - least * (count - 1)
    while rest > 0:
        free = [i for i in range(1, count) if counts[i] < largest] or [i for i in range(1, count) if counts[i] < reach]
        whole, left = sum([portions[i] for i in free]), rest
        for i in free:
            addition = min(reach - counts[i], max(1, left * portions[i] // whole), rest)
            counts[i] = counts[i] + addition
            rest = rest - addition
    return np.array(counts)


def setup_inputs(seed: int = 0) -> dict:
    splits = jax.random.split(jax.random.key(seed), 10)
    initial_estimate = jnp.clip(0.5 + 1.0 * jax.random.uniform(splits[0], (PLANES, ROWS, W), jnp.float32) ** block_scale(splits[0], (PLANES, ROWS, W), ((0, 4), (1, 8)), -0.2, 0.2), 0.5, 1.5)
    raw_views = jnp.clip(1.0 + 2.0 * jax.random.uniform(splits[1], (VIEWS, PLANES, ROWS, W), jnp.float32) ** block_scale(splits[1], (VIEWS, PLANES, ROWS, W), ((0, 4), (2, 8)), -0.2, 0.2), 1.0, 3.0).astype(jnp.bfloat16)
    route_tile_keys = jax.random.split(jax.random.fold_in(splits[2], 1), VIEWS * TILE_BLOCKS // BLK)
    route_tile_turns = jax.random.permutation(jax.random.fold_in(splits[2], 3), VIEWS * TILE_BLOCKS // BLK)
    route_tile = jax.vmap(lambda own, number: routed_block(jax.random.fold_in(splits[2], 2), own, number, BLK, TILES, 1, CAP, 2))(route_tile_keys, route_tile_turns).reshape((VIEWS, TILE_BLOCKS, 1))
    route_block = with_ends(jax.random.randint(splits[3], (VIEWS, TILE_BLOCKS), 0, BLK), jax.random.fold_in(splits[3], 1), 0, BLK - 1).astype(jnp.int32)
    interp = draw_interp(jax.random.fold_in(splits[9], 71), 0)
    row_kernel = jnp.clip(jnp.exp(jax.random.uniform(splits[5], (VIEWS, BANDS, TAPS), jnp.float32, math.log(0.05), math.log(1.0))), 0.05, 1.0)
    col_kernel = jnp.clip(jnp.exp(jax.random.uniform(splits[6], (VIEWS, BANDS, TAPS), jnp.float32, math.log(0.05), math.log(1.0))), 0.05, 1.0)
    psf_band = with_ends(jax.random.randint(splits[7], (PLANES,), 0, BANDS), jax.random.fold_in(splits[7], 1), 0, BANDS - 1).astype(jnp.int32)
    background = jnp.clip(jnp.exp(jax.random.uniform(splits[8], (VIEWS,), jnp.float32, math.log(0.2), math.log(1.0))), 0.2, 1.0)
    return {"initial_estimate": initial_estimate, "raw_views": raw_views, "route_tile": route_tile, "route_block": route_block, "interp": interp, "row_kernel": row_kernel, "col_kernel": col_kernel, "psf_band": psf_band, "background": background}


HIGHEST = lax.Precision.HIGHEST


def plane_blocks(values_in):
    shaped = values_in.reshape(N_TILE, TR // BR, BR, W // BW, BW)
    return shaped.transpose(0, 1, 3, 2, 4).reshape(TILE_BLOCKS, BR, BW)


def plane_whole(pieces):
    shaped = pieces.reshape(N_TILE, TR // BR, W // BW, BR, BW)
    return shaped.transpose(0, 1, 3, 2, 4).reshape(ROWS, W)


def column_blur(values_in, taps_in, flipped):
    padded = jnp.pad(values_in.astype(jnp.float32), ((0, 0), (RADIUS, RADIUS)))
    result_sum = jnp.zeros(values_in.shape, jnp.float32)
    for tap_index in range(TAPS):
        start_col = 2 * RADIUS - tap_index if flipped else tap_index
        result_sum = result_sum + taps_in[tap_index].astype(jnp.float32) * padded[:, start_col:start_col + W]
    return result_sum


def row_blur(values_in, taps_in, flipped):
    padded = jnp.pad(values_in.astype(jnp.float32), ((RADIUS, RADIUS), (0, 0)))
    result_sum = jnp.zeros(values_in.shape, jnp.float32)
    for tap_index in range(TAPS):
        start_row = 2 * RADIUS - tap_index if flipped else tap_index
        result_sum = result_sum + taps_in[tap_index].astype(jnp.float32) * padded[start_row:start_row + ROWS, :]
    return result_sum


def update_plane(estimate_plane, raw_plane, matrix, dest_tile, dest_block, row_taps, col_taps, level):
    landing = dest_tile * BLK + dest_block
    matrix_wide = matrix.astype(jnp.float32)
    rounded_estimate = estimate_plane.astype(jnp.bfloat16)
    moved = jnp.einsum('nrj,jk->nrk', plane_blocks(rounded_estimate).astype(jnp.float32), matrix_wide, precision=HIGHEST).astype(jnp.bfloat16)
    summed = jax.ops.segment_sum(moved.astype(jnp.float32), landing, num_segments=TILE_BLOCKS)
    land_count = jax.ops.segment_sum(jnp.ones(landing.shape, jnp.float32), landing, num_segments=TILE_BLOCKS)
    joined_field = plane_whole(summed / jnp.maximum(land_count, 1.0)[:, None, None]).astype(jnp.bfloat16)
    across = column_blur(joined_field, col_taps, False).astype(jnp.bfloat16)
    blurred = row_blur(across, row_taps, False) + level
    ratio_field = (raw_plane.astype(jnp.float32) / blurred).astype(jnp.bfloat16)
    rows_back = row_blur(ratio_field, row_taps, True).astype(jnp.bfloat16)
    spread = column_blur(rows_back, col_taps, True).astype(jnp.bfloat16)
    returned = jnp.einsum('nrj,kj->nrk', plane_blocks(spread).astype(jnp.float32), matrix_wide, precision=HIGHEST).astype(jnp.bfloat16)
    return estimate_plane * plane_whole(returned[landing].astype(jnp.float32))


def reference(initial_estimate, raw_views, route_tile, route_block, interp, row_kernel, col_kernel, psf_band, background):
    row_psf = (row_kernel / jnp.sum(row_kernel, axis=2, keepdims=True)).astype(jnp.bfloat16)
    col_psf = (col_kernel / jnp.sum(col_kernel, axis=2, keepdims=True)).astype(jnp.bfloat16)
    estimate = initial_estimate
    planes_all = jnp.arange(PLANES, dtype=jnp.int32)
    for update_index in range(VIEWS):
        plane_view = ((planes_all // PL) + update_index) % VIEWS
        estimate = jax.vmap(update_plane)(
            estimate,
            raw_views[plane_view, planes_all],
            interp[plane_view],
            route_tile[plane_view, :, 0],
            route_block[plane_view],
            row_psf[plane_view, psf_band],
            col_psf[plane_view, psf_band],
            background[plane_view])
    return estimate
```

```python
import jax
import jax.numpy as jnp
from jax import lax
from jax.sharding import PartitionSpec as P

BR = 8
BW = 128
TAPS = 17


def passed_along(x, axis, by):
    count = lax.axis_size(axis)
    return lax.ppermute(x, axis, [(i, (i + by) % count) for i in range(count)])


def to_blocks(values_in):
    rows, plane_width = values_in.shape
    shaped = values_in.reshape(rows // BR, BR, plane_width // BW, BW)
    return shaped.transpose(0, 2, 1, 3).reshape(-1, BR * BW)


def from_blocks(pieces, rows, plane_width):
    shaped = pieces.reshape(rows // BR, plane_width // BW, BR, BW)
    return shaped.transpose(0, 2, 1, 3).reshape(rows, plane_width)


def banded(taps_in, diff):
    result = jnp.zeros(diff.shape, jnp.float32)
    for tap_index in range(TAPS):
        result = result + jnp.where(diff == tap_index, taps_in[tap_index].astype(jnp.float32), 0.0)
    return result.astype(jnp.bfloat16)


def column_mats(taps_in, flipped):
    radius = (TAPS - 1) // 2
    source_lane = jnp.arange(BW, dtype=jnp.int32)[:, None]
    target_lane = jnp.arange(BW, dtype=jnp.int32)[None, :]
    mats = []
    for offset in (-1, 0, 1):
        if flipped:
            diff = target_lane - source_lane - offset * BW + radius
        else:
            diff = source_lane + offset * BW - target_lane + radius
        mats.append(banded(taps_in, diff))
    return mats


def row_mat(taps_in, rows):
    radius = (TAPS - 1) // 2
    out_row = jnp.arange(rows, dtype=jnp.int32)[:, None]
    src_row = jnp.arange(rows, dtype=jnp.int32)[None, :]
    return banded(taps_in, src_row - out_row + radius)


def column_pass(values_in, mats):
    rows, plane_width = values_in.shape
    col_count = plane_width // BW
    grid_cells = values_in.reshape(rows, col_count, BW)
    padded = jnp.pad(grid_cells, ((0, 0), (1, 1), (0, 0)))
    result_sum = jnp.zeros(grid_cells.shape, jnp.float32)
    for position in range(3):
        result_sum = result_sum + jnp.einsum(
            "rcj,jk->rck",
            padded[:, position : position + col_count],
            mats[position],
            preferred_element_type=jnp.float32,
        )
    return result_sum.reshape(rows, plane_width)


def update_plane(estimate, raw_plane, matrix, landing, row_taps, col_taps, level):
    rows, plane_width = estimate.shape
    blocks = (rows // BR) * (plane_width // BW)
    block_iota = jnp.arange(blocks, dtype=jnp.int32)
    rounded = estimate.astype(jnp.bfloat16).reshape(rows, plane_width // BW, BW)
    moved = jnp.einsum("rcj,jk->rck", rounded, matrix, preferred_element_type=jnp.float32)
    moved = moved.astype(jnp.bfloat16).reshape(rows, plane_width)
    gather_mat = landing[None, :] == block_iota[:, None]
    land_count = jnp.sum(gather_mat.astype(jnp.float32), axis=1)
    summed = jnp.dot(
        gather_mat.astype(jnp.bfloat16), to_blocks(moved), preferred_element_type=jnp.float32
    )
    summed = (summed / jnp.maximum(land_count, 1.0)[:, None]).astype(jnp.bfloat16)
    joined = from_blocks(summed, rows, plane_width)
    across = column_pass(joined, column_mats(col_taps, False)).astype(jnp.bfloat16)
    band = row_mat(row_taps, rows)
    blurred = jnp.dot(band, across, preferred_element_type=jnp.float32) + level
    ratio = (raw_plane.astype(jnp.float32) / blurred).astype(jnp.bfloat16)
    rows_back = jnp.dot(band.T, ratio, preferred_element_type=jnp.float32).astype(jnp.bfloat16)
    spread = column_pass(rows_back, column_mats(col_taps, True)).astype(jnp.bfloat16)
    returned = jnp.einsum(
        "rcj,kj->rck",
        spread.reshape(rows, plane_width // BW, BW),
        matrix,
        preferred_element_type=jnp.float32,
    ).astype(jnp.bfloat16)
    correction = jnp.take(to_blocks(returned.reshape(rows, plane_width)), landing, axis=0)
    return estimate * from_blocks(correction, rows, plane_width).astype(jnp.float32)


def with_halo(cells, sides, width):
    for axis, dim in sides:
        count = lax.axis_size(axis)
        ends = count - 1
        head = lax.slice_in_dim(cells, 0, width, axis=dim)
        tail = lax.slice_in_dim(cells, cells.shape[dim] - width, cells.shape[dim], axis=dim)
        cells = jnp.concatenate(
            [
                lax.ppermute(tail, axis, [(i, (i + 1) % count) for i in range(ends)]),
                cells,
                lax.ppermute(head, axis, [((i + 1) % count, i) for i in range(ends)]),
            ],
            axis=dim,
        )
    return cells


def sharded_to_blocks(values_in):
    planes, tile_rows, plane_width = values_in.shape
    shaped = values_in.reshape(planes, tile_rows // BR, BR, plane_width // BW, BW)
    return shaped.transpose(1, 3, 0, 2, 4).reshape(-1, planes, BR, BW)


def sharded_from_blocks(pieces, tile_rows, plane_width):
    planes = pieces.shape[1]
    shaped = pieces.reshape(tile_rows // BR, plane_width // BW, planes, BR, BW)
    return shaped.transpose(2, 0, 3, 1, 4).reshape(planes, tile_rows, plane_width)


def sharded_column_pass(values_in, taps_in, flipped):
    planes, tile_rows, plane_width = values_in.shape
    radius = (taps_in.shape[1] - 1) // 2
    lane_iota = jnp.arange(BW, dtype=jnp.int32)
    source_lane = lane_iota[:, None]
    target_lane = lane_iota[None, :]
    zero_bf = jnp.zeros((), jnp.bfloat16)
    band_mats = []
    for offset in (-1, 0, 1):
        if flipped:
            tap_index = target_lane - source_lane - offset * BW + radius
        else:
            tap_index = source_lane + offset * BW - target_lane + radius
        inside = (tap_index >= 0) & (tap_index <= 2 * radius)
        picked = taps_in[:, jnp.clip(tap_index, 0, 2 * radius)]
        band_mats.append(jnp.where(inside[None, :, :], picked, zero_bf))
    col_count = plane_width // BW
    grid_cells = values_in.reshape(planes, tile_rows, col_count, BW)
    padded = jnp.pad(grid_cells, ((0, 0), (0, 0), (1, 1), (0, 0)))
    result_sum = jnp.zeros(grid_cells.shape, jnp.float32)
    for position in range(3):
        result_sum = result_sum + jnp.einsum(
            "prcj,pjk->prck",
            padded[:, :, position : position + col_count],
            band_mats[position],
            preferred_element_type=jnp.float32,
        )
    return result_sum.reshape(planes, tile_rows, plane_width)


def row_pass(padded, taps_in, flipped):
    planes, extended, plane_width = padded.shape
    radius = (taps_in.shape[1] - 1) // 2
    tile_rows = extended - 2 * radius
    row_iota = jnp.arange(tile_rows, dtype=jnp.int32)[:, None]
    src_iota = jnp.arange(extended, dtype=jnp.int32)[None, :]
    if flipped:
        tap_index = row_iota + 2 * radius - src_iota
    else:
        tap_index = src_iota - row_iota
    inside = (tap_index >= 0) & (tap_index <= 2 * radius)
    band_rows = jnp.where(
        inside[None, :, :],
        taps_in[:, jnp.clip(tap_index, 0, 2 * radius)],
        jnp.zeros((), jnp.bfloat16),
    )
    return jnp.einsum("prs,psw->prw", band_rows, padded, preferred_element_type=jnp.float32)


def sharded_update(
    estimate,
    raw_piece,
    view_index,
    slab_index,
    route_tile,
    route_block,
    interp,
    row_psf,
    col_psf,
    psf_band,
    background,
):
    tile_count = lax.axis_size("tile")
    my_tile = lax.axis_index("tile")
    planes, tile_rows, plane_width = estimate.shape
    blocks = tile_rows // BR * (plane_width // BW)
    capacity = max(2, 2 * blocks // tile_count)
    radius = (TAPS - 1) // 2
    matrix = interp[view_index]
    dest_tile = route_tile[view_index, :, 0].reshape(tile_count, blocks)
    dest_block = route_block[view_index].reshape(tile_count, blocks)
    tiles_iota = jnp.arange(tile_count, dtype=jnp.int32)
    one_hot = (dest_tile[:, :, None] == tiles_iota[None, None, :]).astype(jnp.int32)
    slot_rank = jnp.sum((jnp.cumsum(one_hot, axis=1) - one_hot) * one_hot, axis=2)
    slot_index = dest_tile * capacity + slot_rank
    my_slots = slot_index[my_tile]
    slots_iota = jnp.arange(tile_count * capacity, dtype=jnp.int32)
    block_iota = jnp.arange(blocks, dtype=jnp.int32)
    match_send = my_slots[None, :] == slots_iota[:, None]
    send_ok = jnp.any(match_send, axis=1)
    send_src = jnp.sum(jnp.where(match_send, block_iota[None, :], 0), axis=1)
    match_recv = (dest_tile == my_tile)[:, None, :] & (
        slot_rank[:, None, :] == jnp.arange(capacity, dtype=jnp.int32)[None, :, None]
    )
    recv_ok = jnp.any(match_recv, axis=2).reshape(-1)
    recv_off = jnp.sum(jnp.where(match_recv, dest_block[:, None, :], 0), axis=2).reshape(-1)
    zero_bf = jnp.zeros((), jnp.bfloat16)
    rounded_estimate = estimate.astype(jnp.bfloat16)
    interpolated = jnp.einsum(
        "bprj,jk->bprk", sharded_to_blocks(rounded_estimate), matrix, preferred_element_type=jnp.float32
    ).astype(jnp.bfloat16)
    outgoing = jnp.where(send_ok[:, None, None, None], interpolated[send_src], zero_bf)
    outgoing = outgoing.reshape(tile_count, capacity, planes, BR, BW)
    incoming = lax.all_to_all(outgoing, "tile", split_axis=0, concat_axis=0, tiled=True)
    incoming = incoming.reshape(tile_count * capacity, planes * BR * BW)
    landing = (recv_off[None, :] == block_iota[:, None]) & recv_ok[None, :]
    land_count = jnp.sum(landing.astype(jnp.float32), axis=1)
    summed = jnp.dot(landing.astype(jnp.bfloat16), incoming, preferred_element_type=jnp.float32)
    summed = (summed / jnp.maximum(land_count, 1.0)[:, None]).astype(jnp.bfloat16)
    joined_field = sharded_from_blocks(summed.reshape(blocks, planes, BR, BW), tile_rows, plane_width)
    plane_bands = lax.dynamic_slice_in_dim(psf_band, slab_index * planes, planes, 0)
    row_taps = row_psf[view_index][plane_bands]
    col_taps = col_psf[view_index][plane_bands]
    across = sharded_column_pass(joined_field, col_taps, False).astype(jnp.bfloat16)
    padded = with_halo(across, (("tile", 1),), radius)
    blurred = row_pass(padded, row_taps, False) + background[view_index]
    ratio_field = (raw_piece.astype(jnp.float32) / blurred).astype(jnp.bfloat16)
    padded_ratio = with_halo(ratio_field, (("tile", 1),), radius)
    rows_back = row_pass(padded_ratio, row_taps, True).astype(jnp.bfloat16)
    spread = sharded_column_pass(rows_back, col_taps, True).astype(jnp.bfloat16)
    returned_blocks = jnp.einsum(
        "bprj,kj->bprk", sharded_to_blocks(spread), matrix, preferred_element_type=jnp.float32
    ).astype(jnp.bfloat16)
    returning = jnp.where(recv_ok[:, None, None, None], returned_blocks[recv_off], zero_bf)
    returning = returning.reshape(tile_count, capacity, planes, BR, BW)
    arrived = lax.all_to_all(returning, "tile", split_axis=0, concat_axis=0, tiled=True)
    arrived = arrived.reshape(tile_count * capacity, planes, BR, BW)
    correction = arrived[my_slots]
    return estimate * sharded_from_blocks(correction.astype(jnp.float32), tile_rows, plane_width)


def local(
    initial_estimate,
    raw_views,
    route_tile,
    route_block,
    interp,
    row_kernel,
    col_kernel,
    psf_band,
    background,
):
    view_count = lax.axis_size("view")
    my_group = lax.axis_index("view")
    my_tile = lax.axis_index("tile")
    planes, tile_rows, plane_width = initial_estimate.shape
    tile_blocks = (tile_rows // BR) * (plane_width // BW)
    row_psf = (row_kernel / jnp.sum(row_kernel, axis=2, keepdims=True)).astype(jnp.bfloat16)
    col_psf = (col_kernel / jnp.sum(col_kernel, axis=2, keepdims=True)).astype(jnp.bfloat16)
    if view_count * tile_rows * plane_width * lax.axis_size("tile") > (1 << 22):
        estimate = initial_estimate
        for update_index in range(view_count):
            view_index = (my_group + update_index) % view_count
            own_piece = lax.dynamic_slice_in_dim(
                raw_views[0], (my_group - update_index) % view_count * planes, planes, 0
            )
            raw_piece = (
                own_piece if update_index == 0 else passed_along(own_piece, "view", -update_index)
            )
            estimate = sharded_update(
                estimate, raw_piece, view_index, my_group, route_tile, route_block,
                interp, row_psf, col_psf, psf_band, background,
            )
        return estimate
    pieces = []
    for update_index in range(view_count):
        own_piece = lax.dynamic_slice_in_dim(
            raw_views[0], (my_group - update_index) % view_count * planes, planes, 0
        )
        piece = own_piece if update_index == 0 else passed_along(own_piece, "view", -update_index)
        pieces.append(lax.all_gather(piece, "tile", axis=1, tiled=True))
    estimate = lax.all_gather(initial_estimate, "tile", axis=1, tiled=True)
    plane_bands = lax.dynamic_slice_in_dim(psf_band, my_group * planes, planes, 0)
    for update_index in range(view_count):
        view_index = (my_group + update_index) % view_count
        matrix = interp[view_index]
        landing = route_tile[view_index, :, 0] * tile_blocks + route_block[view_index]
        row_taps = row_psf[view_index][plane_bands]
        col_taps = col_psf[view_index][plane_bands]
        level = background[view_index]
        estimate = jnp.stack(
            [
                update_plane(
                    estimate[p],
                    pieces[update_index][p],
                    matrix,
                    landing,
                    row_taps[p],
                    col_taps[p],
                    level,
                )
                for p in range(planes)
            ]
        )
    return lax.dynamic_slice_in_dim(estimate, my_tile * tile_rows, tile_rows, 1)


def solution(mesh):
    return jax.shard_map(
        local,
        mesh=mesh,
        in_specs=(
            P("view", "tile", None),
            P("view", None, "tile", None),
            P(),
            P(),
            P(),
            P(),
            P(),
            P(),
            P(),
        ),
        out_specs=P("view", "tile", None),
        check_vma=False,
    )
```

```python
import jax
import jax.numpy as jnp
from jax import lax
from jax.sharding import PartitionSpec as P
from jax.experimental import pallas as pl
from jax.experimental.pallas import tpu as pltpu

BR = 8
BW = 128
TAPS = 17


def passed_along(x, axis, by):
    count = lax.axis_size(axis)
    return lax.ppermute(x, axis, [(i, (i + by) % count) for i in range(count)])


def to_blocks(values_in):
    rows, plane_width = values_in.shape
    shaped = values_in.reshape(rows // BR, BR, plane_width // BW, BW)
    return shaped.transpose(0, 2, 1, 3).reshape(-1, BR * BW)


def from_blocks(pieces, rows, plane_width):
    shaped = pieces.reshape(rows // BR, plane_width // BW, BR, BW)
    return shaped.transpose(0, 2, 1, 3).reshape(rows, plane_width)


def banded(taps_in, diff):
    result = jnp.zeros(diff.shape, jnp.float32)
    for tap_index in range(TAPS):
        result = result + jnp.where(diff == tap_index, taps_in[tap_index].astype(jnp.float32), 0.0)
    return result.astype(jnp.bfloat16)


def column_mats(taps_in, flipped):
    radius = (TAPS - 1) // 2
    source_lane = jnp.arange(BW, dtype=jnp.int32)[:, None]
    target_lane = jnp.arange(BW, dtype=jnp.int32)[None, :]
    mats = []
    for offset in (-1, 0, 1):
        if flipped:
            diff = target_lane - source_lane - offset * BW + radius
        else:
            diff = source_lane + offset * BW - target_lane + radius
        mats.append(banded(taps_in, diff))
    return mats


def row_mat(taps_in, rows):
    radius = (TAPS - 1) // 2
    out_row = jnp.arange(rows, dtype=jnp.int32)[:, None]
    src_row = jnp.arange(rows, dtype=jnp.int32)[None, :]
    return banded(taps_in, src_row - out_row + radius)


def column_pass(values_in, mats):
    rows, plane_width = values_in.shape
    col_count = plane_width // BW
    grid_cells = values_in.reshape(rows, col_count, BW)
    padded = jnp.pad(grid_cells, ((0, 0), (1, 1), (0, 0)))
    result_sum = jnp.zeros(grid_cells.shape, jnp.float32)
    for position in range(3):
        result_sum = result_sum + jnp.einsum(
            "rcj,jk->rck",
            padded[:, position : position + col_count],
            mats[position],
            preferred_element_type=jnp.float32,
        )
    return result_sum.reshape(rows, plane_width)


def update_plane(estimate, raw_plane, matrix, landing, row_taps, col_taps, level):
    rows, plane_width = estimate.shape
    blocks = (rows // BR) * (plane_width // BW)
    block_iota = jnp.arange(blocks, dtype=jnp.int32)
    rounded = estimate.astype(jnp.bfloat16).reshape(rows, plane_width // BW, BW)
    moved = jnp.einsum("rcj,jk->rck", rounded, matrix, preferred_element_type=jnp.float32)
    moved = moved.astype(jnp.bfloat16).reshape(rows, plane_width)
    gather_mat = landing[None, :] == block_iota[:, None]
    land_count = jnp.sum(gather_mat.astype(jnp.float32), axis=1)
    summed = jnp.dot(
        gather_mat.astype(jnp.bfloat16), to_blocks(moved), preferred_element_type=jnp.float32
    )
    summed = (summed / jnp.maximum(land_count, 1.0)[:, None]).astype(jnp.bfloat16)
    joined = from_blocks(summed, rows, plane_width)
    across = column_pass(joined, column_mats(col_taps, False)).astype(jnp.bfloat16)
    band = row_mat(row_taps, rows)
    blurred = jnp.dot(band, across, preferred_element_type=jnp.float32) + level
    ratio = (raw_plane.astype(jnp.float32) / blurred).astype(jnp.bfloat16)
    rows_back = jnp.dot(band.T, ratio, preferred_element_type=jnp.float32).astype(jnp.bfloat16)
    spread = column_pass(rows_back, column_mats(col_taps, True)).astype(jnp.bfloat16)
    returned = jnp.einsum(
        "rcj,kj->rck",
        spread.reshape(rows, plane_width // BW, BW),
        matrix,
        preferred_element_type=jnp.float32,
    ).astype(jnp.bfloat16)
    correction = jnp.take(to_blocks(returned.reshape(rows, plane_width)), landing, axis=0)
    return estimate * from_blocks(correction, rows, plane_width).astype(jnp.float32)


def plane_kernel(est_ref, raw_ref, m_ref, mt_ref, s_ref, cnt_ref, g_ref, bf_ref, bb_ref, a_ref,
                 at_ref, bg_ref, out_ref, work, joined, across, ratio):
    rows, plane_width = est_ref.shape
    nt = rows // BR
    nc = plane_width // BW
    f32 = jnp.float32
    bf16 = jnp.bfloat16

    def cols(c):
        return slice(c * BW, (c + 1) * BW)

    for c in range(nc):
        blk = est_ref[:, cols(c)].astype(bf16)
        moved = jnp.dot(blk, m_ref[...], preferred_element_type=f32)
        work[c] = moved.astype(bf16).astype(f32)

    def regroup(src, mat_ref, dst, post):
        for r in range(BR):
            stacked = jnp.concatenate(
                [src[c, pl.ds(r, nt, stride=BR), :] for c in range(nc)], axis=0
            )
            result = jnp.dot(mat_ref[...], stacked.astype(bf16), preferred_element_type=f32)
            result = post(result)
            for c in range(nc):
                dst[c, pl.ds(r, nt, stride=BR), :] = result[c * nt:(c + 1) * nt, :]

    regroup(work, s_ref, joined,
            lambda v: (v / cnt_ref[...]).astype(bf16).astype(f32))

    def column_blur(take, mats_ref, c):
        total = None
        for offset in (-1, 0, 1):
            if 0 <= c + offset < nc:
                part = jnp.dot(take(c + offset).astype(bf16), mats_ref[offset + 1],
                               preferred_element_type=f32)
                total = part if total is None else total + part
        return total

    for c in range(nc):
        across[:, cols(c)] = column_blur(lambda i: joined[i], bf_ref, c).astype(bf16)
    level = bg_ref[0]
    for c in range(nc):
        blurred = jnp.dot(a_ref[...], across[:, cols(c)], preferred_element_type=f32) + level
        quotient = (raw_ref[:, cols(c)].astype(f32) / blurred).astype(bf16)
        ratio[:, cols(c)] = jnp.dot(at_ref[...], quotient, preferred_element_type=f32).astype(bf16)
    for c in range(nc):
        spread = column_blur(lambda i: ratio[:, cols(i)], bb_ref, c).astype(bf16)
        back = jnp.dot(spread, mt_ref[...], preferred_element_type=f32)
        work[c] = back.astype(bf16).astype(f32)
    regroup(work, g_ref, joined, lambda v: v)
    for c in range(nc):
        out_ref[:, cols(c)] = est_ref[:, cols(c)] * joined[c]


def kernel_update(estimate, raw_plane, matrix, landing, row_taps, col_taps, level):
    rows, plane_width = estimate.shape
    nt = rows // BR
    nc = plane_width // BW
    blocks = nt * nc
    order = landing.reshape(nt, nc).T.reshape(-1)
    place = (order % nc) * nt + order // nc
    spots = jnp.arange(blocks, dtype=jnp.int32)
    sum_mat = place[None, :] == spots[:, None]
    pick_mat = place[:, None] == spots[None, :]
    count = jnp.sum(sum_mat.astype(jnp.float32), axis=1)
    count = jnp.broadcast_to(jnp.maximum(count, 1.0)[:, None], (blocks, BW))
    band = row_mat(row_taps, rows)
    vmem = pl.BlockSpec(memory_space=pltpu.VMEM)
    return pl.pallas_call(
        plane_kernel,
        out_shape=jax.ShapeDtypeStruct((rows, plane_width), jnp.float32),
        in_specs=[vmem] * 11 + [pl.BlockSpec(memory_space=pltpu.SMEM)],
        out_specs=vmem,
        scratch_shapes=[
            pltpu.VMEM((nc, rows, BW), jnp.float32),
            pltpu.VMEM((nc, rows, BW), jnp.float32),
            pltpu.VMEM((rows, plane_width), jnp.bfloat16),
            pltpu.VMEM((rows, plane_width), jnp.bfloat16),
        ],
        compiler_params=pltpu.CompilerParams(vmem_limit_bytes=48 * 1024 * 1024),
        cost_estimate=pl.CostEstimate(
            flops=2 * rows * plane_width * (4 * BW + 2 * rows + 2 * blocks // BR * BR),
            bytes_accessed=rows * plane_width * 10,
            transcendentals=0,
        ),
    )(
        estimate,
        raw_plane,
        matrix,
        matrix.T,
        sum_mat.astype(jnp.bfloat16),
        count,
        pick_mat.astype(jnp.bfloat16),
        jnp.stack(column_mats(col_taps, False)),
        jnp.stack(column_mats(col_taps, True)),
        band,
        band.T,
        jnp.reshape(level, (1,)).astype(jnp.float32),
    )


def with_halo(cells, sides, width):
    for axis, dim in sides:
        count = lax.axis_size(axis)
        ends = count - 1
        head = lax.slice_in_dim(cells, 0, width, axis=dim)
        tail = lax.slice_in_dim(cells, cells.shape[dim] - width, cells.shape[dim], axis=dim)
        cells = jnp.concatenate(
            [
                lax.ppermute(tail, axis, [(i, (i + 1) % count) for i in range(ends)]),
                cells,
                lax.ppermute(head, axis, [((i + 1) % count, i) for i in range(ends)]),
            ],
            axis=dim,
        )
    return cells


def sharded_to_blocks(values_in):
    planes, tile_rows, plane_width = values_in.shape
    shaped = values_in.reshape(planes, tile_rows // BR, BR, plane_width // BW, BW)
    return shaped.transpose(1, 3, 0, 2, 4).reshape(-1, planes, BR, BW)


def sharded_from_blocks(pieces, tile_rows, plane_width):
    planes = pieces.shape[1]
    shaped = pieces.reshape(tile_rows // BR, plane_width // BW, planes, BR, BW)
    return shaped.transpose(2, 0, 3, 1, 4).reshape(planes, tile_rows, plane_width)


def sharded_column_pass(values_in, taps_in, flipped):
    planes, tile_rows, plane_width = values_in.shape
    radius = (taps_in.shape[1] - 1) // 2
    lane_iota = jnp.arange(BW, dtype=jnp.int32)
    source_lane = lane_iota[:, None]
    target_lane = lane_iota[None, :]
    zero_bf = jnp.zeros((), jnp.bfloat16)
    band_mats = []
    for offset in (-1, 0, 1):
        if flipped:
            tap_index = target_lane - source_lane - offset * BW + radius
        else:
            tap_index = source_lane + offset * BW - target_lane + radius
        inside = (tap_index >= 0) & (tap_index <= 2 * radius)
        picked = taps_in[:, jnp.clip(tap_index, 0, 2 * radius)]
        band_mats.append(jnp.where(inside[None, :, :], picked, zero_bf))
    col_count = plane_width // BW
    grid_cells = values_in.reshape(planes, tile_rows, col_count, BW)
    padded = jnp.pad(grid_cells, ((0, 0), (0, 0), (1, 1), (0, 0)))
    result_sum = jnp.zeros(grid_cells.shape, jnp.float32)
    for position in range(3):
        result_sum = result_sum + jnp.einsum(
            "prcj,pjk->prck",
            padded[:, :, position : position + col_count],
            band_mats[position],
            preferred_element_type=jnp.float32,
        )
    return result_sum.reshape(planes, tile_rows, plane_width)


def row_pass(padded, taps_in, flipped):
    planes, extended, plane_width = padded.shape
    radius = (taps_in.shape[1] - 1) // 2
    tile_rows = extended - 2 * radius
    row_iota = jnp.arange(tile_rows, dtype=jnp.int32)[:, None]
    src_iota = jnp.arange(extended, dtype=jnp.int32)[None, :]
    if flipped:
        tap_index = row_iota + 2 * radius - src_iota
    else:
        tap_index = src_iota - row_iota
    inside = (tap_index >= 0) & (tap_index <= 2 * radius)
    band_rows = jnp.where(
        inside[None, :, :],
        taps_in[:, jnp.clip(tap_index, 0, 2 * radius)],
        jnp.zeros((), jnp.bfloat16),
    )
    return jnp.einsum("prs,psw->prw", band_rows, padded, preferred_element_type=jnp.float32)


def sharded_update(
    estimate,
    raw_piece,
    view_index,
    slab_index,
    route_tile,
    route_block,
    interp,
    row_psf,
    col_psf,
    psf_band,
    background,
):
    tile_count = lax.axis_size("tile")
    my_tile = lax.axis_index("tile")
    planes, tile_rows, plane_width = estimate.shape
    blocks = tile_rows // BR * (plane_width // BW)
    capacity = max(2, 2 * blocks // tile_count)
    radius = (TAPS - 1) // 2
    matrix = interp[view_index]
    dest_tile = route_tile[view_index, :, 0].reshape(tile_count, blocks)
    dest_block = route_block[view_index].reshape(tile_count, blocks)
    tiles_iota = jnp.arange(tile_count, dtype=jnp.int32)
    one_hot = (dest_tile[:, :, None] == tiles_iota[None, None, :]).astype(jnp.int32)
    slot_rank = jnp.sum((jnp.cumsum(one_hot, axis=1) - one_hot) * one_hot, axis=2)
    slot_index = dest_tile * capacity + slot_rank
    my_slots = slot_index[my_tile]
    slots_iota = jnp.arange(tile_count * capacity, dtype=jnp.int32)
    block_iota = jnp.arange(blocks, dtype=jnp.int32)
    match_send = my_slots[None, :] == slots_iota[:, None]
    send_ok = jnp.any(match_send, axis=1)
    send_src = jnp.sum(jnp.where(match_send, block_iota[None, :], 0), axis=1)
    match_recv = (dest_tile == my_tile)[:, None, :] & (
        slot_rank[:, None, :] == jnp.arange(capacity, dtype=jnp.int32)[None, :, None]
    )
    recv_ok = jnp.any(match_recv, axis=2).reshape(-1)
    recv_off = jnp.sum(jnp.where(match_recv, dest_block[:, None, :], 0), axis=2).reshape(-1)
    zero_bf = jnp.zeros((), jnp.bfloat16)
    rounded_estimate = estimate.astype(jnp.bfloat16)
    interpolated = jnp.einsum(
        "bprj,jk->bprk", sharded_to_blocks(rounded_estimate), matrix, preferred_element_type=jnp.float32
    ).astype(jnp.bfloat16)
    outgoing = jnp.where(send_ok[:, None, None, None], interpolated[send_src], zero_bf)
    outgoing = outgoing.reshape(tile_count, capacity, planes, BR, BW)
    incoming = lax.all_to_all(outgoing, "tile", split_axis=0, concat_axis=0, tiled=True)
    incoming = incoming.reshape(tile_count * capacity, planes * BR * BW)
    landing = (recv_off[None, :] == block_iota[:, None]) & recv_ok[None, :]
    land_count = jnp.sum(landing.astype(jnp.float32), axis=1)
    summed = jnp.dot(landing.astype(jnp.bfloat16), incoming, preferred_element_type=jnp.float32)
    summed = (summed / jnp.maximum(land_count, 1.0)[:, None]).astype(jnp.bfloat16)
    joined_field = sharded_from_blocks(summed.reshape(blocks, planes, BR, BW), tile_rows, plane_width)
    plane_bands = lax.dynamic_slice_in_dim(psf_band, slab_index * planes, planes, 0)
    row_taps = row_psf[view_index][plane_bands]
    col_taps = col_psf[view_index][plane_bands]
    across = sharded_column_pass(joined_field, col_taps, False).astype(jnp.bfloat16)
    padded = with_halo(across, (("tile", 1),), radius)
    blurred = row_pass(padded, row_taps, False) + background[view_index]
    ratio_field = (raw_piece.astype(jnp.float32) / blurred).astype(jnp.bfloat16)
    padded_ratio = with_halo(ratio_field, (("tile", 1),), radius)
    rows_back = row_pass(padded_ratio, row_taps, True).astype(jnp.bfloat16)
    spread = sharded_column_pass(rows_back, col_taps, True).astype(jnp.bfloat16)
    returned_blocks = jnp.einsum(
        "bprj,kj->bprk", sharded_to_blocks(spread), matrix, preferred_element_type=jnp.float32
    ).astype(jnp.bfloat16)
    returning = jnp.where(recv_ok[:, None, None, None], returned_blocks[recv_off], zero_bf)
    returning = returning.reshape(tile_count, capacity, planes, BR, BW)
    arrived = lax.all_to_all(returning, "tile", split_axis=0, concat_axis=0, tiled=True)
    arrived = arrived.reshape(tile_count * capacity, planes, BR, BW)
    correction = arrived[my_slots]
    return estimate * sharded_from_blocks(correction.astype(jnp.float32), tile_rows, plane_width)


def local(
    initial_estimate,
    raw_views,
    route_tile,
    route_block,
    interp,
    row_kernel,
    col_kernel,
    psf_band,
    background,
):
    view_count = lax.axis_size("view")
    my_group = lax.axis_index("view")
    my_tile = lax.axis_index("tile")
    planes, tile_rows, plane_width = initial_estimate.shape
    tile_blocks = (tile_rows // BR) * (plane_width // BW)
    row_psf = (row_kernel / jnp.sum(row_kernel, axis=2, keepdims=True)).astype(jnp.bfloat16)
    col_psf = (col_kernel / jnp.sum(col_kernel, axis=2, keepdims=True)).astype(jnp.bfloat16)
    if view_count * tile_rows * plane_width * lax.axis_size("tile") > (1 << 22):
        estimate = initial_estimate
        for update_index in range(view_count):
            view_index = (my_group + update_index) % view_count
            own_piece = lax.dynamic_slice_in_dim(
                raw_views[0], (my_group - update_index) % view_count * planes, planes, 0
            )
            raw_piece = (
                own_piece if update_index == 0 else passed_along(own_piece, "view", -update_index)
            )
            estimate = sharded_update(
                estimate, raw_piece, view_index, my_group, route_tile, route_block,
                interp, row_psf, col_psf, psf_band, background,
            )
        return estimate
    pieces = []
    for update_index in range(view_count):
        own_piece = lax.dynamic_slice_in_dim(
            raw_views[0], (my_group - update_index) % view_count * planes, planes, 0
        )
        piece = own_piece if update_index == 0 else passed_along(own_piece, "view", -update_index)
        if pieces:
            piece, _ = lax.optimization_barrier((piece, pieces[-1]))
        else:
            estimate = lax.all_gather(initial_estimate, "tile", axis=1, tiled=True)
            piece, _ = lax.optimization_barrier((piece, estimate))
        pieces.append(lax.all_gather(piece, "tile", axis=1, tiled=True))
    plane_bands = lax.dynamic_slice_in_dim(psf_band, my_group * planes, planes, 0)
    for update_index in range(view_count):
        view_index = (my_group + update_index) % view_count
        matrix = interp[view_index]
        landing = route_tile[view_index, :, 0] * tile_blocks + route_block[view_index]
        row_taps = row_psf[view_index][plane_bands]
        col_taps = col_psf[view_index][plane_bands]
        level = background[view_index]
        estimate = jnp.stack(
            [
                kernel_update(
                    estimate[p],
                    pieces[update_index][p],
                    matrix,
                    landing,
                    row_taps[p],
                    col_taps[p],
                    level,
                )
                for p in range(planes)
            ]
        )
    return lax.dynamic_slice_in_dim(estimate, my_tile * tile_rows, tile_rows, 1)


def solution(mesh):
    return jax.shard_map(
        local,
        mesh=mesh,
        in_specs=(
            P("view", "tile", None),
            P("view", None, "tile", None),
            P(),
            P(),
            P(),
            P(),
            P(),
            P(),
            P(),
        ),
        out_specs=P("view", "tile", None),
        check_vma=False,
    )
```

```python
import jax
import jax.numpy as jnp
from jax import lax
from jax.sharding import PartitionSpec as P
from jax.experimental import pallas as pl
from jax.experimental.pallas import tpu as pltpu

BR = 8
BW = 128
TAPS = 17


def passed_along(x, axis, by):
    count = lax.axis_size(axis)
    return lax.ppermute(x, axis, [(i, (i + by) % count) for i in range(count)])


def to_blocks(values_in):
    rows, plane_width = values_in.shape
    shaped = values_in.reshape(rows // BR, BR, plane_width // BW, BW)
    return shaped.transpose(0, 2, 1, 3).reshape(-1, BR * BW)


def from_blocks(pieces, rows, plane_width):
    shaped = pieces.reshape(rows // BR, plane_width // BW, BR, BW)
    return shaped.transpose(0, 2, 1, 3).reshape(rows, plane_width)


def banded(taps_in, diff):
    result = jnp.zeros(diff.shape, jnp.float32)
    for tap_index in range(TAPS):
        result = result + jnp.where(diff == tap_index, taps_in[tap_index].astype(jnp.float32), 0.0)
    return result.astype(jnp.bfloat16)


def column_mats(taps_in, flipped):
    radius = (TAPS - 1) // 2
    source_lane = jnp.arange(BW, dtype=jnp.int32)[:, None]
    target_lane = jnp.arange(BW, dtype=jnp.int32)[None, :]
    mats = []
    for offset in (-1, 0, 1):
        if flipped:
            diff = target_lane - source_lane - offset * BW + radius
        else:
            diff = source_lane + offset * BW - target_lane + radius
        mats.append(banded(taps_in, diff))
    return mats


def row_mat(taps_in, rows):
    radius = (TAPS - 1) // 2
    out_row = jnp.arange(rows, dtype=jnp.int32)[:, None]
    src_row = jnp.arange(rows, dtype=jnp.int32)[None, :]
    return banded(taps_in, src_row - out_row + radius)


def column_pass(values_in, mats):
    rows, plane_width = values_in.shape
    col_count = plane_width // BW
    grid_cells = values_in.reshape(rows, col_count, BW)
    padded = jnp.pad(grid_cells, ((0, 0), (1, 1), (0, 0)))
    result_sum = jnp.zeros(grid_cells.shape, jnp.float32)
    for position in range(3):
        result_sum = result_sum + jnp.einsum(
            "rcj,jk->rck",
            padded[:, position : position + col_count],
            mats[position],
            preferred_element_type=jnp.float32,
        )
    return result_sum.reshape(rows, plane_width)


def update_plane(estimate, raw_plane, matrix, landing, row_taps, col_taps, level):
    rows, plane_width = estimate.shape
    blocks = (rows // BR) * (plane_width // BW)
    block_iota = jnp.arange(blocks, dtype=jnp.int32)
    rounded = estimate.astype(jnp.bfloat16).reshape(rows, plane_width // BW, BW)
    moved = jnp.einsum("rcj,jk->rck", rounded, matrix, preferred_element_type=jnp.float32)
    moved = moved.astype(jnp.bfloat16).reshape(rows, plane_width)
    gather_mat = landing[None, :] == block_iota[:, None]
    land_count = jnp.sum(gather_mat.astype(jnp.float32), axis=1)
    summed = jnp.dot(
        gather_mat.astype(jnp.bfloat16), to_blocks(moved), preferred_element_type=jnp.float32
    )
    summed = (summed / jnp.maximum(land_count, 1.0)[:, None]).astype(jnp.bfloat16)
    joined = from_blocks(summed, rows, plane_width)
    across = column_pass(joined, column_mats(col_taps, False)).astype(jnp.bfloat16)
    band = row_mat(row_taps, rows)
    blurred = jnp.dot(band, across, preferred_element_type=jnp.float32) + level
    ratio = (raw_plane.astype(jnp.float32) / blurred).astype(jnp.bfloat16)
    rows_back = jnp.dot(band.T, ratio, preferred_element_type=jnp.float32).astype(jnp.bfloat16)
    spread = column_pass(rows_back, column_mats(col_taps, True)).astype(jnp.bfloat16)
    returned = jnp.einsum(
        "rcj,kj->rck",
        spread.reshape(rows, plane_width // BW, BW),
        matrix,
        preferred_element_type=jnp.float32,
    ).astype(jnp.bfloat16)
    correction = jnp.take(to_blocks(returned.reshape(rows, plane_width)), landing, axis=0)
    return estimate * from_blocks(correction, rows, plane_width).astype(jnp.float32)


def plane_kernel(est_ref, raw_ref, m_ref, mt_ref, s_ref, cnt_ref, g_ref, bf_ref, bb_ref, a_ref,
                 at_ref, bg_ref, out_ref, work, joined, across, ratio):
    rows, plane_width = est_ref.shape
    nt = rows // BR
    nc = plane_width // BW
    f32 = jnp.float32
    bf16 = jnp.bfloat16

    def cols(c):
        return slice(c * BW, (c + 1) * BW)

    for c in range(nc):
        blk = est_ref[:, cols(c)].astype(bf16)
        moved = jnp.dot(blk, m_ref[...], preferred_element_type=f32)
        work[c] = moved.astype(bf16).astype(f32)

    def regroup(src, mat_ref, dst, post):
        for r in range(BR):
            stacked = jnp.concatenate(
                [src[c, pl.ds(r, nt, stride=BR), :] for c in range(nc)], axis=0
            )
            result = jnp.dot(mat_ref[...], stacked.astype(bf16), preferred_element_type=f32)
            result = post(result)
            for c in range(nc):
                dst[c, pl.ds(r, nt, stride=BR), :] = result[c * nt:(c + 1) * nt, :]

    regroup(work, s_ref, joined,
            lambda v: (v / cnt_ref[...]).astype(bf16).astype(f32))

    def column_blur(take, mats_ref, c):
        total = None
        for offset in (-1, 0, 1):
            if 0 <= c + offset < nc:
                part = jnp.dot(take(c + offset).astype(bf16), mats_ref[offset + 1],
                               preferred_element_type=f32)
                total = part if total is None else total + part
        return total

    for c in range(nc):
        across[:, cols(c)] = column_blur(lambda i: joined[i], bf_ref, c).astype(bf16)
    level = bg_ref[0]
    for c in range(nc):
        blurred = jnp.dot(a_ref[...], across[:, cols(c)], preferred_element_type=f32) + level
        quotient = (raw_ref[:, cols(c)].astype(f32) / blurred).astype(bf16)
        ratio[:, cols(c)] = jnp.dot(at_ref[...], quotient, preferred_element_type=f32).astype(bf16)
    for c in range(nc):
        spread = column_blur(lambda i: ratio[:, cols(i)], bb_ref, c).astype(bf16)
        back = jnp.dot(spread, mt_ref[...], preferred_element_type=f32)
        work[c] = back.astype(bf16).astype(f32)
    regroup(work, g_ref, joined, lambda v: v)
    for c in range(nc):
        out_ref[:, cols(c)] = est_ref[:, cols(c)] * joined[c]


def band_kernel(row_ref, col_ref, a_ref, at_ref, bf_ref, bb_ref):
    count, rows, _ = a_ref.shape
    radius = (TAPS - 1) // 2
    out_row = lax.broadcasted_iota(jnp.int32, (rows, rows), 0)
    src_row = lax.broadcasted_iota(jnp.int32, (rows, rows), 1)
    source_lane = lax.broadcasted_iota(jnp.int32, (BW, BW), 0)
    target_lane = lax.broadcasted_iota(jnp.int32, (BW, BW), 1)

    def build(diff, taps_ref, base):
        result = jnp.zeros(diff.shape, jnp.float32)
        for tap_index in range(TAPS):
            result = jnp.where(diff == tap_index, taps_ref[base + tap_index], result)
        return result.astype(jnp.bfloat16)

    for i in range(count):
        base = i * TAPS
        a_ref[i] = build(src_row - out_row + radius, row_ref, base)
        at_ref[i] = build(out_row - src_row + radius, row_ref, base)
        for offset in (-1, 0, 1):
            forward = source_lane + offset * BW - target_lane + radius
            bf_ref[i, offset + 1] = build(forward, col_ref, base)
            backward = target_lane - source_lane - offset * BW + radius
            bb_ref[i, offset + 1] = build(backward, col_ref, base)


def all_bands(row_taps, col_taps, rows):
    count = row_taps.shape[0]
    smem = pl.BlockSpec(memory_space=pltpu.SMEM)
    vmem = pl.BlockSpec(memory_space=pltpu.VMEM)
    return pl.pallas_call(
        band_kernel,
        out_shape=(
            jax.ShapeDtypeStruct((count, rows, rows), jnp.bfloat16),
            jax.ShapeDtypeStruct((count, rows, rows), jnp.bfloat16),
            jax.ShapeDtypeStruct((count, 3, BW, BW), jnp.bfloat16),
            jax.ShapeDtypeStruct((count, 3, BW, BW), jnp.bfloat16),
        ),
        in_specs=[smem, smem],
        out_specs=(vmem, vmem, vmem, vmem),
    )(row_taps.astype(jnp.float32).reshape(-1), col_taps.astype(jnp.float32).reshape(-1))


def kernel_update(estimate, raw_plane, matrix, landing, bands, level):
    rows, plane_width = estimate.shape
    nt = rows // BR
    nc = plane_width // BW
    blocks = nt * nc
    order = landing.reshape(nt, nc).T.reshape(-1)
    place = (order % nc) * nt + order // nc
    spots = jnp.arange(blocks, dtype=jnp.int32)
    sum_mat = place[None, :] == spots[:, None]
    pick_mat = place[:, None] == spots[None, :]
    count = jnp.sum(sum_mat.astype(jnp.float32), axis=1)
    count = jnp.broadcast_to(jnp.maximum(count, 1.0)[:, None], (blocks, BW))
    vmem = pl.BlockSpec(memory_space=pltpu.VMEM)
    return pl.pallas_call(
        plane_kernel,
        out_shape=jax.ShapeDtypeStruct((rows, plane_width), jnp.float32),
        in_specs=[vmem] * 11 + [pl.BlockSpec(memory_space=pltpu.SMEM)],
        out_specs=vmem,
        scratch_shapes=[
            pltpu.VMEM((nc, rows, BW), jnp.float32),
            pltpu.VMEM((nc, rows, BW), jnp.float32),
            pltpu.VMEM((rows, plane_width), jnp.bfloat16),
            pltpu.VMEM((rows, plane_width), jnp.bfloat16),
        ],
        compiler_params=pltpu.CompilerParams(vmem_limit_bytes=48 * 1024 * 1024),
        cost_estimate=pl.CostEstimate(
            flops=2 * rows * plane_width * (4 * BW + 2 * rows + 2 * blocks // BR * BR),
            bytes_accessed=rows * plane_width * 10,
            transcendentals=0,
        ),
    )(
        estimate,
        raw_plane,
        matrix,
        matrix.T,
        sum_mat.astype(jnp.bfloat16),
        count,
        pick_mat.astype(jnp.bfloat16),
        bands[2],
        bands[3],
        bands[0],
        bands[1],
        jnp.reshape(level, (1,)).astype(jnp.float32),
    )


def with_halo(cells, sides, width):
    for axis, dim in sides:
        count = lax.axis_size(axis)
        ends = count - 1
        head = lax.slice_in_dim(cells, 0, width, axis=dim)
        tail = lax.slice_in_dim(cells, cells.shape[dim] - width, cells.shape[dim], axis=dim)
        cells = jnp.concatenate(
            [
                lax.ppermute(tail, axis, [(i, (i + 1) % count) for i in range(ends)]),
                cells,
                lax.ppermute(head, axis, [((i + 1) % count, i) for i in range(ends)]),
            ],
            axis=dim,
        )
    return cells


def sharded_to_blocks(values_in):
    planes, tile_rows, plane_width = values_in.shape
    shaped = values_in.reshape(planes, tile_rows // BR, BR, plane_width // BW, BW)
    return shaped.transpose(1, 3, 0, 2, 4).reshape(-1, planes, BR, BW)


def sharded_from_blocks(pieces, tile_rows, plane_width):
    planes = pieces.shape[1]
    shaped = pieces.reshape(tile_rows // BR, plane_width // BW, planes, BR, BW)
    return shaped.transpose(2, 0, 3, 1, 4).reshape(planes, tile_rows, plane_width)


def sharded_column_pass(values_in, taps_in, flipped):
    planes, tile_rows, plane_width = values_in.shape
    radius = (taps_in.shape[1] - 1) // 2
    lane_iota = jnp.arange(BW, dtype=jnp.int32)
    source_lane = lane_iota[:, None]
    target_lane = lane_iota[None, :]
    zero_bf = jnp.zeros((), jnp.bfloat16)
    band_mats = []
    for offset in (-1, 0, 1):
        if flipped:
            tap_index = target_lane - source_lane - offset * BW + radius
        else:
            tap_index = source_lane + offset * BW - target_lane + radius
        inside = (tap_index >= 0) & (tap_index <= 2 * radius)
        picked = taps_in[:, jnp.clip(tap_index, 0, 2 * radius)]
        band_mats.append(jnp.where(inside[None, :, :], picked, zero_bf))
    col_count = plane_width // BW
    grid_cells = values_in.reshape(planes, tile_rows, col_count, BW)
    padded = jnp.pad(grid_cells, ((0, 0), (0, 0), (1, 1), (0, 0)))
    result_sum = jnp.zeros(grid_cells.shape, jnp.float32)
    for position in range(3):
        result_sum = result_sum + jnp.einsum(
            "prcj,pjk->prck",
            padded[:, :, position : position + col_count],
            band_mats[position],
            preferred_element_type=jnp.float32,
        )
    return result_sum.reshape(planes, tile_rows, plane_width)


def row_pass(padded, taps_in, flipped):
    planes, extended, plane_width = padded.shape
    radius = (taps_in.shape[1] - 1) // 2
    tile_rows = extended - 2 * radius
    row_iota = jnp.arange(tile_rows, dtype=jnp.int32)[:, None]
    src_iota = jnp.arange(extended, dtype=jnp.int32)[None, :]
    if flipped:
        tap_index = row_iota + 2 * radius - src_iota
    else:
        tap_index = src_iota - row_iota
    inside = (tap_index >= 0) & (tap_index <= 2 * radius)
    band_rows = jnp.where(
        inside[None, :, :],
        taps_in[:, jnp.clip(tap_index, 0, 2 * radius)],
        jnp.zeros((), jnp.bfloat16),
    )
    return jnp.einsum("prs,psw->prw", band_rows, padded, preferred_element_type=jnp.float32)


def sharded_update(
    estimate,
    raw_piece,
    view_index,
    slab_index,
    route_tile,
    route_block,
    interp,
    row_psf,
    col_psf,
    psf_band,
    background,
):
    tile_count = lax.axis_size("tile")
    my_tile = lax.axis_index("tile")
    planes, tile_rows, plane_width = estimate.shape
    blocks = tile_rows // BR * (plane_width // BW)
    capacity = max(2, 2 * blocks // tile_count)
    radius = (TAPS - 1) // 2
    matrix = interp[view_index]
    dest_tile = route_tile[view_index, :, 0].reshape(tile_count, blocks)
    dest_block = route_block[view_index].reshape(tile_count, blocks)
    tiles_iota = jnp.arange(tile_count, dtype=jnp.int32)
    one_hot = (dest_tile[:, :, None] == tiles_iota[None, None, :]).astype(jnp.int32)
    slot_rank = jnp.sum((jnp.cumsum(one_hot, axis=1) - one_hot) * one_hot, axis=2)
    slot_index = dest_tile * capacity + slot_rank
    my_slots = slot_index[my_tile]
    slots_iota = jnp.arange(tile_count * capacity, dtype=jnp.int32)
    block_iota = jnp.arange(blocks, dtype=jnp.int32)
    match_send = my_slots[None, :] == slots_iota[:, None]
    send_ok = jnp.any(match_send, axis=1)
    send_src = jnp.sum(jnp.where(match_send, block_iota[None, :], 0), axis=1)
    match_recv = (dest_tile == my_tile)[:, None, :] & (
        slot_rank[:, None, :] == jnp.arange(capacity, dtype=jnp.int32)[None, :, None]
    )
    recv_ok = jnp.any(match_recv, axis=2).reshape(-1)
    recv_off = jnp.sum(jnp.where(match_recv, dest_block[:, None, :], 0), axis=2).reshape(-1)
    zero_bf = jnp.zeros((), jnp.bfloat16)
    rounded_estimate = estimate.astype(jnp.bfloat16)
    interpolated = jnp.einsum(
        "bprj,jk->bprk", sharded_to_blocks(rounded_estimate), matrix, preferred_element_type=jnp.float32
    ).astype(jnp.bfloat16)
    outgoing = jnp.where(send_ok[:, None, None, None], interpolated[send_src], zero_bf)
    outgoing = outgoing.reshape(tile_count, capacity, planes, BR, BW)
    incoming = lax.all_to_all(outgoing, "tile", split_axis=0, concat_axis=0, tiled=True)
    incoming = incoming.reshape(tile_count * capacity, planes * BR * BW)
    landing = (recv_off[None, :] == block_iota[:, None]) & recv_ok[None, :]
    land_count = jnp.sum(landing.astype(jnp.float32), axis=1)
    summed = jnp.dot(landing.astype(jnp.bfloat16), incoming, preferred_element_type=jnp.float32)
    summed = (summed / jnp.maximum(land_count, 1.0)[:, None]).astype(jnp.bfloat16)
    joined_field = sharded_from_blocks(summed.reshape(blocks, planes, BR, BW), tile_rows, plane_width)
    plane_bands = lax.dynamic_slice_in_dim(psf_band, slab_index * planes, planes, 0)
    row_taps = row_psf[view_index][plane_bands]
    col_taps = col_psf[view_index][plane_bands]
    across = sharded_column_pass(joined_field, col_taps, False).astype(jnp.bfloat16)
    padded = with_halo(across, (("tile", 1),), radius)
    blurred = row_pass(padded, row_taps, False) + background[view_index]
    ratio_field = (raw_piece.astype(jnp.float32) / blurred).astype(jnp.bfloat16)
    padded_ratio = with_halo(ratio_field, (("tile", 1),), radius)
    rows_back = row_pass(padded_ratio, row_taps, True).astype(jnp.bfloat16)
    spread = sharded_column_pass(rows_back, col_taps, True).astype(jnp.bfloat16)
    returned_blocks = jnp.einsum(
        "bprj,kj->bprk", sharded_to_blocks(spread), matrix, preferred_element_type=jnp.float32
    ).astype(jnp.bfloat16)
    returning = jnp.where(recv_ok[:, None, None, None], returned_blocks[recv_off], zero_bf)
    returning = returning.reshape(tile_count, capacity, planes, BR, BW)
    arrived = lax.all_to_all(returning, "tile", split_axis=0, concat_axis=0, tiled=True)
    arrived = arrived.reshape(tile_count * capacity, planes, BR, BW)
    correction = arrived[my_slots]
    return estimate * sharded_from_blocks(correction.astype(jnp.float32), tile_rows, plane_width)


def local(
    initial_estimate,
    raw_views,
    route_tile,
    route_block,
    interp,
    row_kernel,
    col_kernel,
    psf_band,
    background,
):
    view_count = lax.axis_size("view")
    my_group = lax.axis_index("view")
    my_tile = lax.axis_index("tile")
    planes, tile_rows, plane_width = initial_estimate.shape
    tile_blocks = (tile_rows // BR) * (plane_width // BW)
    row_psf = (row_kernel / jnp.sum(row_kernel, axis=2, keepdims=True)).astype(jnp.bfloat16)
    col_psf = (col_kernel / jnp.sum(col_kernel, axis=2, keepdims=True)).astype(jnp.bfloat16)
    if view_count * tile_rows * plane_width * lax.axis_size("tile") > (1 << 22):
        estimate = initial_estimate
        for update_index in range(view_count):
            view_index = (my_group + update_index) % view_count
            own_piece = lax.dynamic_slice_in_dim(
                raw_views[0], (my_group - update_index) % view_count * planes, planes, 0
            )
            raw_piece = (
                own_piece if update_index == 0 else passed_along(own_piece, "view", -update_index)
            )
            estimate = sharded_update(
                estimate, raw_piece, view_index, my_group, route_tile, route_block,
                interp, row_psf, col_psf, psf_band, background,
            )
        return estimate
    pieces = []
    for update_index in range(view_count):
        own_piece = lax.dynamic_slice_in_dim(
            raw_views[0], (my_group - update_index) % view_count * planes, planes, 0
        )
        piece = own_piece if update_index == 0 else passed_along(own_piece, "view", -update_index)
        if pieces:
            piece, _ = lax.optimization_barrier((piece, pieces[-1]))
        pieces.append(lax.all_gather(piece, "tile", axis=1, tiled=True))
    estimate = lax.all_gather(initial_estimate, "tile", axis=1, tiled=True)
    plane_bands = lax.dynamic_slice_in_dim(psf_band, my_group * planes, planes, 0)
    views_in_order = (my_group + jnp.arange(view_count, dtype=jnp.int32)) % view_count
    bands = all_bands(
        row_psf[views_in_order][:, plane_bands].reshape(view_count * planes, TAPS),
        col_psf[views_in_order][:, plane_bands].reshape(view_count * planes, TAPS),
        tile_rows * lax.axis_size("tile"),
    )
    for update_index in range(view_count):
        view_index = (my_group + update_index) % view_count
        matrix = interp[view_index]
        landing = route_tile[view_index, :, 0] * tile_blocks + route_block[view_index]
        level = background[view_index]
        estimate = jnp.stack(
            [
                kernel_update(
                    estimate[p],
                    pieces[update_index][p],
                    matrix,
                    landing,
                    [b[update_index * planes + p] for b in bands],
                    level,
                )
                for p in range(planes)
            ]
        )
    return lax.dynamic_slice_in_dim(estimate, my_tile * tile_rows, tile_rows, 1)


def solution(mesh):
    return jax.shard_map(
        local,
        mesh=mesh,
        in_specs=(
            P("view", "tile", None),
            P("view", None, "tile", None),
            P(),
            P(),
            P(),
            P(),
            P(),
            P(),
            P(),
        ),
        out_specs=P("view", "tile", None),
        check_vma=False,
    )
```

```python
import jax
import jax.numpy as jnp
from jax import lax
from jax.sharding import PartitionSpec as P
from jax.experimental import pallas as pl
from jax.experimental.pallas import tpu as pltpu

BR = 8
BW = 128
TAPS = 17


def passed_along(x, axis, by):
    count = lax.axis_size(axis)
    return lax.ppermute(x, axis, [(i, (i + by) % count) for i in range(count)])


def to_blocks(values_in):
    rows, plane_width = values_in.shape
    shaped = values_in.reshape(rows // BR, BR, plane_width // BW, BW)
    return shaped.transpose(0, 2, 1, 3).reshape(-1, BR * BW)


def from_blocks(pieces, rows, plane_width):
    shaped = pieces.reshape(rows // BR, plane_width // BW, BR, BW)
    return shaped.transpose(0, 2, 1, 3).reshape(rows, plane_width)


def banded(taps_in, diff):
    result = jnp.zeros(diff.shape, jnp.float32)
    for tap_index in range(TAPS):
        result = result + jnp.where(diff == tap_index, taps_in[tap_index].astype(jnp.float32), 0.0)
    return result.astype(jnp.bfloat16)


def column_mats(taps_in, flipped):
    radius = (TAPS - 1) // 2
    source_lane = jnp.arange(BW, dtype=jnp.int32)[:, None]
    target_lane = jnp.arange(BW, dtype=jnp.int32)[None, :]
    mats = []
    for offset in (-1, 0, 1):
        if flipped:
            diff = target_lane - source_lane - offset * BW + radius
        else:
            diff = source_lane + offset * BW - target_lane + radius
        mats.append(banded(taps_in, diff))
    return mats


def row_mat(taps_in, rows):
    radius = (TAPS - 1) // 2
    out_row = jnp.arange(rows, dtype=jnp.int32)[:, None]
    src_row = jnp.arange(rows, dtype=jnp.int32)[None, :]
    return banded(taps_in, src_row - out_row + radius)


def column_pass(values_in, mats):
    rows, plane_width = values_in.shape
    col_count = plane_width // BW
    grid_cells = values_in.reshape(rows, col_count, BW)
    padded = jnp.pad(grid_cells, ((0, 0), (1, 1), (0, 0)))
    result_sum = jnp.zeros(grid_cells.shape, jnp.float32)
    for position in range(3):
        result_sum = result_sum + jnp.einsum(
            "rcj,jk->rck",
            padded[:, position : position + col_count],
            mats[position],
            preferred_element_type=jnp.float32,
        )
    return result_sum.reshape(rows, plane_width)


def update_plane(estimate, raw_plane, matrix, landing, row_taps, col_taps, level):
    rows, plane_width = estimate.shape
    blocks = (rows // BR) * (plane_width // BW)
    block_iota = jnp.arange(blocks, dtype=jnp.int32)
    rounded = estimate.astype(jnp.bfloat16).reshape(rows, plane_width // BW, BW)
    moved = jnp.einsum("rcj,jk->rck", rounded, matrix, preferred_element_type=jnp.float32)
    moved = moved.astype(jnp.bfloat16).reshape(rows, plane_width)
    gather_mat = landing[None, :] == block_iota[:, None]
    land_count = jnp.sum(gather_mat.astype(jnp.float32), axis=1)
    summed = jnp.dot(
        gather_mat.astype(jnp.bfloat16), to_blocks(moved), preferred_element_type=jnp.float32
    )
    summed = (summed / jnp.maximum(land_count, 1.0)[:, None]).astype(jnp.bfloat16)
    joined = from_blocks(summed, rows, plane_width)
    across = column_pass(joined, column_mats(col_taps, False)).astype(jnp.bfloat16)
    band = row_mat(row_taps, rows)
    blurred = jnp.dot(band, across, preferred_element_type=jnp.float32) + level
    ratio = (raw_plane.astype(jnp.float32) / blurred).astype(jnp.bfloat16)
    rows_back = jnp.dot(band.T, ratio, preferred_element_type=jnp.float32).astype(jnp.bfloat16)
    spread = column_pass(rows_back, column_mats(col_taps, True)).astype(jnp.bfloat16)
    returned = jnp.einsum(
        "rcj,kj->rck",
        spread.reshape(rows, plane_width // BW, BW),
        matrix,
        preferred_element_type=jnp.float32,
    ).astype(jnp.bfloat16)
    correction = jnp.take(to_blocks(returned.reshape(rows, plane_width)), landing, axis=0)
    return estimate * from_blocks(correction, rows, plane_width).astype(jnp.float32)


def plane_kernel(est_ref, raw_ref, m_ref, mt_ref, s_ref, cnt_ref, g_ref, bf_ref, bb_ref, a_ref,
                 at_ref, bg_ref, out_ref, work, joined, across, ratio):
    rows, plane_width = est_ref.shape
    nt = rows // BR
    nc = plane_width // BW
    f32 = jnp.float32
    bf16 = jnp.bfloat16

    def cols(c):
        return slice(c * BW, (c + 1) * BW)

    for c in range(nc):
        blk = est_ref[:, cols(c)].astype(bf16)
        moved = jnp.dot(blk, m_ref[...], preferred_element_type=f32)
        work[c] = moved.astype(bf16).astype(f32)

    def regroup(src, mat_ref, dst, post):
        for r in range(BR):
            stacked = jnp.concatenate(
                [src[c, pl.ds(r, nt, stride=BR), :] for c in range(nc)], axis=0
            )
            result = jnp.dot(mat_ref[...], stacked.astype(bf16), preferred_element_type=f32)
            result = post(result)
            for c in range(nc):
                dst[c, pl.ds(r, nt, stride=BR), :] = result[c * nt:(c + 1) * nt, :]

    regroup(work, s_ref, joined,
            lambda v: (v / cnt_ref[...]).astype(bf16).astype(f32))

    def column_blur(take, mats_ref, c):
        total = None
        for offset in (-1, 0, 1):
            if 0 <= c + offset < nc:
                part = jnp.dot(take(c + offset).astype(bf16), mats_ref[offset + 1],
                               preferred_element_type=f32)
                total = part if total is None else total + part
        return total

    for c in range(nc):
        across[:, cols(c)] = column_blur(lambda i: joined[i], bf_ref, c).astype(bf16)
    level = bg_ref[0]
    for c in range(nc):
        blurred = jnp.dot(a_ref[...], across[:, cols(c)], preferred_element_type=f32) + level
        quotient = (raw_ref[:, cols(c)].astype(f32) / blurred).astype(bf16)
        ratio[:, cols(c)] = jnp.dot(at_ref[...], quotient, preferred_element_type=f32).astype(bf16)
    for c in range(nc):
        spread = column_blur(lambda i: ratio[:, cols(i)], bb_ref, c).astype(bf16)
        back = jnp.dot(spread, mt_ref[...], preferred_element_type=f32)
        work[c] = back.astype(bf16).astype(f32)
    regroup(work, g_ref, joined, lambda v: v)
    for c in range(nc):
        out_ref[:, cols(c)] = est_ref[:, cols(c)] * joined[c]


def band_kernel(row_ref, col_ref, a_ref, at_ref, bf_ref, bb_ref):
    count, rows, _ = a_ref.shape
    radius = (TAPS - 1) // 2
    out_row = lax.broadcasted_iota(jnp.int32, (rows, rows), 0)
    src_row = lax.broadcasted_iota(jnp.int32, (rows, rows), 1)
    source_lane = lax.broadcasted_iota(jnp.int32, (BW, BW), 0)
    target_lane = lax.broadcasted_iota(jnp.int32, (BW, BW), 1)

    def build(diff, taps_ref, base):
        result = jnp.zeros(diff.shape, jnp.float32)
        for tap_index in range(TAPS):
            result = jnp.where(diff == tap_index, taps_ref[base + tap_index], result)
        return result.astype(jnp.bfloat16)

    for i in range(count):
        base = i * TAPS
        a_ref[i] = build(src_row - out_row + radius, row_ref, base)
        at_ref[i] = build(out_row - src_row + radius, row_ref, base)
        for offset in (-1, 0, 1):
            forward = source_lane + offset * BW - target_lane + radius
            bf_ref[i, offset + 1] = build(forward, col_ref, base)
            backward = target_lane - source_lane - offset * BW + radius
            bb_ref[i, offset + 1] = build(backward, col_ref, base)


def all_bands(row_taps, col_taps, rows):
    count = row_taps.shape[0]
    smem = pl.BlockSpec(memory_space=pltpu.SMEM)
    vmem = pl.BlockSpec(memory_space=pltpu.VMEM)
    return pl.pallas_call(
        band_kernel,
        out_shape=(
            jax.ShapeDtypeStruct((count, rows, rows), jnp.bfloat16),
            jax.ShapeDtypeStruct((count, rows, rows), jnp.bfloat16),
            jax.ShapeDtypeStruct((count, 3, BW, BW), jnp.bfloat16),
            jax.ShapeDtypeStruct((count, 3, BW, BW), jnp.bfloat16),
        ),
        in_specs=[smem, smem],
        out_specs=(vmem, vmem, vmem, vmem),
    )(row_taps.astype(jnp.float32).reshape(-1), col_taps.astype(jnp.float32).reshape(-1))


def kernel_update(estimate, raw_plane, matrix, landing, bands, level):
    rows, plane_width = estimate.shape
    nt = rows // BR
    nc = plane_width // BW
    blocks = nt * nc
    order = landing.reshape(nt, nc).T.reshape(-1)
    place = (order % nc) * nt + order // nc
    spots = jnp.arange(blocks, dtype=jnp.int32)
    sum_mat = place[None, :] == spots[:, None]
    pick_mat = place[:, None] == spots[None, :]
    count = jnp.sum(sum_mat.astype(jnp.float32), axis=1)
    count = jnp.broadcast_to(jnp.maximum(count, 1.0)[:, None], (blocks, BW))
    vmem = pl.BlockSpec(memory_space=pltpu.VMEM)
    return pl.pallas_call(
        plane_kernel,
        out_shape=jax.ShapeDtypeStruct((rows, plane_width), jnp.float32),
        in_specs=[vmem] * 11 + [pl.BlockSpec(memory_space=pltpu.SMEM)],
        out_specs=vmem,
        scratch_shapes=[
            pltpu.VMEM((nc, rows, BW), jnp.float32),
            pltpu.VMEM((nc, rows, BW), jnp.float32),
            pltpu.VMEM((rows, plane_width), jnp.bfloat16),
            pltpu.VMEM((rows, plane_width), jnp.bfloat16),
        ],
        compiler_params=pltpu.CompilerParams(vmem_limit_bytes=48 * 1024 * 1024),
        cost_estimate=pl.CostEstimate(
            flops=2 * rows * plane_width * (4 * BW + 2 * rows + 2 * blocks // BR * BR),
            bytes_accessed=rows * plane_width * 10,
            transcendentals=0,
        ),
    )(
        estimate,
        raw_plane,
        matrix,
        matrix.T,
        sum_mat.astype(jnp.bfloat16),
        count,
        pick_mat.astype(jnp.bfloat16),
        bands[2],
        bands[3],
        bands[0],
        bands[1],
        jnp.reshape(level, (1,)).astype(jnp.float32),
    )


def with_halo(cells, sides, width):
    for axis, dim in sides:
        count = lax.axis_size(axis)
        ends = count - 1
        head = lax.slice_in_dim(cells, 0, width, axis=dim)
        tail = lax.slice_in_dim(cells, cells.shape[dim] - width, cells.shape[dim], axis=dim)
        cells = jnp.concatenate(
            [
                lax.ppermute(tail, axis, [(i, (i + 1) % count) for i in range(ends)]),
                cells,
                lax.ppermute(head, axis, [((i + 1) % count, i) for i in range(ends)]),
            ],
            axis=dim,
        )
    return cells


def sharded_to_blocks(values_in):
    planes, tile_rows, plane_width = values_in.shape
    shaped = values_in.reshape(planes, tile_rows // BR, BR, plane_width // BW, BW)
    return shaped.transpose(1, 3, 0, 2, 4).reshape(-1, planes, BR, BW)


def sharded_from_blocks(pieces, tile_rows, plane_width):
    planes = pieces.shape[1]
    shaped = pieces.reshape(tile_rows // BR, plane_width // BW, planes, BR, BW)
    return shaped.transpose(2, 0, 3, 1, 4).reshape(planes, tile_rows, plane_width)


def sharded_column_pass(values_in, taps_in, flipped):
    planes, tile_rows, plane_width = values_in.shape
    radius = (taps_in.shape[1] - 1) // 2
    lane_iota = jnp.arange(BW, dtype=jnp.int32)
    source_lane = lane_iota[:, None]
    target_lane = lane_iota[None, :]
    zero_bf = jnp.zeros((), jnp.bfloat16)
    band_mats = []
    for offset in (-1, 0, 1):
        if flipped:
            tap_index = target_lane - source_lane - offset * BW + radius
        else:
            tap_index = source_lane + offset * BW - target_lane + radius
        inside = (tap_index >= 0) & (tap_index <= 2 * radius)
        picked = taps_in[:, jnp.clip(tap_index, 0, 2 * radius)]
        band_mats.append(jnp.where(inside[None, :, :], picked, zero_bf))
    col_count = plane_width // BW
    grid_cells = values_in.reshape(planes, tile_rows, col_count, BW)
    padded = jnp.pad(grid_cells, ((0, 0), (0, 0), (1, 1), (0, 0)))
    result_sum = jnp.zeros(grid_cells.shape, jnp.float32)
    for position in range(3):
        result_sum = result_sum + jnp.einsum(
            "prcj,pjk->prck",
            padded[:, :, position : position + col_count],
            band_mats[position],
            preferred_element_type=jnp.float32,
        )
    return result_sum.reshape(planes, tile_rows, plane_width)


def row_pass(padded, taps_in, flipped):
    planes, extended, plane_width = padded.shape
    radius = (taps_in.shape[1] - 1) // 2
    tile_rows = extended - 2 * radius
    row_iota = jnp.arange(tile_rows, dtype=jnp.int32)[:, None]
    src_iota = jnp.arange(extended, dtype=jnp.int32)[None, :]
    if flipped:
        tap_index = row_iota + 2 * radius - src_iota
    else:
        tap_index = src_iota - row_iota
    inside = (tap_index >= 0) & (tap_index <= 2 * radius)
    band_rows = jnp.where(
        inside[None, :, :],
        taps_in[:, jnp.clip(tap_index, 0, 2 * radius)],
        jnp.zeros((), jnp.bfloat16),
    )
    return jnp.einsum("prs,psw->prw", band_rows, padded, preferred_element_type=jnp.float32)


def sharded_update(
    estimate,
    raw_piece,
    view_index,
    slab_index,
    route_tile,
    route_block,
    interp,
    row_psf,
    col_psf,
    psf_band,
    background,
):
    tile_count = lax.axis_size("tile")
    my_tile = lax.axis_index("tile")
    planes, tile_rows, plane_width = estimate.shape
    blocks = tile_rows // BR * (plane_width // BW)
    capacity = max(2, 2 * blocks // tile_count)
    radius = (TAPS - 1) // 2
    matrix = interp[view_index]
    dest_tile = route_tile[view_index, :, 0].reshape(tile_count, blocks)
    dest_block = route_block[view_index].reshape(tile_count, blocks)
    tiles_iota = jnp.arange(tile_count, dtype=jnp.int32)
    one_hot = (dest_tile[:, :, None] == tiles_iota[None, None, :]).astype(jnp.int32)
    slot_rank = jnp.sum((jnp.cumsum(one_hot, axis=1) - one_hot) * one_hot, axis=2)
    slot_index = dest_tile * capacity + slot_rank
    my_slots = slot_index[my_tile]
    slots_iota = jnp.arange(tile_count * capacity, dtype=jnp.int32)
    block_iota = jnp.arange(blocks, dtype=jnp.int32)
    match_send = my_slots[None, :] == slots_iota[:, None]
    send_ok = jnp.any(match_send, axis=1)
    send_src = jnp.sum(jnp.where(match_send, block_iota[None, :], 0), axis=1)
    match_recv = (dest_tile == my_tile)[:, None, :] & (
        slot_rank[:, None, :] == jnp.arange(capacity, dtype=jnp.int32)[None, :, None]
    )
    recv_ok = jnp.any(match_recv, axis=2).reshape(-1)
    recv_off = jnp.sum(jnp.where(match_recv, dest_block[:, None, :], 0), axis=2).reshape(-1)
    zero_bf = jnp.zeros((), jnp.bfloat16)
    rounded_estimate = estimate.astype(jnp.bfloat16)
    interpolated = jnp.einsum(
        "bprj,jk->bprk", sharded_to_blocks(rounded_estimate), matrix, preferred_element_type=jnp.float32
    ).astype(jnp.bfloat16)
    outgoing = jnp.where(send_ok[:, None, None, None], interpolated[send_src], zero_bf)
    outgoing = outgoing.reshape(tile_count, capacity, planes, BR, BW)
    incoming = lax.all_to_all(outgoing, "tile", split_axis=0, concat_axis=0, tiled=True)
    incoming = incoming.reshape(tile_count * capacity, planes * BR * BW)
    landing = (recv_off[None, :] == block_iota[:, None]) & recv_ok[None, :]
    land_count = jnp.sum(landing.astype(jnp.float32), axis=1)
    summed = jnp.dot(landing.astype(jnp.bfloat16), incoming, preferred_element_type=jnp.float32)
    summed = (summed / jnp.maximum(land_count, 1.0)[:, None]).astype(jnp.bfloat16)
    joined_field = sharded_from_blocks(summed.reshape(blocks, planes, BR, BW), tile_rows, plane_width)
    plane_bands = lax.dynamic_slice_in_dim(psf_band, slab_index * planes, planes, 0)
    row_taps = row_psf[view_index][plane_bands]
    col_taps = col_psf[view_index][plane_bands]
    across = sharded_column_pass(joined_field, col_taps, False).astype(jnp.bfloat16)
    padded = with_halo(across, (("tile", 1),), radius)
    blurred = row_pass(padded, row_taps, False) + background[view_index]
    ratio_field = (raw_piece.astype(jnp.float32) / blurred).astype(jnp.bfloat16)
    padded_ratio = with_halo(ratio_field, (("tile", 1),), radius)
    rows_back = row_pass(padded_ratio, row_taps, True).astype(jnp.bfloat16)
    spread = sharded_column_pass(rows_back, col_taps, True).astype(jnp.bfloat16)
    returned_blocks = jnp.einsum(
        "bprj,kj->bprk", sharded_to_blocks(spread), matrix, preferred_element_type=jnp.float32
    ).astype(jnp.bfloat16)
    returning = jnp.where(recv_ok[:, None, None, None], returned_blocks[recv_off], zero_bf)
    returning = returning.reshape(tile_count, capacity, planes, BR, BW)
    arrived = lax.all_to_all(returning, "tile", split_axis=0, concat_axis=0, tiled=True)
    arrived = arrived.reshape(tile_count * capacity, planes, BR, BW)
    correction = arrived[my_slots]
    return estimate * sharded_from_blocks(correction.astype(jnp.float32), tile_rows, plane_width)


def local(
    initial_estimate,
    raw_views,
    route_tile,
    route_block,
    interp,
    row_kernel,
    col_kernel,
    psf_band,
    background,
):
    view_count = lax.axis_size("view")
    my_group = lax.axis_index("view")
    my_tile = lax.axis_index("tile")
    planes, tile_rows, plane_width = initial_estimate.shape
    tile_blocks = (tile_rows // BR) * (plane_width // BW)
    row_psf = (row_kernel / jnp.sum(row_kernel, axis=2, keepdims=True)).astype(jnp.bfloat16)
    col_psf = (col_kernel / jnp.sum(col_kernel, axis=2, keepdims=True)).astype(jnp.bfloat16)
    if view_count * tile_rows * plane_width * lax.axis_size("tile") > (1 << 22):
        estimate = initial_estimate
        for update_index in range(view_count):
            view_index = (my_group + update_index) % view_count
            own_piece = lax.dynamic_slice_in_dim(
                raw_views[0], (my_group - update_index) % view_count * planes, planes, 0
            )
            raw_piece = (
                own_piece if update_index == 0 else passed_along(own_piece, "view", -update_index)
            )
            estimate = sharded_update(
                estimate, raw_piece, view_index, my_group, route_tile, route_block,
                interp, row_psf, col_psf, psf_band, background,
            )
        return estimate
    pieces = []
    for update_index in range(view_count):
        own_piece = lax.dynamic_slice_in_dim(
            raw_views[0], (my_group - update_index) % view_count * planes, planes, 0
        )
        piece = own_piece if update_index == 0 else passed_along(own_piece, "view", -update_index)
        pieces.append(piece)
    pieces = lax.all_gather(jnp.stack(pieces), "tile", axis=2, tiled=True)
    tile_count = lax.axis_size("tile")
    arrived = [initial_estimate] + [
        passed_along(initial_estimate, "tile", shift) for shift in range(1, tile_count)
    ]
    source_order = (my_tile - jnp.arange(tile_count, dtype=jnp.int32)) % tile_count
    estimate = jnp.take(jnp.stack(arrived), source_order, axis=0)
    estimate = jnp.swapaxes(estimate, 0, 1).reshape(planes, tile_count * tile_rows, plane_width)
    plane_bands = lax.dynamic_slice_in_dim(psf_band, my_group * planes, planes, 0)
    views_in_order = (my_group + jnp.arange(view_count, dtype=jnp.int32)) % view_count
    bands = all_bands(
        row_psf[views_in_order][:, plane_bands].reshape(view_count * planes, TAPS),
        col_psf[views_in_order][:, plane_bands].reshape(view_count * planes, TAPS),
        tile_rows * lax.axis_size("tile"),
    )
    for update_index in range(view_count):
        view_index = (my_group + update_index) % view_count
        matrix = interp[view_index]
        landing = route_tile[view_index, :, 0] * tile_blocks + route_block[view_index]
        level = background[view_index]
        estimate = jnp.stack(
            [
                kernel_update(
                    estimate[p],
                    pieces[update_index][p],
                    matrix,
                    landing,
                    [b[update_index * planes + p] for b in bands],
                    level,
                )
                for p in range(planes)
            ]
        )
    return lax.dynamic_slice_in_dim(estimate, my_tile * tile_rows, tile_rows, 1)


def solution(mesh):
    return jax.shard_map(
        local,
        mesh=mesh,
        in_specs=(
            P("view", "tile", None),
            P("view", None, "tile", None),
            P(),
            P(),
            P(),
            P(),
            P(),
            P(),
            P(),
        ),
        out_specs=P("view", "tile", None),
        check_vma=False,
    )
```

```python
import jax
import jax.numpy as jnp
from jax import lax
from jax.sharding import PartitionSpec as P
from jax.experimental import pallas as pl
from jax.experimental.pallas import tpu as pltpu

BR = 8
BW = 128
TAPS = 17


def passed_along(x, axis, by):
    count = lax.axis_size(axis)
    return lax.ppermute(x, axis, [(i, (i + by) % count) for i in range(count)])


def to_blocks(values_in):
    rows, plane_width = values_in.shape
    shaped = values_in.reshape(rows // BR, BR, plane_width // BW, BW)
    return shaped.transpose(0, 2, 1, 3).reshape(-1, BR * BW)


def from_blocks(pieces, rows, plane_width):
    shaped = pieces.reshape(rows // BR, plane_width // BW, BR, BW)
    return shaped.transpose(0, 2, 1, 3).reshape(rows, plane_width)


def banded(taps_in, diff):
    result = jnp.zeros(diff.shape, jnp.float32)
    for tap_index in range(TAPS):
        result = result + jnp.where(diff == tap_index, taps_in[tap_index].astype(jnp.float32), 0.0)
    return result.astype(jnp.bfloat16)


def column_mats(taps_in, flipped):
    radius = (TAPS - 1) // 2
    source_lane = jnp.arange(BW, dtype=jnp.int32)[:, None]
    target_lane = jnp.arange(BW, dtype=jnp.int32)[None, :]
    mats = []
    for offset in (-1, 0, 1):
        if flipped:
            diff = target_lane - source_lane - offset * BW + radius
        else:
            diff = source_lane + offset * BW - target_lane + radius
        mats.append(banded(taps_in, diff))
    return mats


def row_mat(taps_in, rows):
    radius = (TAPS - 1) // 2
    out_row = jnp.arange(rows, dtype=jnp.int32)[:, None]
    src_row = jnp.arange(rows, dtype=jnp.int32)[None, :]
    return banded(taps_in, src_row - out_row + radius)


def column_pass(values_in, mats):
    rows, plane_width = values_in.shape
    col_count = plane_width // BW
    grid_cells = values_in.reshape(rows, col_count, BW)
    padded = jnp.pad(grid_cells, ((0, 0), (1, 1), (0, 0)))
    result_sum = jnp.zeros(grid_cells.shape, jnp.float32)
    for position in range(3):
        result_sum = result_sum + jnp.einsum(
            "rcj,jk->rck",
            padded[:, position : position + col_count],
            mats[position],
            preferred_element_type=jnp.float32,
        )
    return result_sum.reshape(rows, plane_width)


def update_plane(estimate, raw_plane, matrix, landing, row_taps, col_taps, level):
    rows, plane_width = estimate.shape
    blocks = (rows // BR) * (plane_width // BW)
    block_iota = jnp.arange(blocks, dtype=jnp.int32)
    rounded = estimate.astype(jnp.bfloat16).reshape(rows, plane_width // BW, BW)
    moved = jnp.einsum("rcj,jk->rck", rounded, matrix, preferred_element_type=jnp.float32)
    moved = moved.astype(jnp.bfloat16).reshape(rows, plane_width)
    gather_mat = landing[None, :] == block_iota[:, None]
    land_count = jnp.sum(gather_mat.astype(jnp.float32), axis=1)
    summed = jnp.dot(
        gather_mat.astype(jnp.bfloat16), to_blocks(moved), preferred_element_type=jnp.float32
    )
    summed = (summed / jnp.maximum(land_count, 1.0)[:, None]).astype(jnp.bfloat16)
    joined = from_blocks(summed, rows, plane_width)
    across = column_pass(joined, column_mats(col_taps, False)).astype(jnp.bfloat16)
    band = row_mat(row_taps, rows)
    blurred = jnp.dot(band, across, preferred_element_type=jnp.float32) + level
    ratio = (raw_plane.astype(jnp.float32) / blurred).astype(jnp.bfloat16)
    rows_back = jnp.dot(band.T, ratio, preferred_element_type=jnp.float32).astype(jnp.bfloat16)
    spread = column_pass(rows_back, column_mats(col_taps, True)).astype(jnp.bfloat16)
    returned = jnp.einsum(
        "rcj,kj->rck",
        spread.reshape(rows, plane_width // BW, BW),
        matrix,
        preferred_element_type=jnp.float32,
    ).astype(jnp.bfloat16)
    correction = jnp.take(to_blocks(returned.reshape(rows, plane_width)), landing, axis=0)
    return estimate * from_blocks(correction, rows, plane_width).astype(jnp.float32)


def plane_kernel(offs_ref, bg_ref, raw_ref, m_ref, mt_ref, s_ref, cnt_ref, g_ref, bf_ref, bb_ref,
                 a_ref, at_ref, *rest):
    *piece_refs, out_ref, est_whole, work, joined, across, ratio = rest
    rows, plane_width = out_ref.shape
    if len(piece_refs) == 1:
        est_ref = piece_refs[0]
    else:
        est_ref = est_whole
        for k, piece in enumerate(piece_refs):
            piece_rows = piece.shape[0]
            est_ref[pl.ds(pl.multiple_of(offs_ref[k], BR), piece_rows), :] = piece[...]
    nt = rows // BR
    nc = plane_width // BW
    f32 = jnp.float32
    bf16 = jnp.bfloat16

    def cols(c):
        return slice(c * BW, (c + 1) * BW)

    for c in range(nc):
        blk = est_ref[:, cols(c)].astype(bf16)
        moved = jnp.dot(blk, m_ref[...], preferred_element_type=f32)
        work[c] = moved.astype(bf16).astype(f32)

    def regroup(src, mat_ref, dst, post):
        for r in range(BR):
            stacked = jnp.concatenate(
                [src[c, pl.ds(r, nt, stride=BR), :] for c in range(nc)], axis=0
            )
            result = jnp.dot(mat_ref[...], stacked.astype(bf16), preferred_element_type=f32)
            result = post(result)
            for c in range(nc):
                dst[c, pl.ds(r, nt, stride=BR), :] = result[c * nt:(c + 1) * nt, :]

    regroup(work, s_ref, joined,
            lambda v: (v / cnt_ref[...]).astype(bf16).astype(f32))

    def column_blur(take, mats_ref, c):
        total = None
        for offset in (-1, 0, 1):
            if 0 <= c + offset < nc:
                part = jnp.dot(take(c + offset).astype(bf16), mats_ref[offset + 1],
                               preferred_element_type=f32)
                total = part if total is None else total + part
        return total

    for c in range(nc):
        across[:, cols(c)] = column_blur(lambda i: joined[i], bf_ref, c).astype(bf16)
    level = bg_ref[0]
    for c in range(nc):
        blurred = jnp.dot(a_ref[...], across[:, cols(c)], preferred_element_type=f32) + level
        quotient = (raw_ref[:, cols(c)].astype(f32) / blurred).astype(bf16)
        ratio[:, cols(c)] = jnp.dot(at_ref[...], quotient, preferred_element_type=f32).astype(bf16)
    for c in range(nc):
        spread = column_blur(lambda i: ratio[:, cols(i)], bb_ref, c).astype(bf16)
        back = jnp.dot(spread, mt_ref[...], preferred_element_type=f32)
        work[c] = back.astype(bf16).astype(f32)
    regroup(work, g_ref, joined, lambda v: v)
    for c in range(nc):
        out_ref[:, cols(c)] = est_ref[:, cols(c)] * joined[c]


def band_kernel(row_ref, col_ref, a_ref, at_ref, bf_ref, bb_ref):
    count, rows, _ = a_ref.shape
    radius = (TAPS - 1) // 2
    out_row = lax.broadcasted_iota(jnp.int32, (rows, rows), 0)
    src_row = lax.broadcasted_iota(jnp.int32, (rows, rows), 1)
    source_lane = lax.broadcasted_iota(jnp.int32, (BW, BW), 0)
    target_lane = lax.broadcasted_iota(jnp.int32, (BW, BW), 1)

    def build(diff, taps_ref, base):
        result = jnp.zeros(diff.shape, jnp.float32)
        for tap_index in range(TAPS):
            result = jnp.where(diff == tap_index, taps_ref[base + tap_index], result)
        return result.astype(jnp.bfloat16)

    for i in range(count):
        base = i * TAPS
        a_ref[i] = build(src_row - out_row + radius, row_ref, base)
        at_ref[i] = build(out_row - src_row + radius, row_ref, base)
        for offset in (-1, 0, 1):
            forward = source_lane + offset * BW - target_lane + radius
            bf_ref[i, offset + 1] = build(forward, col_ref, base)
            backward = target_lane - source_lane - offset * BW + radius
            bb_ref[i, offset + 1] = build(backward, col_ref, base)


def all_bands(row_taps, col_taps, rows):
    count = row_taps.shape[0]
    smem = pl.BlockSpec(memory_space=pltpu.SMEM)
    vmem = pl.BlockSpec(memory_space=pltpu.VMEM)
    return pl.pallas_call(
        band_kernel,
        out_shape=(
            jax.ShapeDtypeStruct((count, rows, rows), jnp.bfloat16),
            jax.ShapeDtypeStruct((count, rows, rows), jnp.bfloat16),
            jax.ShapeDtypeStruct((count, 3, BW, BW), jnp.bfloat16),
            jax.ShapeDtypeStruct((count, 3, BW, BW), jnp.bfloat16),
        ),
        in_specs=[smem, smem],
        out_specs=(vmem, vmem, vmem, vmem),
    )(row_taps.astype(jnp.float32).reshape(-1), col_taps.astype(jnp.float32).reshape(-1))


def kernel_update(est_pieces, offsets, raw_all, raw_index, matrix, landing, bands, level):
    rows, plane_width = raw_all.shape[-2:]
    nt = rows // BR
    nc = plane_width // BW
    blocks = nt * nc
    order = landing.reshape(nt, nc).T.reshape(-1)
    place = (order % nc) * nt + order // nc
    spots = jnp.arange(blocks, dtype=jnp.int32)
    sum_mat = place[None, :] == spots[:, None]
    pick_mat = place[:, None] == spots[None, :]
    count = jnp.sum(sum_mat.astype(jnp.float32), axis=1)
    count = jnp.broadcast_to(jnp.maximum(count, 1.0)[:, None], (blocks, BW))
    vmem = pl.BlockSpec(memory_space=pltpu.VMEM)
    smem = pl.BlockSpec(memory_space=pltpu.SMEM)
    raw_spec = pl.BlockSpec((None, None, rows, plane_width), lambda i: raw_index + (0, 0))
    return pl.pallas_call(
        plane_kernel,
        grid=(1,),
        out_shape=jax.ShapeDtypeStruct((rows, plane_width), jnp.float32),
        in_specs=[smem, smem, raw_spec] + [vmem] * (9 + len(est_pieces)),
        out_specs=vmem,
        scratch_shapes=[
            pltpu.VMEM((rows, plane_width), jnp.float32),
            pltpu.VMEM((nc, rows, BW), jnp.float32),
            pltpu.VMEM((nc, rows, BW), jnp.float32),
            pltpu.VMEM((rows, plane_width), jnp.bfloat16),
            pltpu.VMEM((rows, plane_width), jnp.bfloat16),
        ],
        compiler_params=pltpu.CompilerParams(vmem_limit_bytes=48 * 1024 * 1024),
        cost_estimate=pl.CostEstimate(
            flops=2 * rows * plane_width * (4 * BW + 2 * rows + 2 * blocks // BR * BR),
            bytes_accessed=rows * plane_width * 10,
            transcendentals=0,
        ),
    )(
        offsets,
        jnp.reshape(level, (1,)).astype(jnp.float32),
        raw_all,
        matrix,
        matrix.T,
        sum_mat.astype(jnp.bfloat16),
        count,
        pick_mat.astype(jnp.bfloat16),
        bands[2],
        bands[3],
        bands[0],
        bands[1],
        *est_pieces,
    )


def with_halo(cells, sides, width):
    for axis, dim in sides:
        count = lax.axis_size(axis)
        ends = count - 1
        head = lax.slice_in_dim(cells, 0, width, axis=dim)
        tail = lax.slice_in_dim(cells, cells.shape[dim] - width, cells.shape[dim], axis=dim)
        cells = jnp.concatenate(
            [
                lax.ppermute(tail, axis, [(i, (i + 1) % count) for i in range(ends)]),
                cells,
                lax.ppermute(head, axis, [((i + 1) % count, i) for i in range(ends)]),
            ],
            axis=dim,
        )
    return cells


def sharded_to_blocks(values_in):
    planes, tile_rows, plane_width = values_in.shape
    shaped = values_in.reshape(planes, tile_rows // BR, BR, plane_width // BW, BW)
    return shaped.transpose(1, 3, 0, 2, 4).reshape(-1, planes, BR, BW)


def sharded_from_blocks(pieces, tile_rows, plane_width):
    planes = pieces.shape[1]
    shaped = pieces.reshape(tile_rows // BR, plane_width // BW, planes, BR, BW)
    return shaped.transpose(2, 0, 3, 1, 4).reshape(planes, tile_rows, plane_width)


def sharded_column_pass(values_in, taps_in, flipped):
    planes, tile_rows, plane_width = values_in.shape
    radius = (taps_in.shape[1] - 1) // 2
    lane_iota = jnp.arange(BW, dtype=jnp.int32)
    source_lane = lane_iota[:, None]
    target_lane = lane_iota[None, :]
    zero_bf = jnp.zeros((), jnp.bfloat16)
    band_mats = []
    for offset in (-1, 0, 1):
        if flipped:
            tap_index = target_lane - source_lane - offset * BW + radius
        else:
            tap_index = source_lane + offset * BW - target_lane + radius
        inside = (tap_index >= 0) & (tap_index <= 2 * radius)
        picked = taps_in[:, jnp.clip(tap_index, 0, 2 * radius)]
        band_mats.append(jnp.where(inside[None, :, :], picked, zero_bf))
    col_count = plane_width // BW
    grid_cells = values_in.reshape(planes, tile_rows, col_count, BW)
    padded = jnp.pad(grid_cells, ((0, 0), (0, 0), (1, 1), (0, 0)))
    result_sum = jnp.zeros(grid_cells.shape, jnp.float32)
    for position in range(3):
        result_sum = result_sum + jnp.einsum(
            "prcj,pjk->prck",
            padded[:, :, position : position + col_count],
            band_mats[position],
            preferred_element_type=jnp.float32,
        )
    return result_sum.reshape(planes, tile_rows, plane_width)


def row_pass(padded, taps_in, flipped):
    planes, extended, plane_width = padded.shape
    radius = (taps_in.shape[1] - 1) // 2
    tile_rows = extended - 2 * radius
    row_iota = jnp.arange(tile_rows, dtype=jnp.int32)[:, None]
    src_iota = jnp.arange(extended, dtype=jnp.int32)[None, :]
    if flipped:
        tap_index = row_iota + 2 * radius - src_iota
    else:
        tap_index = src_iota - row_iota
    inside = (tap_index >= 0) & (tap_index <= 2 * radius)
    band_rows = jnp.where(
        inside[None, :, :],
        taps_in[:, jnp.clip(tap_index, 0, 2 * radius)],
        jnp.zeros((), jnp.bfloat16),
    )
    return jnp.einsum("prs,psw->prw", band_rows, padded, preferred_element_type=jnp.float32)


def sharded_update(
    estimate,
    raw_piece,
    view_index,
    slab_index,
    route_tile,
    route_block,
    interp,
    row_psf,
    col_psf,
    psf_band,
    background,
):
    tile_count = lax.axis_size("tile")
    my_tile = lax.axis_index("tile")
    planes, tile_rows, plane_width = estimate.shape
    blocks = tile_rows // BR * (plane_width // BW)
    capacity = max(2, 2 * blocks // tile_count)
    radius = (TAPS - 1) // 2
    matrix = interp[view_index]
    dest_tile = route_tile[view_index, :, 0].reshape(tile_count, blocks)
    dest_block = route_block[view_index].reshape(tile_count, blocks)
    tiles_iota = jnp.arange(tile_count, dtype=jnp.int32)
    one_hot = (dest_tile[:, :, None] == tiles_iota[None, None, :]).astype(jnp.int32)
    slot_rank = jnp.sum((jnp.cumsum(one_hot, axis=1) - one_hot) * one_hot, axis=2)
    slot_index = dest_tile * capacity + slot_rank
    my_slots = slot_index[my_tile]
    slots_iota = jnp.arange(tile_count * capacity, dtype=jnp.int32)
    block_iota = jnp.arange(blocks, dtype=jnp.int32)
    match_send = my_slots[None, :] == slots_iota[:, None]
    send_ok = jnp.any(match_send, axis=1)
    send_src = jnp.sum(jnp.where(match_send, block_iota[None, :], 0), axis=1)
    match_recv = (dest_tile == my_tile)[:, None, :] & (
        slot_rank[:, None, :] == jnp.arange(capacity, dtype=jnp.int32)[None, :, None]
    )
    recv_ok = jnp.any(match_recv, axis=2).reshape(-1)
    recv_off = jnp.sum(jnp.where(match_recv, dest_block[:, None, :], 0), axis=2).reshape(-1)
    zero_bf = jnp.zeros((), jnp.bfloat16)
    rounded_estimate = estimate.astype(jnp.bfloat16)
    interpolated = jnp.einsum(
        "bprj,jk->bprk", sharded_to_blocks(rounded_estimate), matrix, preferred_element_type=jnp.float32
    ).astype(jnp.bfloat16)
    outgoing = jnp.where(send_ok[:, None, None, None], interpolated[send_src], zero_bf)
    outgoing = outgoing.reshape(tile_count, capacity, planes, BR, BW)
    incoming = lax.all_to_all(outgoing, "tile", split_axis=0, concat_axis=0, tiled=True)
    incoming = incoming.reshape(tile_count * capacity, planes * BR * BW)
    landing = (recv_off[None, :] == block_iota[:, None]) & recv_ok[None, :]
    land_count = jnp.sum(landing.astype(jnp.float32), axis=1)
    summed = jnp.dot(landing.astype(jnp.bfloat16), incoming, preferred_element_type=jnp.float32)
    summed = (summed / jnp.maximum(land_count, 1.0)[:, None]).astype(jnp.bfloat16)
    joined_field = sharded_from_blocks(summed.reshape(blocks, planes, BR, BW), tile_rows, plane_width)
    plane_bands = lax.dynamic_slice_in_dim(psf_band, slab_index * planes, planes, 0)
    row_taps = row_psf[view_index][plane_bands]
    col_taps = col_psf[view_index][plane_bands]
    across = sharded_column_pass(joined_field, col_taps, False).astype(jnp.bfloat16)
    padded = with_halo(across, (("tile", 1),), radius)
    blurred = row_pass(padded, row_taps, False) + background[view_index]
    ratio_field = (raw_piece.astype(jnp.float32) / blurred).astype(jnp.bfloat16)
    padded_ratio = with_halo(ratio_field, (("tile", 1),), radius)
    rows_back = row_pass(padded_ratio, row_taps, True).astype(jnp.bfloat16)
    spread = sharded_column_pass(rows_back, col_taps, True).astype(jnp.bfloat16)
    returned_blocks = jnp.einsum(
        "bprj,kj->bprk", sharded_to_blocks(spread), matrix, preferred_element_type=jnp.float32
    ).astype(jnp.bfloat16)
    returning = jnp.where(recv_ok[:, None, None, None], returned_blocks[recv_off], zero_bf)
    returning = returning.reshape(tile_count, capacity, planes, BR, BW)
    arrived = lax.all_to_all(returning, "tile", split_axis=0, concat_axis=0, tiled=True)
    arrived = arrived.reshape(tile_count * capacity, planes, BR, BW)
    correction = arrived[my_slots]
    return estimate * sharded_from_blocks(correction.astype(jnp.float32), tile_rows, plane_width)


def local(
    initial_estimate,
    raw_views,
    route_tile,
    route_block,
    interp,
    row_kernel,
    col_kernel,
    psf_band,
    background,
):
    view_count = lax.axis_size("view")
    my_group = lax.axis_index("view")
    my_tile = lax.axis_index("tile")
    planes, tile_rows, plane_width = initial_estimate.shape
    tile_blocks = (tile_rows // BR) * (plane_width // BW)
    row_psf = (row_kernel / jnp.sum(row_kernel, axis=2, keepdims=True)).astype(jnp.bfloat16)
    col_psf = (col_kernel / jnp.sum(col_kernel, axis=2, keepdims=True)).astype(jnp.bfloat16)
    if view_count * tile_rows * plane_width * lax.axis_size("tile") > (1 << 22):
        estimate = initial_estimate
        for update_index in range(view_count):
            view_index = (my_group + update_index) % view_count
            own_piece = lax.dynamic_slice_in_dim(
                raw_views[0], (my_group - update_index) % view_count * planes, planes, 0
            )
            raw_piece = (
                own_piece if update_index == 0 else passed_along(own_piece, "view", -update_index)
            )
            estimate = sharded_update(
                estimate, raw_piece, view_index, my_group, route_tile, route_block,
                interp, row_psf, col_psf, psf_band, background,
            )
        return estimate
    pieces = []
    for update_index in range(view_count):
        own_piece = lax.dynamic_slice_in_dim(
            raw_views[0], (my_group - update_index) % view_count * planes, planes, 0
        )
        piece = own_piece if update_index == 0 else passed_along(own_piece, "view", -update_index)
        pieces.append(piece)
    pieces = lax.all_gather(jnp.stack(pieces), "tile", axis=2, tiled=True)
    tile_count = lax.axis_size("tile")
    arrived = [initial_estimate] + [
        passed_along(initial_estimate, "tile", shift) for shift in range(1, tile_count)
    ]
    offsets = (my_tile - jnp.arange(tile_count, dtype=jnp.int32)) % tile_count * tile_rows
    whole_plane = jnp.zeros((1,), jnp.int32)
    plane_bands = lax.dynamic_slice_in_dim(psf_band, my_group * planes, planes, 0)
    views_in_order = (my_group + jnp.arange(view_count, dtype=jnp.int32)) % view_count
    bands = all_bands(
        row_psf[views_in_order][:, plane_bands].reshape(view_count * planes, TAPS),
        col_psf[views_in_order][:, plane_bands].reshape(view_count * planes, TAPS),
        tile_rows * lax.axis_size("tile"),
    )
    for update_index in range(view_count):
        view_index = (my_group + update_index) % view_count
        matrix = interp[view_index]
        landing = route_tile[view_index, :, 0] * tile_blocks + route_block[view_index]
        level = background[view_index]
        estimate = jnp.stack(
            [
                kernel_update(
                    [piece[p] for piece in arrived] if update_index == 0 else [estimate[p]],
                    offsets if update_index == 0 else whole_plane,
                    pieces,
                    (update_index, p),
                    matrix,
                    landing,
                    [b[update_index * planes + p] for b in bands],
                    level,
                )
                for p in range(planes)
            ]
        )
    return lax.dynamic_slice_in_dim(estimate, my_tile * tile_rows, tile_rows, 1)


def solution(mesh):
    return jax.shard_map(
        local,
        mesh=mesh,
        in_specs=(
            P("view", "tile", None),
            P("view", None, "tile", None),
            P(),
            P(),
            P(),
            P(),
            P(),
            P(),
            P(),
        ),
        out_specs=P("view", "tile", None),
        check_vma=False,
    )
```

```python
import jax
import jax.numpy as jnp
from jax import lax
from jax.sharding import PartitionSpec as P
from jax.experimental import pallas as pl
from jax.experimental.pallas import tpu as pltpu

BR = 8
BW = 128
TAPS = 17


def passed_along(x, axis, by):
    count = lax.axis_size(axis)
    return lax.ppermute(x, axis, [(i, (i + by) % count) for i in range(count)])


def to_blocks(values_in):
    rows, plane_width = values_in.shape
    shaped = values_in.reshape(rows // BR, BR, plane_width // BW, BW)
    return shaped.transpose(0, 2, 1, 3).reshape(-1, BR * BW)


def from_blocks(pieces, rows, plane_width):
    shaped = pieces.reshape(rows // BR, plane_width // BW, BR, BW)
    return shaped.transpose(0, 2, 1, 3).reshape(rows, plane_width)


def banded(taps_in, diff):
    result = jnp.zeros(diff.shape, jnp.float32)
    for tap_index in range(TAPS):
        result = result + jnp.where(diff == tap_index, taps_in[tap_index].astype(jnp.float32), 0.0)
    return result.astype(jnp.bfloat16)


def column_mats(taps_in, flipped):
    radius = (TAPS - 1) // 2
    source_lane = jnp.arange(BW, dtype=jnp.int32)[:, None]
    target_lane = jnp.arange(BW, dtype=jnp.int32)[None, :]
    mats = []
    for offset in (-1, 0, 1):
        if flipped:
            diff = target_lane - source_lane - offset * BW + radius
        else:
            diff = source_lane + offset * BW - target_lane + radius
        mats.append(banded(taps_in, diff))
    return mats


def row_mat(taps_in, rows):
    radius = (TAPS - 1) // 2
    out_row = jnp.arange(rows, dtype=jnp.int32)[:, None]
    src_row = jnp.arange(rows, dtype=jnp.int32)[None, :]
    return banded(taps_in, src_row - out_row + radius)


def column_pass(values_in, mats):
    rows, plane_width = values_in.shape
    col_count = plane_width // BW
    grid_cells = values_in.reshape(rows, col_count, BW)
    padded = jnp.pad(grid_cells, ((0, 0), (1, 1), (0, 0)))
    result_sum = jnp.zeros(grid_cells.shape, jnp.float32)
    for position in range(3):
        result_sum = result_sum + jnp.einsum(
            "rcj,jk->rck",
            padded[:, position : position + col_count],
            mats[position],
            preferred_element_type=jnp.float32,
        )
    return result_sum.reshape(rows, plane_width)


def update_plane(estimate, raw_plane, matrix, landing, row_taps, col_taps, level):
    rows, plane_width = estimate.shape
    blocks = (rows // BR) * (plane_width // BW)
    block_iota = jnp.arange(blocks, dtype=jnp.int32)
    rounded = estimate.astype(jnp.bfloat16).reshape(rows, plane_width // BW, BW)
    moved = jnp.einsum("rcj,jk->rck", rounded, matrix, preferred_element_type=jnp.float32)
    moved = moved.astype(jnp.bfloat16).reshape(rows, plane_width)
    gather_mat = landing[None, :] == block_iota[:, None]
    land_count = jnp.sum(gather_mat.astype(jnp.float32), axis=1)
    summed = jnp.dot(
        gather_mat.astype(jnp.bfloat16), to_blocks(moved), preferred_element_type=jnp.float32
    )
    summed = (summed / jnp.maximum(land_count, 1.0)[:, None]).astype(jnp.bfloat16)
    joined = from_blocks(summed, rows, plane_width)
    across = column_pass(joined, column_mats(col_taps, False)).astype(jnp.bfloat16)
    band = row_mat(row_taps, rows)
    blurred = jnp.dot(band, across, preferred_element_type=jnp.float32) + level
    ratio = (raw_plane.astype(jnp.float32) / blurred).astype(jnp.bfloat16)
    rows_back = jnp.dot(band.T, ratio, preferred_element_type=jnp.float32).astype(jnp.bfloat16)
    spread = column_pass(rows_back, column_mats(col_taps, True)).astype(jnp.bfloat16)
    returned = jnp.einsum(
        "rcj,kj->rck",
        spread.reshape(rows, plane_width // BW, BW),
        matrix,
        preferred_element_type=jnp.float32,
    ).astype(jnp.bfloat16)
    correction = jnp.take(to_blocks(returned.reshape(rows, plane_width)), landing, axis=0)
    return estimate * from_blocks(correction, rows, plane_width).astype(jnp.float32)


def plane_kernel(offs_ref, bg_ref, raw_ref, m_ref, mt_ref, s_ref, cnt_ref, g_ref, bf_ref, bb_ref,
                 a_ref, at_ref, *rest):
    *piece_refs, out_ref, est_whole, work, joined, across, ratio = rest
    rows, plane_width = out_ref.shape
    if len(piece_refs) == 1:
        est_ref = piece_refs[0]
    else:
        est_ref = est_whole
        for k, piece in enumerate(piece_refs):
            piece_rows = piece.shape[0]
            est_ref[pl.ds(pl.multiple_of(offs_ref[k], BR), piece_rows), :] = piece[...]
    nt = rows // BR
    nc = plane_width // BW
    f32 = jnp.float32
    bf16 = jnp.bfloat16

    def cols(c):
        return slice(c * BW, (c + 1) * BW)

    for c in range(nc):
        blk = est_ref[:, cols(c)].astype(bf16)
        moved = jnp.dot(blk, m_ref[...], preferred_element_type=f32)
        work[c] = moved.astype(bf16).astype(f32)

    def regroup(src, mat_ref, dst, post):
        for r in range(BR):
            stacked = jnp.concatenate(
                [src[c, pl.ds(r, nt, stride=BR), :] for c in range(nc)], axis=0
            )
            result = jnp.dot(mat_ref[...], stacked.astype(bf16), preferred_element_type=f32)
            result = post(result)
            for c in range(nc):
                dst[c, pl.ds(r, nt, stride=BR), :] = result[c * nt:(c + 1) * nt, :]

    regroup(work, s_ref, joined,
            lambda v: (v / cnt_ref[...]).astype(bf16).astype(f32))

    def column_blur(take, mats_ref, c):
        total = None
        for offset in (-1, 0, 1):
            if 0 <= c + offset < nc:
                part = jnp.dot(take(c + offset).astype(bf16), mats_ref[offset + 1],
                               preferred_element_type=f32)
                total = part if total is None else total + part
        return total

    for c in range(nc):
        across[:, cols(c)] = column_blur(lambda i: joined[i], bf_ref, c).astype(bf16)
    level = bg_ref[0]
    for c in range(nc):
        blurred = jnp.dot(a_ref[...], across[:, cols(c)], preferred_element_type=f32) + level
        quotient = (raw_ref[:, cols(c)].astype(f32) / blurred).astype(bf16)
        ratio[:, cols(c)] = jnp.dot(at_ref[...], quotient, preferred_element_type=f32).astype(bf16)
    for c in range(nc):
        spread = column_blur(lambda i: ratio[:, cols(i)], bb_ref, c).astype(bf16)
        back = jnp.dot(spread, mt_ref[...], preferred_element_type=f32)
        work[c] = back.astype(bf16).astype(f32)
    regroup(work, g_ref, joined, lambda v: v)
    for c in range(nc):
        out_ref[:, cols(c)] = est_ref[:, cols(c)] * joined[c]


def band_kernel(row_ref, col_ref, a_ref, at_ref, bf_ref, bb_ref):
    count, rows, _ = a_ref.shape
    radius = (TAPS - 1) // 2
    out_row = lax.broadcasted_iota(jnp.int32, (rows, rows), 0)
    src_row = lax.broadcasted_iota(jnp.int32, (rows, rows), 1)
    source_lane = lax.broadcasted_iota(jnp.int32, (BW, BW), 0)
    target_lane = lax.broadcasted_iota(jnp.int32, (BW, BW), 1)

    def build(diff, taps_ref, base):
        result = jnp.zeros(diff.shape, jnp.float32)
        for tap_index in range(TAPS):
            result = jnp.where(diff == tap_index, taps_ref[base + tap_index], result)
        return result.astype(jnp.bfloat16)

    for i in range(count):
        base = i * TAPS
        a_ref[i] = build(src_row - out_row + radius, row_ref, base)
        at_ref[i] = build(out_row - src_row + radius, row_ref, base)
        for offset in (-1, 0, 1):
            forward = source_lane + offset * BW - target_lane + radius
            bf_ref[i, offset + 1] = build(forward, col_ref, base)
            backward = target_lane - source_lane - offset * BW + radius
            bb_ref[i, offset + 1] = build(backward, col_ref, base)


def all_bands(row_taps, col_taps, rows):
    count = row_taps.shape[0]
    smem = pl.BlockSpec(memory_space=pltpu.SMEM)
    vmem = pl.BlockSpec(memory_space=pltpu.VMEM)
    return pl.pallas_call(
        band_kernel,
        out_shape=(
            jax.ShapeDtypeStruct((count, rows, rows), jnp.bfloat16),
            jax.ShapeDtypeStruct((count, rows, rows), jnp.bfloat16),
            jax.ShapeDtypeStruct((count, 3, BW, BW), jnp.bfloat16),
            jax.ShapeDtypeStruct((count, 3, BW, BW), jnp.bfloat16),
        ),
        in_specs=[smem, smem],
        out_specs=(vmem, vmem, vmem, vmem),
    )(row_taps.astype(jnp.float32).reshape(-1), col_taps.astype(jnp.float32).reshape(-1))


def kernel_update(est_pieces, offsets, raw_all, raw_index, matrix, landing, bands, level):
    rows, plane_width = raw_all.shape[-2:]
    nt = rows // BR
    nc = plane_width // BW
    blocks = nt * nc
    order = landing.reshape(nt, nc).T.reshape(-1)
    place = (order % nc) * nt + order // nc
    spots = jnp.arange(blocks, dtype=jnp.int32)
    sum_mat = place[None, :] == spots[:, None]
    pick_mat = place[:, None] == spots[None, :]
    count = jnp.sum(sum_mat.astype(jnp.float32), axis=1)
    count = jnp.broadcast_to(jnp.maximum(count, 1.0)[:, None], (blocks, BW))
    vmem = pl.BlockSpec(memory_space=pltpu.VMEM)
    smem = pl.BlockSpec(memory_space=pltpu.SMEM)
    raw_spec = pl.BlockSpec((None, None, rows, plane_width), lambda i: raw_index + (0, 0))
    return pl.pallas_call(
        plane_kernel,
        grid=(1,),
        out_shape=jax.ShapeDtypeStruct((rows, plane_width), jnp.float32),
        in_specs=[smem, smem, raw_spec] + [vmem] * (9 + len(est_pieces)),
        out_specs=vmem,
        scratch_shapes=[
            pltpu.VMEM((rows, plane_width), jnp.float32),
            pltpu.VMEM((nc, rows, BW), jnp.float32),
            pltpu.VMEM((nc, rows, BW), jnp.float32),
            pltpu.VMEM((rows, plane_width), jnp.bfloat16),
            pltpu.VMEM((rows, plane_width), jnp.bfloat16),
        ],
        compiler_params=pltpu.CompilerParams(vmem_limit_bytes=48 * 1024 * 1024),
        cost_estimate=pl.CostEstimate(
            flops=2 * rows * plane_width * (4 * BW + 2 * rows + 2 * blocks // BR * BR),
            bytes_accessed=rows * plane_width * 10,
            transcendentals=0,
        ),
    )(
        offsets,
        jnp.reshape(level, (1,)).astype(jnp.float32),
        raw_all,
        matrix,
        matrix.T,
        sum_mat.astype(jnp.bfloat16),
        count,
        pick_mat.astype(jnp.bfloat16),
        bands[2],
        bands[3],
        bands[0],
        bands[1],
        *est_pieces,
    )


def with_halo(cells, sides, width):
    for axis, dim in sides:
        count = lax.axis_size(axis)
        ends = count - 1
        head = lax.slice_in_dim(cells, 0, width, axis=dim)
        tail = lax.slice_in_dim(cells, cells.shape[dim] - width, cells.shape[dim], axis=dim)
        cells = jnp.concatenate(
            [
                lax.ppermute(tail, axis, [(i, (i + 1) % count) for i in range(ends)]),
                cells,
                lax.ppermute(head, axis, [((i + 1) % count, i) for i in range(ends)]),
            ],
            axis=dim,
        )
    return cells


def sharded_to_blocks(values_in):
    planes, tile_rows, plane_width = values_in.shape
    shaped = values_in.reshape(planes, tile_rows // BR, BR, plane_width // BW, BW)
    return shaped.transpose(1, 3, 0, 2, 4).reshape(-1, planes, BR, BW)


def sharded_from_blocks(pieces, tile_rows, plane_width):
    planes = pieces.shape[1]
    shaped = pieces.reshape(tile_rows // BR, plane_width // BW, planes, BR, BW)
    return shaped.transpose(2, 0, 3, 1, 4).reshape(planes, tile_rows, plane_width)


def sharded_column_pass(values_in, taps_in, flipped):
    planes, tile_rows, plane_width = values_in.shape
    radius = (taps_in.shape[1] - 1) // 2
    lane_iota = jnp.arange(BW, dtype=jnp.int32)
    source_lane = lane_iota[:, None]
    target_lane = lane_iota[None, :]
    zero_bf = jnp.zeros((), jnp.bfloat16)
    band_mats = []
    for offset in (-1, 0, 1):
        if flipped:
            tap_index = target_lane - source_lane - offset * BW + radius
        else:
            tap_index = source_lane + offset * BW - target_lane + radius
        inside = (tap_index >= 0) & (tap_index <= 2 * radius)
        picked = taps_in[:, jnp.clip(tap_index, 0, 2 * radius)]
        band_mats.append(jnp.where(inside[None, :, :], picked, zero_bf))
    col_count = plane_width // BW
    grid_cells = values_in.reshape(planes, tile_rows, col_count, BW)
    padded = jnp.pad(grid_cells, ((0, 0), (0, 0), (1, 1), (0, 0)))
    result_sum = jnp.zeros(grid_cells.shape, jnp.float32)
    for position in range(3):
        result_sum = result_sum + jnp.einsum(
            "prcj,pjk->prck",
            padded[:, :, position : position + col_count],
            band_mats[position],
            preferred_element_type=jnp.float32,
        )
    return result_sum.reshape(planes, tile_rows, plane_width)


def row_pass(padded, taps_in, flipped):
    planes, extended, plane_width = padded.shape
    radius = (taps_in.shape[1] - 1) // 2
    tile_rows = extended - 2 * radius
    row_iota = jnp.arange(tile_rows, dtype=jnp.int32)[:, None]
    src_iota = jnp.arange(extended, dtype=jnp.int32)[None, :]
    if flipped:
        tap_index = row_iota + 2 * radius - src_iota
    else:
        tap_index = src_iota - row_iota
    inside = (tap_index >= 0) & (tap_index <= 2 * radius)
    band_rows = jnp.where(
        inside[None, :, :],
        taps_in[:, jnp.clip(tap_index, 0, 2 * radius)],
        jnp.zeros((), jnp.bfloat16),
    )
    return jnp.einsum("prs,psw->prw", band_rows, padded, preferred_element_type=jnp.float32)


def sharded_update(
    estimate,
    raw_piece,
    view_index,
    slab_index,
    route_tile,
    route_block,
    interp,
    row_psf,
    col_psf,
    psf_band,
    background,
):
    tile_count = lax.axis_size("tile")
    my_tile = lax.axis_index("tile")
    planes, tile_rows, plane_width = estimate.shape
    blocks = tile_rows // BR * (plane_width // BW)
    capacity = max(2, 2 * blocks // tile_count)
    radius = (TAPS - 1) // 2
    matrix = interp[view_index]
    dest_tile = route_tile[view_index, :, 0].reshape(tile_count, blocks)
    dest_block = route_block[view_index].reshape(tile_count, blocks)
    tiles_iota = jnp.arange(tile_count, dtype=jnp.int32)
    one_hot = (dest_tile[:, :, None] == tiles_iota[None, None, :]).astype(jnp.int32)
    slot_rank = jnp.sum((jnp.cumsum(one_hot, axis=1) - one_hot) * one_hot, axis=2)
    slot_index = dest_tile * capacity + slot_rank
    my_slots = slot_index[my_tile]
    slots_iota = jnp.arange(tile_count * capacity, dtype=jnp.int32)
    block_iota = jnp.arange(blocks, dtype=jnp.int32)
    match_send = my_slots[None, :] == slots_iota[:, None]
    send_ok = jnp.any(match_send, axis=1)
    send_src = jnp.sum(jnp.where(match_send, block_iota[None, :], 0), axis=1)
    match_recv = (dest_tile == my_tile)[:, None, :] & (
        slot_rank[:, None, :] == jnp.arange(capacity, dtype=jnp.int32)[None, :, None]
    )
    recv_ok = jnp.any(match_recv, axis=2).reshape(-1)
    recv_off = jnp.sum(jnp.where(match_recv, dest_block[:, None, :], 0), axis=2).reshape(-1)
    zero_bf = jnp.zeros((), jnp.bfloat16)
    rounded_estimate = estimate.astype(jnp.bfloat16)
    interpolated = jnp.einsum(
        "bprj,jk->bprk", sharded_to_blocks(rounded_estimate), matrix, preferred_element_type=jnp.float32
    ).astype(jnp.bfloat16)
    outgoing = jnp.where(send_ok[:, None, None, None], interpolated[send_src], zero_bf)
    outgoing = outgoing.reshape(tile_count, capacity, planes, BR, BW)
    incoming = lax.all_to_all(outgoing, "tile", split_axis=0, concat_axis=0, tiled=True)
    incoming = incoming.reshape(tile_count * capacity, planes * BR * BW)
    landing = (recv_off[None, :] == block_iota[:, None]) & recv_ok[None, :]
    land_count = jnp.sum(landing.astype(jnp.float32), axis=1)
    summed = jnp.dot(landing.astype(jnp.bfloat16), incoming, preferred_element_type=jnp.float32)
    summed = (summed / jnp.maximum(land_count, 1.0)[:, None]).astype(jnp.bfloat16)
    joined_field = sharded_from_blocks(summed.reshape(blocks, planes, BR, BW), tile_rows, plane_width)
    plane_bands = lax.dynamic_slice_in_dim(psf_band, slab_index * planes, planes, 0)
    row_taps = row_psf[view_index][plane_bands]
    col_taps = col_psf[view_index][plane_bands]
    across = sharded_column_pass(joined_field, col_taps, False).astype(jnp.bfloat16)
    padded = with_halo(across, (("tile", 1),), radius)
    blurred = row_pass(padded, row_taps, False) + background[view_index]
    ratio_field = (raw_piece.astype(jnp.float32) / blurred).astype(jnp.bfloat16)
    padded_ratio = with_halo(ratio_field, (("tile", 1),), radius)
    rows_back = row_pass(padded_ratio, row_taps, True).astype(jnp.bfloat16)
    spread = sharded_column_pass(rows_back, col_taps, True).astype(jnp.bfloat16)
    returned_blocks = jnp.einsum(
        "bprj,kj->bprk", sharded_to_blocks(spread), matrix, preferred_element_type=jnp.float32
    ).astype(jnp.bfloat16)
    returning = jnp.where(recv_ok[:, None, None, None], returned_blocks[recv_off], zero_bf)
    returning = returning.reshape(tile_count, capacity, planes, BR, BW)
    arrived = lax.all_to_all(returning, "tile", split_axis=0, concat_axis=0, tiled=True)
    arrived = arrived.reshape(tile_count * capacity, planes, BR, BW)
    correction = arrived[my_slots]
    return estimate * sharded_from_blocks(correction.astype(jnp.float32), tile_rows, plane_width)


def local(
    initial_estimate,
    raw_views,
    route_tile,
    route_block,
    interp,
    row_kernel,
    col_kernel,
    psf_band,
    background,
):
    view_count = lax.axis_size("view")
    my_group = lax.axis_index("view")
    my_tile = lax.axis_index("tile")
    planes, tile_rows, plane_width = initial_estimate.shape
    tile_blocks = (tile_rows // BR) * (plane_width // BW)
    row_psf = (row_kernel / jnp.sum(row_kernel, axis=2, keepdims=True)).astype(jnp.bfloat16)
    col_psf = (col_kernel / jnp.sum(col_kernel, axis=2, keepdims=True)).astype(jnp.bfloat16)
    if view_count * tile_rows * plane_width * lax.axis_size("tile") > (1 << 22):
        estimate = initial_estimate
        for update_index in range(view_count):
            view_index = (my_group + update_index) % view_count
            own_piece = lax.dynamic_slice_in_dim(
                raw_views[0], (my_group - update_index) % view_count * planes, planes, 0
            )
            raw_piece = (
                own_piece if update_index == 0 else passed_along(own_piece, "view", -update_index)
            )
            estimate = sharded_update(
                estimate, raw_piece, view_index, my_group, route_tile, route_block,
                interp, row_psf, col_psf, psf_band, background,
            )
        return estimate
    pieces = []
    for update_index in range(view_count):
        own_piece = lax.dynamic_slice_in_dim(
            raw_views[0], (my_group - update_index) % view_count * planes, planes, 0
        )
        piece = own_piece if update_index == 0 else passed_along(own_piece, "view", -update_index)
        pieces.append(piece)
    first_raw = lax.all_gather(jnp.stack(pieces[:1]), "tile", axis=2, tiled=True)
    later_raw = lax.all_gather(jnp.stack(pieces[1:]), "tile", axis=2, tiled=True)
    tile_count = lax.axis_size("tile")
    along = [initial_estimate] + [
        passed_along(initial_estimate, "tile", shift) for shift in range(2, tile_count, 2)
    ]
    partner = [(i, i ^ 1) for i in range(tile_count)]
    arrived = along + [lax.ppermute(piece, "tile", partner) for piece in along]
    sources = [(my_tile - shift) % tile_count for shift in range(0, tile_count, 2)]
    sources = sources + [(source ^ 1) for source in sources]
    offsets = jnp.stack(sources).astype(jnp.int32) * tile_rows
    whole_plane = jnp.zeros((1,), jnp.int32)
    plane_bands = lax.dynamic_slice_in_dim(psf_band, my_group * planes, planes, 0)
    views_in_order = (my_group + jnp.arange(view_count, dtype=jnp.int32)) % view_count
    bands = all_bands(
        row_psf[views_in_order][:, plane_bands].reshape(view_count * planes, TAPS),
        col_psf[views_in_order][:, plane_bands].reshape(view_count * planes, TAPS),
        tile_rows * lax.axis_size("tile"),
    )
    for update_index in range(view_count):
        view_index = (my_group + update_index) % view_count
        matrix = interp[view_index]
        landing = route_tile[view_index, :, 0] * tile_blocks + route_block[view_index]
        level = background[view_index]
        estimate = jnp.stack(
            [
                kernel_update(
                    [piece[p] for piece in arrived] if update_index == 0 else [estimate[p]],
                    offsets if update_index == 0 else whole_plane,
                    first_raw if update_index == 0 else later_raw,
                    (0 if update_index == 0 else update_index - 1, p),
                    matrix,
                    landing,
                    [b[update_index * planes + p] for b in bands],
                    level,
                )
                for p in range(planes)
            ]
        )
    return lax.dynamic_slice_in_dim(estimate, my_tile * tile_rows, tile_rows, 1)


def solution(mesh):
    return jax.shard_map(
        local,
        mesh=mesh,
        in_specs=(
            P("view", "tile", None),
            P("view", None, "tile", None),
            P(),
            P(),
            P(),
            P(),
            P(),
            P(),
            P(),
        ),
        out_specs=P("view", "tile", None),
        check_vma=False,
    )
```

```python
import functools

import jax
import jax.numpy as jnp
from jax import lax
from jax.sharding import PartitionSpec as P
from jax.experimental import pallas as pl
from jax.experimental.pallas import tpu as pltpu

BR = 8
BW = 128
TAPS = 17


def passed_along(x, axis, by):
    count = lax.axis_size(axis)
    return lax.ppermute(x, axis, [(i, (i + by) % count) for i in range(count)])


def to_blocks(values_in):
    rows, plane_width = values_in.shape
    shaped = values_in.reshape(rows // BR, BR, plane_width // BW, BW)
    return shaped.transpose(0, 2, 1, 3).reshape(-1, BR * BW)


def from_blocks(pieces, rows, plane_width):
    shaped = pieces.reshape(rows // BR, plane_width // BW, BR, BW)
    return shaped.transpose(0, 2, 1, 3).reshape(rows, plane_width)


def banded(taps_in, diff):
    result = jnp.zeros(diff.shape, jnp.float32)
    for tap_index in range(TAPS):
        result = result + jnp.where(diff == tap_index, taps_in[tap_index].astype(jnp.float32), 0.0)
    return result.astype(jnp.bfloat16)


def column_mats(taps_in, flipped):
    radius = (TAPS - 1) // 2
    source_lane = jnp.arange(BW, dtype=jnp.int32)[:, None]
    target_lane = jnp.arange(BW, dtype=jnp.int32)[None, :]
    mats = []
    for offset in (-1, 0, 1):
        if flipped:
            diff = target_lane - source_lane - offset * BW + radius
        else:
            diff = source_lane + offset * BW - target_lane + radius
        mats.append(banded(taps_in, diff))
    return mats


def row_mat(taps_in, rows):
    radius = (TAPS - 1) // 2
    out_row = jnp.arange(rows, dtype=jnp.int32)[:, None]
    src_row = jnp.arange(rows, dtype=jnp.int32)[None, :]
    return banded(taps_in, src_row - out_row + radius)


def column_pass(values_in, mats):
    rows, plane_width = values_in.shape
    col_count = plane_width // BW
    grid_cells = values_in.reshape(rows, col_count, BW)
    padded = jnp.pad(grid_cells, ((0, 0), (1, 1), (0, 0)))
    result_sum = jnp.zeros(grid_cells.shape, jnp.float32)
    for position in range(3):
        result_sum = result_sum + jnp.einsum(
            "rcj,jk->rck",
            padded[:, position : position + col_count],
            mats[position],
            preferred_element_type=jnp.float32,
        )
    return result_sum.reshape(rows, plane_width)


def update_plane(estimate, raw_plane, matrix, landing, row_taps, col_taps, level):
    rows, plane_width = estimate.shape
    blocks = (rows // BR) * (plane_width // BW)
    block_iota = jnp.arange(blocks, dtype=jnp.int32)
    rounded = estimate.astype(jnp.bfloat16).reshape(rows, plane_width // BW, BW)
    moved = jnp.einsum("rcj,jk->rck", rounded, matrix, preferred_element_type=jnp.float32)
    moved = moved.astype(jnp.bfloat16).reshape(rows, plane_width)
    gather_mat = landing[None, :] == block_iota[:, None]
    land_count = jnp.sum(gather_mat.astype(jnp.float32), axis=1)
    summed = jnp.dot(
        gather_mat.astype(jnp.bfloat16), to_blocks(moved), preferred_element_type=jnp.float32
    )
    summed = (summed / jnp.maximum(land_count, 1.0)[:, None]).astype(jnp.bfloat16)
    joined = from_blocks(summed, rows, plane_width)
    across = column_pass(joined, column_mats(col_taps, False)).astype(jnp.bfloat16)
    band = row_mat(row_taps, rows)
    blurred = jnp.dot(band, across, preferred_element_type=jnp.float32) + level
    ratio = (raw_plane.astype(jnp.float32) / blurred).astype(jnp.bfloat16)
    rows_back = jnp.dot(band.T, ratio, preferred_element_type=jnp.float32).astype(jnp.bfloat16)
    spread = column_pass(rows_back, column_mats(col_taps, True)).astype(jnp.bfloat16)
    returned = jnp.einsum(
        "rcj,kj->rck",
        spread.reshape(rows, plane_width // BW, BW),
        matrix,
        preferred_element_type=jnp.float32,
    ).astype(jnp.bfloat16)
    correction = jnp.take(to_blocks(returned.reshape(rows, plane_width)), landing, axis=0)
    return estimate * from_blocks(correction, rows, plane_width).astype(jnp.float32)


def plane_kernel(est_count, offs_ref, roffs_ref, bg_ref, m_ref, mt_ref, s_ref, cnt_ref, g_ref,
                 bf_ref, bb_ref, a_ref, at_ref, *rest):
    *piece_refs, out_ref, est_whole, raw_whole, work, joined, across, ratio = rest
    rows, plane_width = out_ref.shape

    def assemble(refs, offsets_ref, whole):
        if len(refs) == 1:
            return refs[0]
        for k, piece in enumerate(refs):
            piece_rows = piece.shape[0]
            whole[pl.ds(pl.multiple_of(offsets_ref[k], 2 * BR), piece_rows), :] = piece[...]
        return whole

    est_ref = assemble(piece_refs[:est_count], offs_ref, est_whole)
    raw_ref = assemble(piece_refs[est_count:], roffs_ref, raw_whole)
    nt = rows // BR
    nc = plane_width // BW
    f32 = jnp.float32
    bf16 = jnp.bfloat16

    def cols(c):
        return slice(c * BW, (c + 1) * BW)

    for c in range(nc):
        blk = est_ref[:, cols(c)].astype(bf16)
        moved = jnp.dot(blk, m_ref[...], preferred_element_type=f32)
        work[c] = moved.astype(bf16).astype(f32)

    def regroup(src, mat_ref, dst, post):
        for r in range(BR):
            stacked = jnp.concatenate(
                [src[c, pl.ds(r, nt, stride=BR), :] for c in range(nc)], axis=0
            )
            result = jnp.dot(mat_ref[...], stacked.astype(bf16), preferred_element_type=f32)
            result = post(result)
            for c in range(nc):
                dst[c, pl.ds(r, nt, stride=BR), :] = result[c * nt:(c + 1) * nt, :]

    regroup(work, s_ref, joined,
            lambda v: (v / cnt_ref[...]).astype(bf16).astype(f32))

    def column_blur(take, mats_ref, c):
        total = None
        for offset in (-1, 0, 1):
            if 0 <= c + offset < nc:
                part = jnp.dot(take(c + offset).astype(bf16), mats_ref[offset + 1],
                               preferred_element_type=f32)
                total = part if total is None else total + part
        return total

    for c in range(nc):
        across[:, cols(c)] = column_blur(lambda i: joined[i], bf_ref, c).astype(bf16)
    level = bg_ref[0]
    for c in range(nc):
        blurred = jnp.dot(a_ref[...], across[:, cols(c)], preferred_element_type=f32) + level
        quotient = (raw_ref[:, cols(c)].astype(f32) / blurred).astype(bf16)
        ratio[:, cols(c)] = jnp.dot(at_ref[...], quotient, preferred_element_type=f32).astype(bf16)
    for c in range(nc):
        spread = column_blur(lambda i: ratio[:, cols(i)], bb_ref, c).astype(bf16)
        back = jnp.dot(spread, mt_ref[...], preferred_element_type=f32)
        work[c] = back.astype(bf16).astype(f32)
    regroup(work, g_ref, joined, lambda v: v)
    for c in range(nc):
        out_ref[:, cols(c)] = est_ref[:, cols(c)] * joined[c]


def band_kernel(row_ref, col_ref, a_ref, at_ref, bf_ref, bb_ref):
    count, rows, _ = a_ref.shape
    radius = (TAPS - 1) // 2
    out_row = lax.broadcasted_iota(jnp.int32, (rows, rows), 0)
    src_row = lax.broadcasted_iota(jnp.int32, (rows, rows), 1)
    source_lane = lax.broadcasted_iota(jnp.int32, (BW, BW), 0)
    target_lane = lax.broadcasted_iota(jnp.int32, (BW, BW), 1)

    def build(diff, taps_ref, base):
        result = jnp.zeros(diff.shape, jnp.float32)
        for tap_index in range(TAPS):
            result = jnp.where(diff == tap_index, taps_ref[base + tap_index], result)
        return result.astype(jnp.bfloat16)

    for i in range(count):
        base = i * TAPS
        a_ref[i] = build(src_row - out_row + radius, row_ref, base)
        at_ref[i] = build(out_row - src_row + radius, row_ref, base)
        for offset in (-1, 0, 1):
            forward = source_lane + offset * BW - target_lane + radius
            bf_ref[i, offset + 1] = build(forward, col_ref, base)
            backward = target_lane - source_lane - offset * BW + radius
            bb_ref[i, offset + 1] = build(backward, col_ref, base)


def all_bands(row_taps, col_taps, rows):
    count = row_taps.shape[0]
    smem = pl.BlockSpec(memory_space=pltpu.SMEM)
    vmem = pl.BlockSpec(memory_space=pltpu.VMEM)
    return pl.pallas_call(
        band_kernel,
        out_shape=(
            jax.ShapeDtypeStruct((count, rows, rows), jnp.bfloat16),
            jax.ShapeDtypeStruct((count, rows, rows), jnp.bfloat16),
            jax.ShapeDtypeStruct((count, 3, BW, BW), jnp.bfloat16),
            jax.ShapeDtypeStruct((count, 3, BW, BW), jnp.bfloat16),
        ),
        in_specs=[smem, smem],
        out_specs=(vmem, vmem, vmem, vmem),
    )(row_taps.astype(jnp.float32).reshape(-1), col_taps.astype(jnp.float32).reshape(-1))


def kernel_update(est_pieces, offsets, raw_pieces, raw_offsets, matrix, landing, bands, level):
    rows, plane_width = raw_pieces[0][0].shape[-2] * len(raw_pieces), raw_pieces[0][0].shape[-1]
    nt = rows // BR
    nc = plane_width // BW
    blocks = nt * nc
    order = landing.reshape(nt, nc).T.reshape(-1)
    place = (order % nc) * nt + order // nc
    spots = jnp.arange(blocks, dtype=jnp.int32)
    sum_mat = place[None, :] == spots[:, None]
    pick_mat = place[:, None] == spots[None, :]
    count = jnp.sum(sum_mat.astype(jnp.float32), axis=1)
    count = jnp.broadcast_to(jnp.maximum(count, 1.0)[:, None], (blocks, BW))
    vmem = pl.BlockSpec(memory_space=pltpu.VMEM)
    smem = pl.BlockSpec(memory_space=pltpu.SMEM)
    raw_specs = [
        pl.BlockSpec((None, None) + array.shape[2:], lambda i, at=at: at + (0, 0))
        for array, at in raw_pieces
    ]
    return pl.pallas_call(
        functools.partial(plane_kernel, len(est_pieces)),
        grid=(1,),
        out_shape=jax.ShapeDtypeStruct((rows, plane_width), jnp.float32),
        in_specs=[smem, smem, smem] + [vmem] * (9 + len(est_pieces)) + raw_specs,
        out_specs=vmem,
        scratch_shapes=[
            pltpu.VMEM((rows, plane_width), jnp.float32),
            pltpu.VMEM((rows, plane_width), jnp.bfloat16),
            pltpu.VMEM((nc, rows, BW), jnp.float32),
            pltpu.VMEM((nc, rows, BW), jnp.float32),
            pltpu.VMEM((rows, plane_width), jnp.bfloat16),
            pltpu.VMEM((rows, plane_width), jnp.bfloat16),
        ],
        compiler_params=pltpu.CompilerParams(vmem_limit_bytes=48 * 1024 * 1024),
        cost_estimate=pl.CostEstimate(
            flops=2 * rows * plane_width * (4 * BW + 2 * rows + 2 * blocks // BR * BR),
            bytes_accessed=rows * plane_width * 10,
            transcendentals=0,
        ),
    )(
        offsets,
        raw_offsets,
        jnp.reshape(level, (1,)).astype(jnp.float32),
        matrix,
        matrix.T,
        sum_mat.astype(jnp.bfloat16),
        count,
        pick_mat.astype(jnp.bfloat16),
        bands[2],
        bands[3],
        bands[0],
        bands[1],
        *est_pieces,
        *[array for array, _ in raw_pieces],
    )


def with_halo(cells, sides, width):
    for axis, dim in sides:
        count = lax.axis_size(axis)
        ends = count - 1
        head = lax.slice_in_dim(cells, 0, width, axis=dim)
        tail = lax.slice_in_dim(cells, cells.shape[dim] - width, cells.shape[dim], axis=dim)
        cells = jnp.concatenate(
            [
                lax.ppermute(tail, axis, [(i, (i + 1) % count) for i in range(ends)]),
                cells,
                lax.ppermute(head, axis, [((i + 1) % count, i) for i in range(ends)]),
            ],
            axis=dim,
        )
    return cells


def sharded_to_blocks(values_in):
    planes, tile_rows, plane_width = values_in.shape
    shaped = values_in.reshape(planes, tile_rows // BR, BR, plane_width // BW, BW)
    return shaped.transpose(1, 3, 0, 2, 4).reshape(-1, planes, BR, BW)


def sharded_from_blocks(pieces, tile_rows, plane_width):
    planes = pieces.shape[1]
    shaped = pieces.reshape(tile_rows // BR, plane_width // BW, planes, BR, BW)
    return shaped.transpose(2, 0, 3, 1, 4).reshape(planes, tile_rows, plane_width)


def sharded_column_pass(values_in, taps_in, flipped):
    planes, tile_rows, plane_width = values_in.shape
    radius = (taps_in.shape[1] - 1) // 2
    lane_iota = jnp.arange(BW, dtype=jnp.int32)
    source_lane = lane_iota[:, None]
    target_lane = lane_iota[None, :]
    zero_bf = jnp.zeros((), jnp.bfloat16)
    band_mats = []
    for offset in (-1, 0, 1):
        if flipped:
            tap_index = target_lane - source_lane - offset * BW + radius
        else:
            tap_index = source_lane + offset * BW - target_lane + radius
        inside = (tap_index >= 0) & (tap_index <= 2 * radius)
        picked = taps_in[:, jnp.clip(tap_index, 0, 2 * radius)]
        band_mats.append(jnp.where(inside[None, :, :], picked, zero_bf))
    col_count = plane_width // BW
    grid_cells = values_in.reshape(planes, tile_rows, col_count, BW)
    padded = jnp.pad(grid_cells, ((0, 0), (0, 0), (1, 1), (0, 0)))
    result_sum = jnp.zeros(grid_cells.shape, jnp.float32)
    for position in range(3):
        result_sum = result_sum + jnp.einsum(
            "prcj,pjk->prck",
            padded[:, :, position : position + col_count],
            band_mats[position],
            preferred_element_type=jnp.float32,
        )
    return result_sum.reshape(planes, tile_rows, plane_width)


def row_pass(padded, taps_in, flipped):
    planes, extended, plane_width = padded.shape
    radius = (taps_in.shape[1] - 1) // 2
    tile_rows = extended - 2 * radius
    row_iota = jnp.arange(tile_rows, dtype=jnp.int32)[:, None]
    src_iota = jnp.arange(extended, dtype=jnp.int32)[None, :]
    if flipped:
        tap_index = row_iota + 2 * radius - src_iota
    else:
        tap_index = src_iota - row_iota
    inside = (tap_index >= 0) & (tap_index <= 2 * radius)
    band_rows = jnp.where(
        inside[None, :, :],
        taps_in[:, jnp.clip(tap_index, 0, 2 * radius)],
        jnp.zeros((), jnp.bfloat16),
    )
    return jnp.einsum("prs,psw->prw", band_rows, padded, preferred_element_type=jnp.float32)


def sharded_update(
    estimate,
    raw_piece,
    view_index,
    slab_index,
    route_tile,
    route_block,
    interp,
    row_psf,
    col_psf,
    psf_band,
    background,
):
    tile_count = lax.axis_size("tile")
    my_tile = lax.axis_index("tile")
    planes, tile_rows, plane_width = estimate.shape
    blocks = tile_rows // BR * (plane_width // BW)
    capacity = max(2, 2 * blocks // tile_count)
    radius = (TAPS - 1) // 2
    matrix = interp[view_index]
    dest_tile = route_tile[view_index, :, 0].reshape(tile_count, blocks)
    dest_block = route_block[view_index].reshape(tile_count, blocks)
    tiles_iota = jnp.arange(tile_count, dtype=jnp.int32)
    one_hot = (dest_tile[:, :, None] == tiles_iota[None, None, :]).astype(jnp.int32)
    slot_rank = jnp.sum((jnp.cumsum(one_hot, axis=1) - one_hot) * one_hot, axis=2)
    slot_index = dest_tile * capacity + slot_rank
    my_slots = slot_index[my_tile]
    slots_iota = jnp.arange(tile_count * capacity, dtype=jnp.int32)
    block_iota = jnp.arange(blocks, dtype=jnp.int32)
    match_send = my_slots[None, :] == slots_iota[:, None]
    send_ok = jnp.any(match_send, axis=1)
    send_src = jnp.sum(jnp.where(match_send, block_iota[None, :], 0), axis=1)
    match_recv = (dest_tile == my_tile)[:, None, :] & (
        slot_rank[:, None, :] == jnp.arange(capacity, dtype=jnp.int32)[None, :, None]
    )
    recv_ok = jnp.any(match_recv, axis=2).reshape(-1)
    recv_off = jnp.sum(jnp.where(match_recv, dest_block[:, None, :], 0), axis=2).reshape(-1)
    zero_bf = jnp.zeros((), jnp.bfloat16)
    rounded_estimate = estimate.astype(jnp.bfloat16)
    interpolated = jnp.einsum(
        "bprj,jk->bprk", sharded_to_blocks(rounded_estimate), matrix, preferred_element_type=jnp.float32
    ).astype(jnp.bfloat16)
    outgoing = jnp.where(send_ok[:, None, None, None], interpolated[send_src], zero_bf)
    outgoing = outgoing.reshape(tile_count, capacity, planes, BR, BW)
    incoming = lax.all_to_all(outgoing, "tile", split_axis=0, concat_axis=0, tiled=True)
    incoming = incoming.reshape(tile_count * capacity, planes * BR * BW)
    landing = (recv_off[None, :] == block_iota[:, None]) & recv_ok[None, :]
    land_count = jnp.sum(landing.astype(jnp.float32), axis=1)
    summed = jnp.dot(landing.astype(jnp.bfloat16), incoming, preferred_element_type=jnp.float32)
    summed = (summed / jnp.maximum(land_count, 1.0)[:, None]).astype(jnp.bfloat16)
    joined_field = sharded_from_blocks(summed.reshape(blocks, planes, BR, BW), tile_rows, plane_width)
    plane_bands = lax.dynamic_slice_in_dim(psf_band, slab_index * planes, planes, 0)
    row_taps = row_psf[view_index][plane_bands]
    col_taps = col_psf[view_index][plane_bands]
    across = sharded_column_pass(joined_field, col_taps, False).astype(jnp.bfloat16)
    padded = with_halo(across, (("tile", 1),), radius)
    blurred = row_pass(padded, row_taps, False) + background[view_index]
    ratio_field = (raw_piece.astype(jnp.float32) / blurred).astype(jnp.bfloat16)
    padded_ratio = with_halo(ratio_field, (("tile", 1),), radius)
    rows_back = row_pass(padded_ratio, row_taps, True).astype(jnp.bfloat16)
    spread = sharded_column_pass(rows_back, col_taps, True).astype(jnp.bfloat16)
    returned_blocks = jnp.einsum(
        "bprj,kj->bprk", sharded_to_blocks(spread), matrix, preferred_element_type=jnp.float32
    ).astype(jnp.bfloat16)
    returning = jnp.where(recv_ok[:, None, None, None], returned_blocks[recv_off], zero_bf)
    returning = returning.reshape(tile_count, capacity, planes, BR, BW)
    arrived = lax.all_to_all(returning, "tile", split_axis=0, concat_axis=0, tiled=True)
    arrived = arrived.reshape(tile_count * capacity, planes, BR, BW)
    correction = arrived[my_slots]
    return estimate * sharded_from_blocks(correction.astype(jnp.float32), tile_rows, plane_width)


def local(
    initial_estimate,
    raw_views,
    route_tile,
    route_block,
    interp,
    row_kernel,
    col_kernel,
    psf_band,
    background,
):
    view_count = lax.axis_size("view")
    my_group = lax.axis_index("view")
    my_tile = lax.axis_index("tile")
    planes, tile_rows, plane_width = initial_estimate.shape
    tile_blocks = (tile_rows // BR) * (plane_width // BW)
    row_psf = (row_kernel / jnp.sum(row_kernel, axis=2, keepdims=True)).astype(jnp.bfloat16)
    col_psf = (col_kernel / jnp.sum(col_kernel, axis=2, keepdims=True)).astype(jnp.bfloat16)
    if view_count * tile_rows * plane_width * lax.axis_size("tile") > (1 << 22):
        estimate = initial_estimate
        for update_index in range(view_count):
            view_index = (my_group + update_index) % view_count
            own_piece = lax.dynamic_slice_in_dim(
                raw_views[0], (my_group - update_index) % view_count * planes, planes, 0
            )
            raw_piece = (
                own_piece if update_index == 0 else passed_along(own_piece, "view", -update_index)
            )
            estimate = sharded_update(
                estimate, raw_piece, view_index, my_group, route_tile, route_block,
                interp, row_psf, col_psf, psf_band, background,
            )
        return estimate
    pieces = []
    for update_index in range(view_count):
        own_piece = lax.dynamic_slice_in_dim(
            raw_views[0], (my_group - update_index) % view_count * planes, planes, 0
        )
        piece = own_piece if update_index == 0 else passed_along(own_piece, "view", -update_index)
        pieces.append(piece)
    first_raw = lax.all_gather(jnp.stack(pieces[:1]), "tile", axis=2, tiled=True)
    second_raw = lax.all_gather(jnp.stack(pieces[1:2]), "tile", axis=2, tiled=True)
    tile_count = lax.axis_size("tile")
    along = [initial_estimate] + [
        passed_along(initial_estimate, "tile", shift) for shift in range(2, tile_count, 2)
    ]
    partner = [(i, i ^ 1) for i in range(tile_count)]
    arrived = along + [lax.ppermute(piece, "tile", partner) for piece in along]
    sources = [(my_tile - shift) % tile_count for shift in range(0, tile_count, 2)]
    sources = sources + [(source ^ 1) for source in sources]
    offsets = jnp.stack(sources).astype(jnp.int32) * tile_rows
    late_raw, _ = lax.optimization_barrier((jnp.stack(pieces[2:]), arrived))
    late_along = [late_raw] + [
        passed_along(late_raw, "tile", shift) for shift in range(2, tile_count, 2)
    ]
    late_arrived = late_along + [lax.ppermute(piece, "tile", partner) for piece in late_along]
    whole_plane = jnp.zeros((1,), jnp.int32)
    plane_bands = lax.dynamic_slice_in_dim(psf_band, my_group * planes, planes, 0)
    views_in_order = (my_group + jnp.arange(view_count, dtype=jnp.int32)) % view_count
    bands = all_bands(
        row_psf[views_in_order][:, plane_bands].reshape(view_count * planes, TAPS),
        col_psf[views_in_order][:, plane_bands].reshape(view_count * planes, TAPS),
        tile_rows * lax.axis_size("tile"),
    )
    def raw_source(update_index, p):
        if update_index < 2:
            return [((first_raw, second_raw)[update_index], (0, p))]
        return [(piece, (update_index - 2, p)) for piece in late_arrived]

    for update_index in range(view_count):
        view_index = (my_group + update_index) % view_count
        matrix = interp[view_index]
        landing = route_tile[view_index, :, 0] * tile_blocks + route_block[view_index]
        level = background[view_index]
        estimate = jnp.stack(
            [
                kernel_update(
                    [piece[p] for piece in arrived] if update_index == 0 else [estimate[p]],
                    offsets if update_index == 0 else whole_plane,
                    raw_source(update_index, p),
                    whole_plane if update_index < 2 else offsets,
                    matrix,
                    landing,
                    [b[update_index * planes + p] for b in bands],
                    level,
                )
                for p in range(planes)
            ]
        )
    return lax.dynamic_slice_in_dim(estimate, my_tile * tile_rows, tile_rows, 1)


def solution(mesh):
    return jax.shard_map(
        local,
        mesh=mesh,
        in_specs=(
            P("view", "tile", None),
            P("view", None, "tile", None),
            P(),
            P(),
            P(),
            P(),
            P(),
            P(),
            P(),
        ),
        out_specs=P("view", "tile", None),
        check_vma=False,
    )
```

```python
import jax
import jax.numpy as jnp
from jax import lax
from jax.sharding import PartitionSpec as P
from jax.experimental import pallas as pl
from jax.experimental.pallas import tpu as pltpu

BR = 8
BW = 128
TAPS = 17


def passed_along(x, axis, by):
    count = lax.axis_size(axis)
    return lax.ppermute(x, axis, [(i, (i + by) % count) for i in range(count)])


def to_blocks(values_in):
    rows, plane_width = values_in.shape
    shaped = values_in.reshape(rows // BR, BR, plane_width // BW, BW)
    return shaped.transpose(0, 2, 1, 3).reshape(-1, BR * BW)


def from_blocks(pieces, rows, plane_width):
    shaped = pieces.reshape(rows // BR, plane_width // BW, BR, BW)
    return shaped.transpose(0, 2, 1, 3).reshape(rows, plane_width)


def banded(taps_in, diff):
    result = jnp.zeros(diff.shape, jnp.float32)
    for tap_index in range(TAPS):
        result = result + jnp.where(diff == tap_index, taps_in[tap_index].astype(jnp.float32), 0.0)
    return result.astype(jnp.bfloat16)


def column_mats(taps_in, flipped):
    radius = (TAPS - 1) // 2
    source_lane = jnp.arange(BW, dtype=jnp.int32)[:, None]
    target_lane = jnp.arange(BW, dtype=jnp.int32)[None, :]
    mats = []
    for offset in (-1, 0, 1):
        if flipped:
            diff = target_lane - source_lane - offset * BW + radius
        else:
            diff = source_lane + offset * BW - target_lane + radius
        mats.append(banded(taps_in, diff))
    return mats


def row_mat(taps_in, rows):
    radius = (TAPS - 1) // 2
    out_row = jnp.arange(rows, dtype=jnp.int32)[:, None]
    src_row = jnp.arange(rows, dtype=jnp.int32)[None, :]
    return banded(taps_in, src_row - out_row + radius)


def column_pass(values_in, mats):
    rows, plane_width = values_in.shape
    col_count = plane_width // BW
    grid_cells = values_in.reshape(rows, col_count, BW)
    padded = jnp.pad(grid_cells, ((0, 0), (1, 1), (0, 0)))
    result_sum = jnp.zeros(grid_cells.shape, jnp.float32)
    for position in range(3):
        result_sum = result_sum + jnp.einsum(
            "rcj,jk->rck",
            padded[:, position : position + col_count],
            mats[position],
            preferred_element_type=jnp.float32,
        )
    return result_sum.reshape(rows, plane_width)


def update_plane(estimate, raw_plane, matrix, landing, row_taps, col_taps, level):
    rows, plane_width = estimate.shape
    blocks = (rows // BR) * (plane_width // BW)
    block_iota = jnp.arange(blocks, dtype=jnp.int32)
    rounded = estimate.astype(jnp.bfloat16).reshape(rows, plane_width // BW, BW)
    moved = jnp.einsum("rcj,jk->rck", rounded, matrix, preferred_element_type=jnp.float32)
    moved = moved.astype(jnp.bfloat16).reshape(rows, plane_width)
    gather_mat = landing[None, :] == block_iota[:, None]
    land_count = jnp.sum(gather_mat.astype(jnp.float32), axis=1)
    summed = jnp.dot(
        gather_mat.astype(jnp.bfloat16), to_blocks(moved), preferred_element_type=jnp.float32
    )
    summed = (summed / jnp.maximum(land_count, 1.0)[:, None]).astype(jnp.bfloat16)
    joined = from_blocks(summed, rows, plane_width)
    across = column_pass(joined, column_mats(col_taps, False)).astype(jnp.bfloat16)
    band = row_mat(row_taps, rows)
    blurred = jnp.dot(band, across, preferred_element_type=jnp.float32) + level
    ratio = (raw_plane.astype(jnp.float32) / blurred).astype(jnp.bfloat16)
    rows_back = jnp.dot(band.T, ratio, preferred_element_type=jnp.float32).astype(jnp.bfloat16)
    spread = column_pass(rows_back, column_mats(col_taps, True)).astype(jnp.bfloat16)
    returned = jnp.einsum(
        "rcj,kj->rck",
        spread.reshape(rows, plane_width // BW, BW),
        matrix,
        preferred_element_type=jnp.float32,
    ).astype(jnp.bfloat16)
    correction = jnp.take(to_blocks(returned.reshape(rows, plane_width)), landing, axis=0)
    return estimate * from_blocks(correction, rows, plane_width).astype(jnp.float32)


def plane_kernel(offs_ref, bg_ref, raw_ref, m_ref, mt_ref, s_ref, cnt_ref, g_ref, bf_ref, bb_ref,
                 a_ref, at_ref, *rest):
    *piece_refs, out_ref, est_whole, work, joined, across, ratio = rest
    rows, plane_width = out_ref.shape
    if len(piece_refs) == 1:
        est_ref = piece_refs[0]
    else:
        est_ref = est_whole
        for k, piece in enumerate(piece_refs):
            piece_rows = piece.shape[0]
            est_ref[pl.ds(pl.multiple_of(offs_ref[k], BR), piece_rows), :] = piece[...]
    nt = rows // BR
    nc = plane_width // BW
    f32 = jnp.float32
    bf16 = jnp.bfloat16

    def cols(c):
        return slice(c * BW, (c + 1) * BW)

    for c in range(nc):
        blk = est_ref[:, cols(c)].astype(bf16)
        moved = jnp.dot(blk, m_ref[...], preferred_element_type=f32)
        work[c] = moved.astype(bf16).astype(f32)

    def regroup(src, mat_ref, dst, post):
        for r in range(BR):
            stacked = jnp.concatenate(
                [src[c, pl.ds(r, nt, stride=BR), :] for c in range(nc)], axis=0
            )
            result = jnp.dot(mat_ref[...], stacked.astype(bf16), preferred_element_type=f32)
            result = post(result)
            for c in range(nc):
                dst[c, pl.ds(r, nt, stride=BR), :] = result[c * nt:(c + 1) * nt, :]

    regroup(work, s_ref, joined,
            lambda v: (v / cnt_ref[...]).astype(bf16).astype(f32))

    def column_blur(take, mats_ref, c):
        total = None
        for offset in (-1, 0, 1):
            if 0 <= c + offset < nc:
                part = jnp.dot(take(c + offset).astype(bf16), mats_ref[offset + 1],
                               preferred_element_type=f32)
                total = part if total is None else total + part
        return total

    for c in range(nc):
        across[:, cols(c)] = column_blur(lambda i: joined[i], bf_ref, c).astype(bf16)
    level = bg_ref[0]
    for c in range(nc):
        blurred = jnp.dot(a_ref[...], across[:, cols(c)], preferred_element_type=f32) + level
        quotient = (raw_ref[:, cols(c)].astype(f32) / blurred).astype(bf16)
        ratio[:, cols(c)] = jnp.dot(at_ref[...], quotient, preferred_element_type=f32).astype(bf16)
    for c in range(nc):
        spread = column_blur(lambda i: ratio[:, cols(i)], bb_ref, c).astype(bf16)
        back = jnp.dot(spread, mt_ref[...], preferred_element_type=f32)
        work[c] = back.astype(bf16).astype(f32)
    regroup(work, g_ref, joined, lambda v: v)
    for c in range(nc):
        out_ref[:, cols(c)] = est_ref[:, cols(c)] * joined[c]


def band_kernel(row_ref, col_ref, a_ref, at_ref, bf_ref, bb_ref):
    count, rows, _ = a_ref.shape
    radius = (TAPS - 1) // 2
    out_row = lax.broadcasted_iota(jnp.int32, (rows, rows), 0)
    src_row = lax.broadcasted_iota(jnp.int32, (rows, rows), 1)
    source_lane = lax.broadcasted_iota(jnp.int32, (BW, BW), 0)
    target_lane = lax.broadcasted_iota(jnp.int32, (BW, BW), 1)

    def build(diff, taps_ref, base):
        result = jnp.zeros(diff.shape, jnp.float32)
        for tap_index in range(TAPS):
            result = jnp.where(diff == tap_index, taps_ref[base + tap_index], result)
        return result.astype(jnp.bfloat16)

    for i in range(count):
        base = i * TAPS
        a_ref[i] = build(src_row - out_row + radius, row_ref, base)
        at_ref[i] = build(out_row - src_row + radius, row_ref, base)
        for offset in (-1, 0, 1):
            forward = source_lane + offset * BW - target_lane + radius
            bf_ref[i, offset + 1] = build(forward, col_ref, base)
            backward = target_lane - source_lane - offset * BW + radius
            bb_ref[i, offset + 1] = build(backward, col_ref, base)


def all_bands(row_taps, col_taps, rows):
    count = row_taps.shape[0]
    smem = pl.BlockSpec(memory_space=pltpu.SMEM)
    vmem = pl.BlockSpec(memory_space=pltpu.VMEM)
    return pl.pallas_call(
        band_kernel,
        out_shape=(
            jax.ShapeDtypeStruct((count, rows, rows), jnp.bfloat16),
            jax.ShapeDtypeStruct((count, rows, rows), jnp.bfloat16),
            jax.ShapeDtypeStruct((count, 3, BW, BW), jnp.bfloat16),
            jax.ShapeDtypeStruct((count, 3, BW, BW), jnp.bfloat16),
        ),
        in_specs=[smem, smem],
        out_specs=(vmem, vmem, vmem, vmem),
    )(row_taps.astype(jnp.float32).reshape(-1), col_taps.astype(jnp.float32).reshape(-1))


def kernel_update(est_pieces, offsets, raw_all, raw_index, matrix, landing, bands, level):
    rows, plane_width = raw_all.shape[-2:]
    nt = rows // BR
    nc = plane_width // BW
    blocks = nt * nc
    order = landing.reshape(nt, nc).T.reshape(-1)
    place = (order % nc) * nt + order // nc
    spots = jnp.arange(blocks, dtype=jnp.int32)
    sum_mat = place[None, :] == spots[:, None]
    pick_mat = place[:, None] == spots[None, :]
    count = jnp.sum(sum_mat.astype(jnp.float32), axis=1)
    count = jnp.broadcast_to(jnp.maximum(count, 1.0)[:, None], (blocks, BW))
    smem = pl.BlockSpec(memory_space=pltpu.SMEM)
    operands = [
        matrix,
        matrix.T,
        sum_mat.astype(jnp.bfloat16),
        count,
        pick_mat.astype(jnp.bfloat16),
        bands[2],
        bands[3],
        bands[0],
        bands[1],
        *est_pieces,
    ]

    def whole(x):
        return pl.BlockSpec(x.shape, lambda i, dims=len(x.shape): (0,) * dims)

    raw_spec = pl.BlockSpec((None, None, rows, plane_width), lambda i: raw_index + (0, 0))
    return pl.pallas_call(
        plane_kernel,
        grid=(1,),
        out_shape=jax.ShapeDtypeStruct((rows, plane_width), jnp.float32),
        in_specs=[smem, smem, raw_spec] + [whole(x) for x in operands],
        out_specs=whole(jax.ShapeDtypeStruct((rows, plane_width), jnp.float32)),
        scratch_shapes=[
            pltpu.VMEM((rows, plane_width), jnp.float32),
            pltpu.VMEM((nc, rows, BW), jnp.float32),
            pltpu.VMEM((nc, rows, BW), jnp.float32),
            pltpu.VMEM((rows, plane_width), jnp.bfloat16),
            pltpu.VMEM((rows, plane_width), jnp.bfloat16),
        ],
        compiler_params=pltpu.CompilerParams(vmem_limit_bytes=48 * 1024 * 1024),
        cost_estimate=pl.CostEstimate(
            flops=2 * rows * plane_width * (4 * BW + 2 * rows + 2 * blocks // BR * BR),
            bytes_accessed=rows * plane_width * 10,
            transcendentals=0,
        ),
    )(offsets, jnp.reshape(level, (1,)).astype(jnp.float32), raw_all, *operands)


def with_halo(cells, sides, width):
    for axis, dim in sides:
        count = lax.axis_size(axis)
        ends = count - 1
        head = lax.slice_in_dim(cells, 0, width, axis=dim)
        tail = lax.slice_in_dim(cells, cells.shape[dim] - width, cells.shape[dim], axis=dim)
        cells = jnp.concatenate(
            [
                lax.ppermute(tail, axis, [(i, (i + 1) % count) for i in range(ends)]),
                cells,
                lax.ppermute(head, axis, [((i + 1) % count, i) for i in range(ends)]),
            ],
            axis=dim,
        )
    return cells


def sharded_to_blocks(values_in):
    planes, tile_rows, plane_width = values_in.shape
    shaped = values_in.reshape(planes, tile_rows // BR, BR, plane_width // BW, BW)
    return shaped.transpose(1, 3, 0, 2, 4).reshape(-1, planes, BR, BW)


def sharded_from_blocks(pieces, tile_rows, plane_width):
    planes = pieces.shape[1]
    shaped = pieces.reshape(tile_rows // BR, plane_width // BW, planes, BR, BW)
    return shaped.transpose(2, 0, 3, 1, 4).reshape(planes, tile_rows, plane_width)


def sharded_column_pass(values_in, taps_in, flipped):
    planes, tile_rows, plane_width = values_in.shape
    radius = (taps_in.shape[1] - 1) // 2
    lane_iota = jnp.arange(BW, dtype=jnp.int32)
    source_lane = lane_iota[:, None]
    target_lane = lane_iota[None, :]
    zero_bf = jnp.zeros((), jnp.bfloat16)
    band_mats = []
    for offset in (-1, 0, 1):
        if flipped:
            tap_index = target_lane - source_lane - offset * BW + radius
        else:
            tap_index = source_lane + offset * BW - target_lane + radius
        inside = (tap_index >= 0) & (tap_index <= 2 * radius)
        picked = taps_in[:, jnp.clip(tap_index, 0, 2 * radius)]
        band_mats.append(jnp.where(inside[None, :, :], picked, zero_bf))
    col_count = plane_width // BW
    grid_cells = values_in.reshape(planes, tile_rows, col_count, BW)
    padded = jnp.pad(grid_cells, ((0, 0), (0, 0), (1, 1), (0, 0)))
    result_sum = jnp.zeros(grid_cells.shape, jnp.float32)
    for position in range(3):
        result_sum = result_sum + jnp.einsum(
            "prcj,pjk->prck",
            padded[:, :, position : position + col_count],
            band_mats[position],
            preferred_element_type=jnp.float32,
        )
    return result_sum.reshape(planes, tile_rows, plane_width)


def row_pass(padded, taps_in, flipped):
    planes, extended, plane_width = padded.shape
    radius = (taps_in.shape[1] - 1) // 2
    tile_rows = extended - 2 * radius
    row_iota = jnp.arange(tile_rows, dtype=jnp.int32)[:, None]
    src_iota = jnp.arange(extended, dtype=jnp.int32)[None, :]
    if flipped:
        tap_index = row_iota + 2 * radius - src_iota
    else:
        tap_index = src_iota - row_iota
    inside = (tap_index >= 0) & (tap_index <= 2 * radius)
    band_rows = jnp.where(
        inside[None, :, :],
        taps_in[:, jnp.clip(tap_index, 0, 2 * radius)],
        jnp.zeros((), jnp.bfloat16),
    )
    return jnp.einsum("prs,psw->prw", band_rows, padded, preferred_element_type=jnp.float32)


def sharded_update(
    estimate,
    raw_piece,
    view_index,
    slab_index,
    route_tile,
    route_block,
    interp,
    row_psf,
    col_psf,
    psf_band,
    background,
):
    tile_count = lax.axis_size("tile")
    my_tile = lax.axis_index("tile")
    planes, tile_rows, plane_width = estimate.shape
    blocks = tile_rows // BR * (plane_width // BW)
    capacity = max(2, 2 * blocks // tile_count)
    radius = (TAPS - 1) // 2
    matrix = interp[view_index]
    dest_tile = route_tile[view_index, :, 0].reshape(tile_count, blocks)
    dest_block = route_block[view_index].reshape(tile_count, blocks)
    tiles_iota = jnp.arange(tile_count, dtype=jnp.int32)
    one_hot = (dest_tile[:, :, None] == tiles_iota[None, None, :]).astype(jnp.int32)
    slot_rank = jnp.sum((jnp.cumsum(one_hot, axis=1) - one_hot) * one_hot, axis=2)
    slot_index = dest_tile * capacity + slot_rank
    my_slots = slot_index[my_tile]
    slots_iota = jnp.arange(tile_count * capacity, dtype=jnp.int32)
    block_iota = jnp.arange(blocks, dtype=jnp.int32)
    match_send = my_slots[None, :] == slots_iota[:, None]
    send_ok = jnp.any(match_send, axis=1)
    send_src = jnp.sum(jnp.where(match_send, block_iota[None, :], 0), axis=1)
    match_recv = (dest_tile == my_tile)[:, None, :] & (
        slot_rank[:, None, :] == jnp.arange(capacity, dtype=jnp.int32)[None, :, None]
    )
    recv_ok = jnp.any(match_recv, axis=2).reshape(-1)
    recv_off = jnp.sum(jnp.where(match_recv, dest_block[:, None, :], 0), axis=2).reshape(-1)
    zero_bf = jnp.zeros((), jnp.bfloat16)
    rounded_estimate = estimate.astype(jnp.bfloat16)
    interpolated = jnp.einsum(
        "bprj,jk->bprk", sharded_to_blocks(rounded_estimate), matrix, preferred_element_type=jnp.float32
    ).astype(jnp.bfloat16)
    outgoing = jnp.where(send_ok[:, None, None, None], interpolated[send_src], zero_bf)
    outgoing = outgoing.reshape(tile_count, capacity, planes, BR, BW)
    incoming = lax.all_to_all(outgoing, "tile", split_axis=0, concat_axis=0, tiled=True)
    incoming = incoming.reshape(tile_count * capacity, planes * BR * BW)
    landing = (recv_off[None, :] == block_iota[:, None]) & recv_ok[None, :]
    land_count = jnp.sum(landing.astype(jnp.float32), axis=1)
    summed = jnp.dot(landing.astype(jnp.bfloat16), incoming, preferred_element_type=jnp.float32)
    summed = (summed / jnp.maximum(land_count, 1.0)[:, None]).astype(jnp.bfloat16)
    joined_field = sharded_from_blocks(summed.reshape(blocks, planes, BR, BW), tile_rows, plane_width)
    plane_bands = lax.dynamic_slice_in_dim(psf_band, slab_index * planes, planes, 0)
    row_taps = row_psf[view_index][plane_bands]
    col_taps = col_psf[view_index][plane_bands]
    across = sharded_column_pass(joined_field, col_taps, False).astype(jnp.bfloat16)
    padded = with_halo(across, (("tile", 1),), radius)
    blurred = row_pass(padded, row_taps, False) + background[view_index]
    ratio_field = (raw_piece.astype(jnp.float32) / blurred).astype(jnp.bfloat16)
    padded_ratio = with_halo(ratio_field, (("tile", 1),), radius)
    rows_back = row_pass(padded_ratio, row_taps, True).astype(jnp.bfloat16)
    spread = sharded_column_pass(rows_back, col_taps, True).astype(jnp.bfloat16)
    returned_blocks = jnp.einsum(
        "bprj,kj->bprk", sharded_to_blocks(spread), matrix, preferred_element_type=jnp.float32
    ).astype(jnp.bfloat16)
    returning = jnp.where(recv_ok[:, None, None, None], returned_blocks[recv_off], zero_bf)
    returning = returning.reshape(tile_count, capacity, planes, BR, BW)
    arrived = lax.all_to_all(returning, "tile", split_axis=0, concat_axis=0, tiled=True)
    arrived = arrived.reshape(tile_count * capacity, planes, BR, BW)
    correction = arrived[my_slots]
    return estimate * sharded_from_blocks(correction.astype(jnp.float32), tile_rows, plane_width)


def local(
    initial_estimate,
    raw_views,
    route_tile,
    route_block,
    interp,
    row_kernel,
    col_kernel,
    psf_band,
    background,
):
    view_count = lax.axis_size("view")
    my_group = lax.axis_index("view")
    my_tile = lax.axis_index("tile")
    planes, tile_rows, plane_width = initial_estimate.shape
    tile_blocks = (tile_rows // BR) * (plane_width // BW)
    row_psf = (row_kernel / jnp.sum(row_kernel, axis=2, keepdims=True)).astype(jnp.bfloat16)
    col_psf = (col_kernel / jnp.sum(col_kernel, axis=2, keepdims=True)).astype(jnp.bfloat16)
    if view_count * tile_rows * plane_width * lax.axis_size("tile") > (1 << 22):
        estimate = initial_estimate
        for update_index in range(view_count):
            view_index = (my_group + update_index) % view_count
            own_piece = lax.dynamic_slice_in_dim(
                raw_views[0], (my_group - update_index) % view_count * planes, planes, 0
            )
            raw_piece = (
                own_piece if update_index == 0 else passed_along(own_piece, "view", -update_index)
            )
            estimate = sharded_update(
                estimate, raw_piece, view_index, my_group, route_tile, route_block,
                interp, row_psf, col_psf, psf_band, background,
            )
        return estimate
    pieces = []
    for update_index in range(view_count):
        own_piece = lax.dynamic_slice_in_dim(
            raw_views[0], (my_group - update_index) % view_count * planes, planes, 0
        )
        piece = own_piece if update_index == 0 else passed_along(own_piece, "view", -update_index)
        pieces.append(piece)
    first_raw = lax.all_gather(jnp.stack(pieces[:1]), "tile", axis=2, tiled=True)
    later_raw = lax.all_gather(jnp.stack(pieces[1:]), "tile", axis=2, tiled=True)
    tile_count = lax.axis_size("tile")
    along = [initial_estimate] + [
        passed_along(initial_estimate, "tile", shift) for shift in range(2, tile_count, 2)
    ]
    partner = [(i, i ^ 1) for i in range(tile_count)]
    arrived = along + [lax.ppermute(piece, "tile", partner) for piece in along]
    sources = [(my_tile - shift) % tile_count for shift in range(0, tile_count, 2)]
    sources = sources + [(source ^ 1) for source in sources]
    offsets = jnp.stack(sources).astype(jnp.int32) * tile_rows
    whole_plane = jnp.zeros((1,), jnp.int32)
    plane_bands = lax.dynamic_slice_in_dim(psf_band, my_group * planes, planes, 0)
    views_in_order = (my_group + jnp.arange(view_count, dtype=jnp.int32)) % view_count
    bands = all_bands(
        row_psf[views_in_order][:, plane_bands].reshape(view_count * planes, TAPS),
        col_psf[views_in_order][:, plane_bands].reshape(view_count * planes, TAPS),
        tile_rows * lax.axis_size("tile"),
    )
    for update_index in range(view_count):
        view_index = (my_group + update_index) % view_count
        matrix = interp[view_index]
        landing = route_tile[view_index, :, 0] * tile_blocks + route_block[view_index]
        level = background[view_index]
        estimate = jnp.stack(
            [
                kernel_update(
                    [piece[p] for piece in arrived] if update_index == 0 else [estimate[p]],
                    offsets if update_index == 0 else whole_plane,
                    first_raw if update_index == 0 else later_raw,
                    (0 if update_index == 0 else update_index - 1, p),
                    matrix,
                    landing,
                    [b[update_index * planes + p] for b in bands],
                    level,
                )
                for p in range(planes)
            ]
        )
    return lax.dynamic_slice_in_dim(estimate, my_tile * tile_rows, tile_rows, 1)


def solution(mesh):
    return jax.shard_map(
        local,
        mesh=mesh,
        in_specs=(
            P("view", "tile", None),
            P("view", None, "tile", None),
            P(),
            P(),
            P(),
            P(),
            P(),
            P(),
            P(),
        ),
        out_specs=P("view", "tile", None),
        check_vma=False,
    )
```

```python
import functools

import jax
import jax.numpy as jnp
from jax import lax
from jax.sharding import PartitionSpec as P
from jax.experimental import pallas as pl
from jax.experimental.pallas import tpu as pltpu

BR = 8
BW = 128
TAPS = 17


def passed_along(x, axis, by):
    count = lax.axis_size(axis)
    return lax.ppermute(x, axis, [(i, (i + by) % count) for i in range(count)])


def to_blocks(values_in):
    rows, plane_width = values_in.shape
    shaped = values_in.reshape(rows // BR, BR, plane_width // BW, BW)
    return shaped.transpose(0, 2, 1, 3).reshape(-1, BR * BW)


def from_blocks(pieces, rows, plane_width):
    shaped = pieces.reshape(rows // BR, plane_width // BW, BR, BW)
    return shaped.transpose(0, 2, 1, 3).reshape(rows, plane_width)


def banded(taps_in, diff):
    result = jnp.zeros(diff.shape, jnp.float32)
    for tap_index in range(TAPS):
        result = result + jnp.where(diff == tap_index, taps_in[tap_index].astype(jnp.float32), 0.0)
    return result.astype(jnp.bfloat16)


def column_mats(taps_in, flipped):
    radius = (TAPS - 1) // 2
    source_lane = jnp.arange(BW, dtype=jnp.int32)[:, None]
    target_lane = jnp.arange(BW, dtype=jnp.int32)[None, :]
    mats = []
    for offset in (-1, 0, 1):
        if flipped:
            diff = target_lane - source_lane - offset * BW + radius
        else:
            diff = source_lane + offset * BW - target_lane + radius
        mats.append(banded(taps_in, diff))
    return mats


def row_mat(taps_in, rows):
    radius = (TAPS - 1) // 2
    out_row = jnp.arange(rows, dtype=jnp.int32)[:, None]
    src_row = jnp.arange(rows, dtype=jnp.int32)[None, :]
    return banded(taps_in, src_row - out_row + radius)


def column_pass(values_in, mats):
    rows, plane_width = values_in.shape
    col_count = plane_width // BW
    grid_cells = values_in.reshape(rows, col_count, BW)
    padded = jnp.pad(grid_cells, ((0, 0), (1, 1), (0, 0)))
    result_sum = jnp.zeros(grid_cells.shape, jnp.float32)
    for position in range(3):
        result_sum = result_sum + jnp.einsum(
            "rcj,jk->rck",
            padded[:, position : position + col_count],
            mats[position],
            preferred_element_type=jnp.float32,
        )
    return result_sum.reshape(rows, plane_width)


def update_plane(estimate, raw_plane, matrix, landing, row_taps, col_taps, level):
    rows, plane_width = estimate.shape
    blocks = (rows // BR) * (plane_width // BW)
    block_iota = jnp.arange(blocks, dtype=jnp.int32)
    rounded = estimate.astype(jnp.bfloat16).reshape(rows, plane_width // BW, BW)
    moved = jnp.einsum("rcj,jk->rck", rounded, matrix, preferred_element_type=jnp.float32)
    moved = moved.astype(jnp.bfloat16).reshape(rows, plane_width)
    gather_mat = landing[None, :] == block_iota[:, None]
    land_count = jnp.sum(gather_mat.astype(jnp.float32), axis=1)
    summed = jnp.dot(
        gather_mat.astype(jnp.bfloat16), to_blocks(moved), preferred_element_type=jnp.float32
    )
    summed = (summed / jnp.maximum(land_count, 1.0)[:, None]).astype(jnp.bfloat16)
    joined = from_blocks(summed, rows, plane_width)
    across = column_pass(joined, column_mats(col_taps, False)).astype(jnp.bfloat16)
    band = row_mat(row_taps, rows)
    blurred = jnp.dot(band, across, preferred_element_type=jnp.float32) + level
    ratio = (raw_plane.astype(jnp.float32) / blurred).astype(jnp.bfloat16)
    rows_back = jnp.dot(band.T, ratio, preferred_element_type=jnp.float32).astype(jnp.bfloat16)
    spread = column_pass(rows_back, column_mats(col_taps, True)).astype(jnp.bfloat16)
    returned = jnp.einsum(
        "rcj,kj->rck",
        spread.reshape(rows, plane_width // BW, BW),
        matrix,
        preferred_element_type=jnp.float32,
    ).astype(jnp.bfloat16)
    correction = jnp.take(to_blocks(returned.reshape(rows, plane_width)), landing, axis=0)
    return estimate * from_blocks(correction, rows, plane_width).astype(jnp.float32)


def plane_kernel(est_count, raw_index, offs_ref, bg_ref, m_ref, mt_ref, raw_hbm, s_hbm, cnt_hbm,
                 g_hbm, bf_hbm, bb_hbm, a_hbm, at_hbm, *rest):
    *est_hbm, out_ref, est_ref, raw_ref, s_ref, cnt_ref, g_ref, bf_ref, bb_ref, a_ref, at_ref = rest[:-5]
    work, joined, across, ratio, sems = rest[-5:]
    rows, plane_width = out_ref.shape
    nt = rows // BR
    nc = plane_width // BW
    f32 = jnp.float32
    bf16 = jnp.bfloat16

    def cols(c):
        return slice(c * BW, (c + 1) * BW)

    est_copies = []
    for k, piece in enumerate(est_hbm):
        if est_count == 1:
            target = est_ref
        else:
            target = est_ref.at[pl.ds(pl.multiple_of(offs_ref[k], BR), piece.shape[0])]
        est_copies.append(pltpu.make_async_copy(piece, target, sems.at[k]))
    sources = [raw_hbm.at[raw_index], s_hbm, cnt_hbm, g_hbm, bf_hbm, bb_hbm, a_hbm, at_hbm]
    targets = [raw_ref, s_ref, cnt_ref, g_ref, bf_ref, bb_ref, a_ref, at_ref]
    copies = [
        pltpu.make_async_copy(src, dst, sems.at[est_count + i])
        for i, (src, dst) in enumerate(zip(sources, targets))
    ]
    raw_copy, s_copy, cnt_copy, g_copy, bf_copy, bb_copy, a_copy, at_copy = copies
    for copy in est_copies + copies:
        copy.start()
    for copy in est_copies:
        copy.wait()

    for c in range(nc):
        blk = est_ref[:, cols(c)].astype(bf16)
        moved = jnp.dot(blk, m_ref[...], preferred_element_type=f32)
        work[c] = moved.astype(bf16).astype(f32)

    def regroup(src, mat_ref, dst, post):
        for r in range(BR):
            stacked = jnp.concatenate(
                [src[c, pl.ds(r, nt, stride=BR), :] for c in range(nc)], axis=0
            )
            result = jnp.dot(mat_ref[...], stacked.astype(bf16), preferred_element_type=f32)
            result = post(result)
            for c in range(nc):
                dst[c, pl.ds(r, nt, stride=BR), :] = result[c * nt:(c + 1) * nt, :]

    s_copy.wait()
    cnt_copy.wait()
    regroup(work, s_ref, joined,
            lambda v: (v / cnt_ref[...]).astype(bf16).astype(f32))

    def column_blur(take, mats_ref, c):
        total = None
        for offset in (-1, 0, 1):
            if 0 <= c + offset < nc:
                part = jnp.dot(take(c + offset).astype(bf16), mats_ref[offset + 1],
                               preferred_element_type=f32)
                total = part if total is None else total + part
        return total

    bf_copy.wait()
    for c in range(nc):
        across[:, cols(c)] = column_blur(lambda i: joined[i], bf_ref, c).astype(bf16)
    level = bg_ref[0]
    a_copy.wait()
    at_copy.wait()
    raw_copy.wait()
    for c in range(nc):
        blurred = jnp.dot(a_ref[...], across[:, cols(c)], preferred_element_type=f32) + level
        quotient = (raw_ref[:, cols(c)].astype(f32) / blurred).astype(bf16)
        ratio[:, cols(c)] = jnp.dot(at_ref[...], quotient, preferred_element_type=f32).astype(bf16)
    bb_copy.wait()
    for c in range(nc):
        spread = column_blur(lambda i: ratio[:, cols(i)], bb_ref, c).astype(bf16)
        back = jnp.dot(spread, mt_ref[...], preferred_element_type=f32)
        work[c] = back.astype(bf16).astype(f32)
    g_copy.wait()
    regroup(work, g_ref, joined, lambda v: v)
    for c in range(nc):
        out_ref[:, cols(c)] = est_ref[:, cols(c)] * joined[c]


def band_kernel(row_ref, col_ref, a_ref, at_ref, bf_ref, bb_ref):
    count, rows, _ = a_ref.shape
    radius = (TAPS - 1) // 2
    out_row = lax.broadcasted_iota(jnp.int32, (rows, rows), 0)
    src_row = lax.broadcasted_iota(jnp.int32, (rows, rows), 1)
    source_lane = lax.broadcasted_iota(jnp.int32, (BW, BW), 0)
    target_lane = lax.broadcasted_iota(jnp.int32, (BW, BW), 1)

    def build(diff, taps_ref, base):
        result = jnp.zeros(diff.shape, jnp.float32)
        for tap_index in range(TAPS):
            result = jnp.where(diff == tap_index, taps_ref[base + tap_index], result)
        return result.astype(jnp.bfloat16)

    for i in range(count):
        base = i * TAPS
        a_ref[i] = build(src_row - out_row + radius, row_ref, base)
        at_ref[i] = build(out_row - src_row + radius, row_ref, base)
        for offset in (-1, 0, 1):
            forward = source_lane + offset * BW - target_lane + radius
            bf_ref[i, offset + 1] = build(forward, col_ref, base)
            backward = target_lane - source_lane - offset * BW + radius
            bb_ref[i, offset + 1] = build(backward, col_ref, base)


def all_bands(row_taps, col_taps, rows):
    count = row_taps.shape[0]
    smem = pl.BlockSpec(memory_space=pltpu.SMEM)
    vmem = pl.BlockSpec(memory_space=pltpu.VMEM)
    return pl.pallas_call(
        band_kernel,
        out_shape=(
            jax.ShapeDtypeStruct((count, rows, rows), jnp.bfloat16),
            jax.ShapeDtypeStruct((count, rows, rows), jnp.bfloat16),
            jax.ShapeDtypeStruct((count, 3, BW, BW), jnp.bfloat16),
            jax.ShapeDtypeStruct((count, 3, BW, BW), jnp.bfloat16),
        ),
        in_specs=[smem, smem],
        out_specs=(vmem, vmem, vmem, vmem),
    )(row_taps.astype(jnp.float32).reshape(-1), col_taps.astype(jnp.float32).reshape(-1))


def kernel_update(est_pieces, offsets, raw_all, raw_index, matrix, landing, bands, level):
    rows, plane_width = raw_all.shape[-2:]
    nt = rows // BR
    nc = plane_width // BW
    blocks = nt * nc
    order = landing.reshape(nt, nc).T.reshape(-1)
    place = (order % nc) * nt + order // nc
    spots = jnp.arange(blocks, dtype=jnp.int32)
    sum_mat = place[None, :] == spots[:, None]
    pick_mat = place[:, None] == spots[None, :]
    count = jnp.sum(sum_mat.astype(jnp.float32), axis=1)
    count = jnp.broadcast_to(jnp.maximum(count, 1.0)[:, None], (blocks, BW))
    smem = pl.BlockSpec(memory_space=pltpu.SMEM)
    vmem = pl.BlockSpec(memory_space=pltpu.VMEM)
    hbm = pl.BlockSpec(memory_space=pl.ANY)
    operands = [
        raw_all,
        sum_mat.astype(jnp.bfloat16),
        count,
        pick_mat.astype(jnp.bfloat16),
        bands[2],
        bands[3],
        bands[0],
        bands[1],
        *est_pieces,
    ]
    return pl.pallas_call(
        functools.partial(plane_kernel, len(est_pieces), raw_index),
        out_shape=jax.ShapeDtypeStruct((rows, plane_width), jnp.float32),
        in_specs=[smem, smem, vmem, vmem] + [hbm] * len(operands),
        out_specs=vmem,
        scratch_shapes=[
            pltpu.VMEM((rows, plane_width), jnp.float32),
            pltpu.VMEM((rows, plane_width), jnp.bfloat16),
            pltpu.VMEM((blocks, blocks), jnp.bfloat16),
            pltpu.VMEM((blocks, BW), jnp.float32),
            pltpu.VMEM((blocks, blocks), jnp.bfloat16),
            pltpu.VMEM((3, BW, BW), jnp.bfloat16),
            pltpu.VMEM((3, BW, BW), jnp.bfloat16),
            pltpu.VMEM((rows, rows), jnp.bfloat16),
            pltpu.VMEM((rows, rows), jnp.bfloat16),
            pltpu.VMEM((nc, rows, BW), jnp.float32),
            pltpu.VMEM((nc, rows, BW), jnp.float32),
            pltpu.VMEM((rows, plane_width), jnp.bfloat16),
            pltpu.VMEM((rows, plane_width), jnp.bfloat16),
            pltpu.SemaphoreType.DMA((len(est_pieces) + 8,)),
        ],
        compiler_params=pltpu.CompilerParams(vmem_limit_bytes=48 * 1024 * 1024),
        cost_estimate=pl.CostEstimate(
            flops=2 * rows * plane_width * (4 * BW + 2 * rows + 2 * blocks // BR * BR),
            bytes_accessed=rows * plane_width * 10,
            transcendentals=0,
        ),
    )(offsets, jnp.reshape(level, (1,)).astype(jnp.float32), matrix, matrix.T, *operands)


def with_halo(cells, sides, width):
    for axis, dim in sides:
        count = lax.axis_size(axis)
        ends = count - 1
        head = lax.slice_in_dim(cells, 0, width, axis=dim)
        tail = lax.slice_in_dim(cells, cells.shape[dim] - width, cells.shape[dim], axis=dim)
        cells = jnp.concatenate(
            [
                lax.ppermute(tail, axis, [(i, (i + 1) % count) for i in range(ends)]),
                cells,
                lax.ppermute(head, axis, [((i + 1) % count, i) for i in range(ends)]),
            ],
            axis=dim,
        )
    return cells


def sharded_to_blocks(values_in):
    planes, tile_rows, plane_width = values_in.shape
    shaped = values_in.reshape(planes, tile_rows // BR, BR, plane_width // BW, BW)
    return shaped.transpose(1, 3, 0, 2, 4).reshape(-1, planes, BR, BW)


def sharded_from_blocks(pieces, tile_rows, plane_width):
    planes = pieces.shape[1]
    shaped = pieces.reshape(tile_rows // BR, plane_width // BW, planes, BR, BW)
    return shaped.transpose(2, 0, 3, 1, 4).reshape(planes, tile_rows, plane_width)


def sharded_column_pass(values_in, taps_in, flipped):
    planes, tile_rows, plane_width = values_in.shape
    radius = (taps_in.shape[1] - 1) // 2
    lane_iota = jnp.arange(BW, dtype=jnp.int32)
    source_lane = lane_iota[:, None]
    target_lane = lane_iota[None, :]
    zero_bf = jnp.zeros((), jnp.bfloat16)
    band_mats = []
    for offset in (-1, 0, 1):
        if flipped:
            tap_index = target_lane - source_lane - offset * BW + radius
        else:
            tap_index = source_lane + offset * BW - target_lane + radius
        inside = (tap_index >= 0) & (tap_index <= 2 * radius)
        picked = taps_in[:, jnp.clip(tap_index, 0, 2 * radius)]
        band_mats.append(jnp.where(inside[None, :, :], picked, zero_bf))
    col_count = plane_width // BW
    grid_cells = values_in.reshape(planes, tile_rows, col_count, BW)
    padded = jnp.pad(grid_cells, ((0, 0), (0, 0), (1, 1), (0, 0)))
    result_sum = jnp.zeros(grid_cells.shape, jnp.float32)
    for position in range(3):
        result_sum = result_sum + jnp.einsum(
            "prcj,pjk->prck",
            padded[:, :, position : position + col_count],
            band_mats[position],
            preferred_element_type=jnp.float32,
        )
    return result_sum.reshape(planes, tile_rows, plane_width)


def row_pass(padded, taps_in, flipped):
    planes, extended, plane_width = padded.shape
    radius = (taps_in.shape[1] - 1) // 2
    tile_rows = extended - 2 * radius
    row_iota = jnp.arange(tile_rows, dtype=jnp.int32)[:, None]
    src_iota = jnp.arange(extended, dtype=jnp.int32)[None, :]
    if flipped:
        tap_index = row_iota + 2 * radius - src_iota
    else:
        tap_index = src_iota - row_iota
    inside = (tap_index >= 0) & (tap_index <= 2 * radius)
    band_rows = jnp.where(
        inside[None, :, :],
        taps_in[:, jnp.clip(tap_index, 0, 2 * radius)],
        jnp.zeros((), jnp.bfloat16),
    )
    return jnp.einsum("prs,psw->prw", band_rows, padded, preferred_element_type=jnp.float32)


def sharded_update(
    estimate,
    raw_piece,
    view_index,
    slab_index,
    route_tile,
    route_block,
    interp,
    row_psf,
    col_psf,
    psf_band,
    background,
):
    tile_count = lax.axis_size("tile")
    my_tile = lax.axis_index("tile")
    planes, tile_rows, plane_width = estimate.shape
    blocks = tile_rows // BR * (plane_width // BW)
    capacity = max(2, 2 * blocks // tile_count)
    radius = (TAPS - 1) // 2
    matrix = interp[view_index]
    dest_tile = route_tile[view_index, :, 0].reshape(tile_count, blocks)
    dest_block = route_block[view_index].reshape(tile_count, blocks)
    tiles_iota = jnp.arange(tile_count, dtype=jnp.int32)
    one_hot = (dest_tile[:, :, None] == tiles_iota[None, None, :]).astype(jnp.int32)
    slot_rank = jnp.sum((jnp.cumsum(one_hot, axis=1) - one_hot) * one_hot, axis=2)
    slot_index = dest_tile * capacity + slot_rank
    my_slots = slot_index[my_tile]
    slots_iota = jnp.arange(tile_count * capacity, dtype=jnp.int32)
    block_iota = jnp.arange(blocks, dtype=jnp.int32)
    match_send = my_slots[None, :] == slots_iota[:, None]
    send_ok = jnp.any(match_send, axis=1)
    send_src = jnp.sum(jnp.where(match_send, block_iota[None, :], 0), axis=1)
    match_recv = (dest_tile == my_tile)[:, None, :] & (
        slot_rank[:, None, :] == jnp.arange(capacity, dtype=jnp.int32)[None, :, None]
    )
    recv_ok = jnp.any(match_recv, axis=2).reshape(-1)
    recv_off = jnp.sum(jnp.where(match_recv, dest_block[:, None, :], 0), axis=2).reshape(-1)
    zero_bf = jnp.zeros((), jnp.bfloat16)
    rounded_estimate = estimate.astype(jnp.bfloat16)
    interpolated = jnp.einsum(
        "bprj,jk->bprk", sharded_to_blocks(rounded_estimate), matrix, preferred_element_type=jnp.float32
    ).astype(jnp.bfloat16)
    outgoing = jnp.where(send_ok[:, None, None, None], interpolated[send_src], zero_bf)
    outgoing = outgoing.reshape(tile_count, capacity, planes, BR, BW)
    incoming = lax.all_to_all(outgoing, "tile", split_axis=0, concat_axis=0, tiled=True)
    incoming = incoming.reshape(tile_count * capacity, planes * BR * BW)
    landing = (recv_off[None, :] == block_iota[:, None]) & recv_ok[None, :]
    land_count = jnp.sum(landing.astype(jnp.float32), axis=1)
    summed = jnp.dot(landing.astype(jnp.bfloat16), incoming, preferred_element_type=jnp.float32)
    summed = (summed / jnp.maximum(land_count, 1.0)[:, None]).astype(jnp.bfloat16)
    joined_field = sharded_from_blocks(summed.reshape(blocks, planes, BR, BW), tile_rows, plane_width)
    plane_bands = lax.dynamic_slice_in_dim(psf_band, slab_index * planes, planes, 0)
    row_taps = row_psf[view_index][plane_bands]
    col_taps = col_psf[view_index][plane_bands]
    across = sharded_column_pass(joined_field, col_taps, False).astype(jnp.bfloat16)
    padded = with_halo(across, (("tile", 1),), radius)
    blurred = row_pass(padded, row_taps, False) + background[view_index]
    ratio_field = (raw_piece.astype(jnp.float32) / blurred).astype(jnp.bfloat16)
    padded_ratio = with_halo(ratio_field, (("tile", 1),), radius)
    rows_back = row_pass(padded_ratio, row_taps, True).astype(jnp.bfloat16)
    spread = sharded_column_pass(rows_back, col_taps, True).astype(jnp.bfloat16)
    returned_blocks = jnp.einsum(
        "bprj,kj->bprk", sharded_to_blocks(spread), matrix, preferred_element_type=jnp.float32
    ).astype(jnp.bfloat16)
    returning = jnp.where(recv_ok[:, None, None, None], returned_blocks[recv_off], zero_bf)
    returning = returning.reshape(tile_count, capacity, planes, BR, BW)
    arrived = lax.all_to_all(returning, "tile", split_axis=0, concat_axis=0, tiled=True)
    arrived = arrived.reshape(tile_count * capacity, planes, BR, BW)
    correction = arrived[my_slots]
    return estimate * sharded_from_blocks(correction.astype(jnp.float32), tile_rows, plane_width)


def local(
    initial_estimate,
    raw_views,
    route_tile,
    route_block,
    interp,
    row_kernel,
    col_kernel,
    psf_band,
    background,
):
    view_count = lax.axis_size("view")
    my_group = lax.axis_index("view")
    my_tile = lax.axis_index("tile")
    planes, tile_rows, plane_width = initial_estimate.shape
    tile_blocks = (tile_rows // BR) * (plane_width // BW)
    row_psf = (row_kernel / jnp.sum(row_kernel, axis=2, keepdims=True)).astype(jnp.bfloat16)
    col_psf = (col_kernel / jnp.sum(col_kernel, axis=2, keepdims=True)).astype(jnp.bfloat16)
    if view_count * tile_rows * plane_width * lax.axis_size("tile") > (1 << 22):
        estimate = initial_estimate
        for update_index in range(view_count):
            view_index = (my_group + update_index) % view_count
            own_piece = lax.dynamic_slice_in_dim(
                raw_views[0], (my_group - update_index) % view_count * planes, planes, 0
            )
            raw_piece = (
                own_piece if update_index == 0 else passed_along(own_piece, "view", -update_index)
            )
            estimate = sharded_update(
                estimate, raw_piece, view_index, my_group, route_tile, route_block,
                interp, row_psf, col_psf, psf_band, background,
            )
        return estimate
    pieces = []
    for update_index in range(view_count):
        own_piece = lax.dynamic_slice_in_dim(
            raw_views[0], (my_group - update_index) % view_count * planes, planes, 0
        )
        piece = own_piece if update_index == 0 else passed_along(own_piece, "view", -update_index)
        pieces.append(piece)
    first_raw = lax.all_gather(jnp.stack(pieces[:1]), "tile", axis=2, tiled=True)
    later_raw = lax.all_gather(jnp.stack(pieces[1:]), "tile", axis=2, tiled=True)
    tile_count = lax.axis_size("tile")
    along = [initial_estimate] + [
        passed_along(initial_estimate, "tile", shift) for shift in range(2, tile_count, 2)
    ]
    partner = [(i, i ^ 1) for i in range(tile_count)]
    arrived = along + [lax.ppermute(piece, "tile", partner) for piece in along]
    sources = [(my_tile - shift) % tile_count for shift in range(0, tile_count, 2)]
    sources = sources + [(source ^ 1) for source in sources]
    offsets = jnp.stack(sources).astype(jnp.int32) * tile_rows
    whole_plane = jnp.zeros((1,), jnp.int32)
    plane_bands = lax.dynamic_slice_in_dim(psf_band, my_group * planes, planes, 0)
    views_in_order = (my_group + jnp.arange(view_count, dtype=jnp.int32)) % view_count
    bands = all_bands(
        row_psf[views_in_order][:, plane_bands].reshape(view_count * planes, TAPS),
        col_psf[views_in_order][:, plane_bands].reshape(view_count * planes, TAPS),
        tile_rows * lax.axis_size("tile"),
    )
    for update_index in range(view_count):
        view_index = (my_group + update_index) % view_count
        matrix = interp[view_index]
        landing = route_tile[view_index, :, 0] * tile_blocks + route_block[view_index]
        level = background[view_index]
        estimate = jnp.stack(
            [
                kernel_update(
                    [piece[p] for piece in arrived] if update_index == 0 else [estimate[p]],
                    offsets if update_index == 0 else whole_plane,
                    first_raw if update_index == 0 else later_raw,
                    (0 if update_index == 0 else update_index - 1, p),
                    matrix,
                    landing,
                    [b[update_index * planes + p] for b in bands],
                    level,
                )
                for p in range(planes)
            ]
        )
    return lax.dynamic_slice_in_dim(estimate, my_tile * tile_rows, tile_rows, 1)


def solution(mesh):
    return jax.shard_map(
        local,
        mesh=mesh,
        in_specs=(
            P("view", "tile", None),
            P("view", None, "tile", None),
            P(),
            P(),
            P(),
            P(),
            P(),
            P(),
            P(),
        ),
        out_specs=P("view", "tile", None),
        check_vma=False,
    )
```

```python
import functools

import jax
import jax.numpy as jnp
from jax import lax
from jax.sharding import PartitionSpec as P
from jax.experimental import pallas as pl
from jax.experimental.pallas import tpu as pltpu

BR = 8
BW = 128
TAPS = 17


def passed_along(x, axis, by):
    count = lax.axis_size(axis)
    return lax.ppermute(x, axis, [(i, (i + by) % count) for i in range(count)])


def to_blocks(values_in):
    rows, plane_width = values_in.shape
    shaped = values_in.reshape(rows // BR, BR, plane_width // BW, BW)
    return shaped.transpose(0, 2, 1, 3).reshape(-1, BR * BW)


def from_blocks(pieces, rows, plane_width):
    shaped = pieces.reshape(rows // BR, plane_width // BW, BR, BW)
    return shaped.transpose(0, 2, 1, 3).reshape(rows, plane_width)


def banded(taps_in, diff):
    result = jnp.zeros(diff.shape, jnp.float32)
    for tap_index in range(TAPS):
        result = result + jnp.where(diff == tap_index, taps_in[tap_index].astype(jnp.float32), 0.0)
    return result.astype(jnp.bfloat16)


def column_mats(taps_in, flipped):
    radius = (TAPS - 1) // 2
    source_lane = jnp.arange(BW, dtype=jnp.int32)[:, None]
    target_lane = jnp.arange(BW, dtype=jnp.int32)[None, :]
    mats = []
    for offset in (-1, 0, 1):
        if flipped:
            diff = target_lane - source_lane - offset * BW + radius
        else:
            diff = source_lane + offset * BW - target_lane + radius
        mats.append(banded(taps_in, diff))
    return mats


def row_mat(taps_in, rows):
    radius = (TAPS - 1) // 2
    out_row = jnp.arange(rows, dtype=jnp.int32)[:, None]
    src_row = jnp.arange(rows, dtype=jnp.int32)[None, :]
    return banded(taps_in, src_row - out_row + radius)


def column_pass(values_in, mats):
    rows, plane_width = values_in.shape
    col_count = plane_width // BW
    grid_cells = values_in.reshape(rows, col_count, BW)
    padded = jnp.pad(grid_cells, ((0, 0), (1, 1), (0, 0)))
    result_sum = jnp.zeros(grid_cells.shape, jnp.float32)
    for position in range(3):
        result_sum = result_sum + jnp.einsum(
            "rcj,jk->rck",
            padded[:, position : position + col_count],
            mats[position],
            preferred_element_type=jnp.float32,
        )
    return result_sum.reshape(rows, plane_width)


def update_plane(estimate, raw_plane, matrix, landing, row_taps, col_taps, level):
    rows, plane_width = estimate.shape
    blocks = (rows // BR) * (plane_width // BW)
    block_iota = jnp.arange(blocks, dtype=jnp.int32)
    rounded = estimate.astype(jnp.bfloat16).reshape(rows, plane_width // BW, BW)
    moved = jnp.einsum("rcj,jk->rck", rounded, matrix, preferred_element_type=jnp.float32)
    moved = moved.astype(jnp.bfloat16).reshape(rows, plane_width)
    gather_mat = landing[None, :] == block_iota[:, None]
    land_count = jnp.sum(gather_mat.astype(jnp.float32), axis=1)
    summed = jnp.dot(
        gather_mat.astype(jnp.bfloat16), to_blocks(moved), preferred_element_type=jnp.float32
    )
    summed = (summed / jnp.maximum(land_count, 1.0)[:, None]).astype(jnp.bfloat16)
    joined = from_blocks(summed, rows, plane_width)
    across = column_pass(joined, column_mats(col_taps, False)).astype(jnp.bfloat16)
    band = row_mat(row_taps, rows)
    blurred = jnp.dot(band, across, preferred_element_type=jnp.float32) + level
    ratio = (raw_plane.astype(jnp.float32) / blurred).astype(jnp.bfloat16)
    rows_back = jnp.dot(band.T, ratio, preferred_element_type=jnp.float32).astype(jnp.bfloat16)
    spread = column_pass(rows_back, column_mats(col_taps, True)).astype(jnp.bfloat16)
    returned = jnp.einsum(
        "rcj,kj->rck",
        spread.reshape(rows, plane_width // BW, BW),
        matrix,
        preferred_element_type=jnp.float32,
    ).astype(jnp.bfloat16)
    correction = jnp.take(to_blocks(returned.reshape(rows, plane_width)), landing, axis=0)
    return estimate * from_blocks(correction, rows, plane_width).astype(jnp.float32)


def plane_kernel(est_count, raw_index, offs_ref, bg_ref, m_ref, mt_ref, raw_hbm, s_hbm, cnt_hbm,
                 g_hbm, bf_hbm, bb_hbm, a_hbm, at_hbm, *rest):
    *est_hbm, out_ref, est_ref, raw_ref, s_ref, cnt_ref, g_ref, bf_ref, bb_ref, a_ref, at_ref = rest[:-5]
    work, joined, across, ratio, sems = rest[-5:]
    rows, plane_width = out_ref.shape
    nt = rows // BR
    nc = plane_width // BW
    f32 = jnp.float32
    bf16 = jnp.bfloat16

    def cols(c):
        return slice(c * BW, (c + 1) * BW)

    est_copies = []
    for k, piece in enumerate(est_hbm):
        if est_count == 1:
            target = est_ref
        else:
            target = est_ref.at[pl.ds(pl.multiple_of(offs_ref[k], BR), piece.shape[0])]
        est_copies.append(pltpu.make_async_copy(piece, target, sems.at[k]))
    sources = [raw_hbm.at[raw_index], s_hbm, cnt_hbm, g_hbm, bf_hbm, bb_hbm, a_hbm, at_hbm]
    targets = [raw_ref, s_ref, cnt_ref, g_ref, bf_ref, bb_ref, a_ref, at_ref]
    copies = [
        pltpu.make_async_copy(src, dst, sems.at[est_count + i])
        for i, (src, dst) in enumerate(zip(sources, targets))
    ]
    raw_copy, s_copy, cnt_copy, g_copy, bf_copy, bb_copy, a_copy, at_copy = copies
    for copy in est_copies + copies:
        copy.start()
    for copy in est_copies:
        copy.wait()

    for c in range(nc):
        blk = est_ref[:, cols(c)].astype(bf16)
        moved = jnp.dot(blk, m_ref[...], preferred_element_type=f32)
        work[c] = moved.astype(bf16).astype(f32)

    def regroup(src, mat_ref, dst, post):
        for r in range(BR):
            stacked = jnp.concatenate(
                [src[c, pl.ds(r, nt, stride=BR), :] for c in range(nc)], axis=0
            )
            result = jnp.dot(mat_ref[...], stacked.astype(bf16), preferred_element_type=f32)
            result = post(result)
            for c in range(nc):
                dst[c, pl.ds(r, nt, stride=BR), :] = result[c * nt:(c + 1) * nt, :]

    s_copy.wait()
    cnt_copy.wait()
    regroup(work, s_ref, joined,
            lambda v: (v / cnt_ref[...]).astype(bf16).astype(f32))

    def column_blur(take, mats_ref, c):
        total = None
        for offset in (-1, 0, 1):
            if 0 <= c + offset < nc:
                part = jnp.dot(take(c + offset).astype(bf16), mats_ref[offset + 1],
                               preferred_element_type=f32)
                total = part if total is None else total + part
        return total

    bf_copy.wait()
    for c in range(nc):
        across[:, cols(c)] = column_blur(lambda i: joined[i], bf_ref, c).astype(bf16)
    level = bg_ref[0]
    a_copy.wait()
    at_copy.wait()
    raw_copy.wait()
    for c in range(nc):
        blurred = jnp.dot(a_ref[...], across[:, cols(c)], preferred_element_type=f32) + level
        quotient = (raw_ref[:, cols(c)].astype(f32) / blurred).astype(bf16)
        ratio[:, cols(c)] = jnp.dot(at_ref[...], quotient, preferred_element_type=f32).astype(bf16)
    bb_copy.wait()
    for c in range(nc):
        spread = column_blur(lambda i: ratio[:, cols(i)], bb_ref, c).astype(bf16)
        back = jnp.dot(spread, mt_ref[...], preferred_element_type=f32)
        work[c] = back.astype(bf16).astype(f32)
    g_copy.wait()
    regroup(work, g_ref, joined, lambda v: v)
    for c in range(nc):
        out_ref[:, cols(c)] = est_ref[:, cols(c)] * joined[c]


def band_kernel(row_ref, col_ref, a_ref, at_ref, bf_ref, bb_ref):
    count, rows, _ = a_ref.shape
    radius = (TAPS - 1) // 2
    out_row = lax.broadcasted_iota(jnp.int32, (rows, rows), 0)
    src_row = lax.broadcasted_iota(jnp.int32, (rows, rows), 1)
    source_lane = lax.broadcasted_iota(jnp.int32, (BW, BW), 0)
    target_lane = lax.broadcasted_iota(jnp.int32, (BW, BW), 1)

    def build(diff, taps_ref, base):
        result = jnp.zeros(diff.shape, jnp.float32)
        for tap_index in range(TAPS):
            result = jnp.where(diff == tap_index, taps_ref[base + tap_index], result)
        return result.astype(jnp.bfloat16)

    for i in range(count):
        base = i * TAPS
        a_ref[i] = build(src_row - out_row + radius, row_ref, base)
        at_ref[i] = build(out_row - src_row + radius, row_ref, base)
        for offset in (-1, 0, 1):
            forward = source_lane + offset * BW - target_lane + radius
            bf_ref[i, offset + 1] = build(forward, col_ref, base)
            backward = target_lane - source_lane - offset * BW + radius
            bb_ref[i, offset + 1] = build(backward, col_ref, base)


def all_bands(row_taps, col_taps, rows):
    count = row_taps.shape[0]
    smem = pl.BlockSpec(memory_space=pltpu.SMEM)
    vmem = pl.BlockSpec(memory_space=pltpu.VMEM)
    return pl.pallas_call(
        band_kernel,
        out_shape=(
            jax.ShapeDtypeStruct((count, rows, rows), jnp.bfloat16),
            jax.ShapeDtypeStruct((count, rows, rows), jnp.bfloat16),
            jax.ShapeDtypeStruct((count, 3, BW, BW), jnp.bfloat16),
            jax.ShapeDtypeStruct((count, 3, BW, BW), jnp.bfloat16),
        ),
        in_specs=[smem, smem],
        out_specs=(vmem, vmem, vmem, vmem),
    )(row_taps.astype(jnp.float32).reshape(-1), col_taps.astype(jnp.float32).reshape(-1))


def kernel_update(est_pieces, offsets, raw_all, raw_index, matrix, landing, bands, level):
    rows, plane_width = raw_all.shape[-2:]
    nt = rows // BR
    nc = plane_width // BW
    blocks = nt * nc
    order = landing.reshape(nt, nc).T.reshape(-1)
    place = (order % nc) * nt + order // nc
    spots = jnp.arange(blocks, dtype=jnp.int32)
    sum_mat = place[None, :] == spots[:, None]
    pick_mat = place[:, None] == spots[None, :]
    count = jnp.sum(sum_mat.astype(jnp.float32), axis=1)
    count = jnp.broadcast_to(jnp.maximum(count, 1.0)[:, None], (blocks, BW))
    smem = pl.BlockSpec(memory_space=pltpu.SMEM)
    vmem = pl.BlockSpec(memory_space=pltpu.VMEM)
    hbm = pl.BlockSpec(memory_space=pl.ANY)
    operands = [
        raw_all,
        sum_mat.astype(jnp.bfloat16),
        count,
        pick_mat.astype(jnp.bfloat16),
        bands[2],
        bands[3],
        bands[0],
        bands[1],
        *est_pieces,
    ]
    return pl.pallas_call(
        functools.partial(plane_kernel, len(est_pieces), raw_index),
        out_shape=jax.ShapeDtypeStruct((rows, plane_width), jnp.float32),
        in_specs=[smem, smem, vmem, vmem] + [hbm] * len(operands),
        out_specs=vmem,
        scratch_shapes=[
            pltpu.VMEM((rows, plane_width), jnp.float32),
            pltpu.VMEM((rows, plane_width), jnp.bfloat16),
            pltpu.VMEM((blocks, blocks), jnp.bfloat16),
            pltpu.VMEM((blocks, BW), jnp.float32),
            pltpu.VMEM((blocks, blocks), jnp.bfloat16),
            pltpu.VMEM((3, BW, BW), jnp.bfloat16),
            pltpu.VMEM((3, BW, BW), jnp.bfloat16),
            pltpu.VMEM((rows, rows), jnp.bfloat16),
            pltpu.VMEM((rows, rows), jnp.bfloat16),
            pltpu.VMEM((nc, rows, BW), jnp.float32),
            pltpu.VMEM((nc, rows, BW), jnp.float32),
            pltpu.VMEM((rows, plane_width), jnp.bfloat16),
            pltpu.VMEM((rows, plane_width), jnp.bfloat16),
            pltpu.SemaphoreType.DMA((len(est_pieces) + 8,)),
        ],
        cost_estimate=pl.CostEstimate(
            flops=2 * rows * plane_width * (4 * BW + 2 * rows + 2 * blocks // BR * BR),
            bytes_accessed=rows * plane_width * 10,
            transcendentals=0,
        ),
    )(offsets, jnp.reshape(level, (1,)).astype(jnp.float32), matrix, matrix.T, *operands)


def with_halo(cells, sides, width):
    for axis, dim in sides:
        count = lax.axis_size(axis)
        ends = count - 1
        head = lax.slice_in_dim(cells, 0, width, axis=dim)
        tail = lax.slice_in_dim(cells, cells.shape[dim] - width, cells.shape[dim], axis=dim)
        cells = jnp.concatenate(
            [
                lax.ppermute(tail, axis, [(i, (i + 1) % count) for i in range(ends)]),
                cells,
                lax.ppermute(head, axis, [((i + 1) % count, i) for i in range(ends)]),
            ],
            axis=dim,
        )
    return cells


def sharded_to_blocks(values_in):
    planes, tile_rows, plane_width = values_in.shape
    shaped = values_in.reshape(planes, tile_rows // BR, BR, plane_width // BW, BW)
    return shaped.transpose(1, 3, 0, 2, 4).reshape(-1, planes, BR, BW)


def sharded_from_blocks(pieces, tile_rows, plane_width):
    planes = pieces.shape[1]
    shaped = pieces.reshape(tile_rows // BR, plane_width // BW, planes, BR, BW)
    return shaped.transpose(2, 0, 3, 1, 4).reshape(planes, tile_rows, plane_width)


def sharded_column_pass(values_in, taps_in, flipped):
    planes, tile_rows, plane_width = values_in.shape
    radius = (taps_in.shape[1] - 1) // 2
    lane_iota = jnp.arange(BW, dtype=jnp.int32)
    source_lane = lane_iota[:, None]
    target_lane = lane_iota[None, :]
    zero_bf = jnp.zeros((), jnp.bfloat16)
    band_mats = []
    for offset in (-1, 0, 1):
        if flipped:
            tap_index = target_lane - source_lane - offset * BW + radius
        else:
            tap_index = source_lane + offset * BW - target_lane + radius
        inside = (tap_index >= 0) & (tap_index <= 2 * radius)
        picked = taps_in[:, jnp.clip(tap_index, 0, 2 * radius)]
        band_mats.append(jnp.where(inside[None, :, :], picked, zero_bf))
    col_count = plane_width // BW
    grid_cells = values_in.reshape(planes, tile_rows, col_count, BW)
    padded = jnp.pad(grid_cells, ((0, 0), (0, 0), (1, 1), (0, 0)))
    result_sum = jnp.zeros(grid_cells.shape, jnp.float32)
    for position in range(3):
        result_sum = result_sum + jnp.einsum(
            "prcj,pjk->prck",
            padded[:, :, position : position + col_count],
            band_mats[position],
            preferred_element_type=jnp.float32,
        )
    return result_sum.reshape(planes, tile_rows, plane_width)


def row_pass(padded, taps_in, flipped):
    planes, extended, plane_width = padded.shape
    radius = (taps_in.shape[1] - 1) // 2
    tile_rows = extended - 2 * radius
    row_iota = jnp.arange(tile_rows, dtype=jnp.int32)[:, None]
    src_iota = jnp.arange(extended, dtype=jnp.int32)[None, :]
    if flipped:
        tap_index = row_iota + 2 * radius - src_iota
    else:
        tap_index = src_iota - row_iota
    inside = (tap_index >= 0) & (tap_index <= 2 * radius)
    band_rows = jnp.where(
        inside[None, :, :],
        taps_in[:, jnp.clip(tap_index, 0, 2 * radius)],
        jnp.zeros((), jnp.bfloat16),
    )
    return jnp.einsum("prs,psw->prw", band_rows, padded, preferred_element_type=jnp.float32)


def sharded_update(
    estimate,
    raw_piece,
    view_index,
    slab_index,
    route_tile,
    route_block,
    interp,
    row_psf,
    col_psf,
    psf_band,
    background,
):
    tile_count = lax.axis_size("tile")
    my_tile = lax.axis_index("tile")
    planes, tile_rows, plane_width = estimate.shape
    blocks = tile_rows // BR * (plane_width // BW)
    capacity = max(2, 2 * blocks // tile_count)
    radius = (TAPS - 1) // 2
    matrix = interp[view_index]
    dest_tile = route_tile[view_index, :, 0].reshape(tile_count, blocks)
    dest_block = route_block[view_index].reshape(tile_count, blocks)
    tiles_iota = jnp.arange(tile_count, dtype=jnp.int32)
    one_hot = (dest_tile[:, :, None] == tiles_iota[None, None, :]).astype(jnp.int32)
    slot_rank = jnp.sum((jnp.cumsum(one_hot, axis=1) - one_hot) * one_hot, axis=2)
    slot_index = dest_tile * capacity + slot_rank
    my_slots = slot_index[my_tile]
    slots_iota = jnp.arange(tile_count * capacity, dtype=jnp.int32)
    block_iota = jnp.arange(blocks, dtype=jnp.int32)
    match_send = my_slots[None, :] == slots_iota[:, None]
    send_ok = jnp.any(match_send, axis=1)
    send_src = jnp.sum(jnp.where(match_send, block_iota[None, :], 0), axis=1)
    match_recv = (dest_tile == my_tile)[:, None, :] & (
        slot_rank[:, None, :] == jnp.arange(capacity, dtype=jnp.int32)[None, :, None]
    )
    recv_ok = jnp.any(match_recv, axis=2).reshape(-1)
    recv_off = jnp.sum(jnp.where(match_recv, dest_block[:, None, :], 0), axis=2).reshape(-1)
    zero_bf = jnp.zeros((), jnp.bfloat16)
    rounded_estimate = estimate.astype(jnp.bfloat16)
    interpolated = jnp.einsum(
        "bprj,jk->bprk", sharded_to_blocks(rounded_estimate), matrix, preferred_element_type=jnp.float32
    ).astype(jnp.bfloat16)
    outgoing = jnp.where(send_ok[:, None, None, None], interpolated[send_src], zero_bf)
    outgoing = outgoing.reshape(tile_count, capacity, planes, BR, BW)
    incoming = lax.all_to_all(outgoing, "tile", split_axis=0, concat_axis=0, tiled=True)
    incoming = incoming.reshape(tile_count * capacity, planes * BR * BW)
    landing = (recv_off[None, :] == block_iota[:, None]) & recv_ok[None, :]
    land_count = jnp.sum(landing.astype(jnp.float32), axis=1)
    summed = jnp.dot(landing.astype(jnp.bfloat16), incoming, preferred_element_type=jnp.float32)
    summed = (summed / jnp.maximum(land_count, 1.0)[:, None]).astype(jnp.bfloat16)
    joined_field = sharded_from_blocks(summed.reshape(blocks, planes, BR, BW), tile_rows, plane_width)
    plane_bands = lax.dynamic_slice_in_dim(psf_band, slab_index * planes, planes, 0)
    row_taps = row_psf[view_index][plane_bands]
    col_taps = col_psf[view_index][plane_bands]
    across = sharded_column_pass(joined_field, col_taps, False).astype(jnp.bfloat16)
    padded = with_halo(across, (("tile", 1),), radius)
    blurred = row_pass(padded, row_taps, False) + background[view_index]
    ratio_field = (raw_piece.astype(jnp.float32) / blurred).astype(jnp.bfloat16)
    padded_ratio = with_halo(ratio_field, (("tile", 1),), radius)
    rows_back = row_pass(padded_ratio, row_taps, True).astype(jnp.bfloat16)
    spread = sharded_column_pass(rows_back, col_taps, True).astype(jnp.bfloat16)
    returned_blocks = jnp.einsum(
        "bprj,kj->bprk", sharded_to_blocks(spread), matrix, preferred_element_type=jnp.float32
    ).astype(jnp.bfloat16)
    returning = jnp.where(recv_ok[:, None, None, None], returned_blocks[recv_off], zero_bf)
    returning = returning.reshape(tile_count, capacity, planes, BR, BW)
    arrived = lax.all_to_all(returning, "tile", split_axis=0, concat_axis=0, tiled=True)
    arrived = arrived.reshape(tile_count * capacity, planes, BR, BW)
    correction = arrived[my_slots]
    return estimate * sharded_from_blocks(correction.astype(jnp.float32), tile_rows, plane_width)


def local(
    initial_estimate,
    raw_views,
    route_tile,
    route_block,
    interp,
    row_kernel,
    col_kernel,
    psf_band,
    background,
):
    view_count = lax.axis_size("view")
    my_group = lax.axis_index("view")
    my_tile = lax.axis_index("tile")
    planes, tile_rows, plane_width = initial_estimate.shape
    tile_blocks = (tile_rows // BR) * (plane_width // BW)
    row_psf = (row_kernel / jnp.sum(row_kernel, axis=2, keepdims=True)).astype(jnp.bfloat16)
    col_psf = (col_kernel / jnp.sum(col_kernel, axis=2, keepdims=True)).astype(jnp.bfloat16)
    if view_count * tile_rows * plane_width * lax.axis_size("tile") > (1 << 22):
        estimate = initial_estimate
        for update_index in range(view_count):
            view_index = (my_group + update_index) % view_count
            own_piece = lax.dynamic_slice_in_dim(
                raw_views[0], (my_group - update_index) % view_count * planes, planes, 0
            )
            raw_piece = (
                own_piece if update_index == 0 else passed_along(own_piece, "view", -update_index)
            )
            estimate = sharded_update(
                estimate, raw_piece, view_index, my_group, route_tile, route_block,
                interp, row_psf, col_psf, psf_band, background,
            )
        return estimate
    pieces = []
    for update_index in range(view_count):
        own_piece = lax.dynamic_slice_in_dim(
            raw_views[0], (my_group - update_index) % view_count * planes, planes, 0
        )
        piece = own_piece if update_index == 0 else passed_along(own_piece, "view", -update_index)
        pieces.append(piece)
    first_raw = lax.all_gather(jnp.stack(pieces[:1]), "tile", axis=2, tiled=True)
    later_raw = lax.all_gather(jnp.stack(pieces[1:]), "tile", axis=2, tiled=True)
    tile_count = lax.axis_size("tile")
    along = [initial_estimate] + [
        passed_along(initial_estimate, "tile", shift) for shift in range(2, tile_count, 2)
    ]
    partner = [(i, i ^ 1) for i in range(tile_count)]
    arrived = along + [lax.ppermute(piece, "tile", partner) for piece in along]
    sources = [(my_tile - shift) % tile_count for shift in range(0, tile_count, 2)]
    sources = sources + [(source ^ 1) for source in sources]
    offsets = jnp.stack(sources).astype(jnp.int32) * tile_rows
    whole_plane = jnp.zeros((1,), jnp.int32)
    plane_bands = lax.dynamic_slice_in_dim(psf_band, my_group * planes, planes, 0)
    views_in_order = (my_group + jnp.arange(view_count, dtype=jnp.int32)) % view_count
    bands = all_bands(
        row_psf[views_in_order][:, plane_bands].reshape(view_count * planes, TAPS),
        col_psf[views_in_order][:, plane_bands].reshape(view_count * planes, TAPS),
        tile_rows * lax.axis_size("tile"),
    )
    for update_index in range(view_count):
        view_index = (my_group + update_index) % view_count
        matrix = interp[view_index]
        landing = route_tile[view_index, :, 0] * tile_blocks + route_block[view_index]
        level = background[view_index]
        estimate = jnp.stack(
            [
                kernel_update(
                    [piece[p] for piece in arrived] if update_index == 0 else [estimate[p]],
                    offsets if update_index == 0 else whole_plane,
                    first_raw if update_index == 0 else later_raw,
                    (0 if update_index == 0 else update_index - 1, p),
                    matrix,
                    landing,
                    [b[update_index * planes + p] for b in bands],
                    level,
                )
                for p in range(planes)
            ]
        )
    return lax.dynamic_slice_in_dim(estimate, my_tile * tile_rows, tile_rows, 1)


def solution(mesh):
    return jax.shard_map(
        local,
        mesh=mesh,
        in_specs=(
            P("view", "tile", None),
            P("view", None, "tile", None),
            P(),
            P(),
            P(),
            P(),
            P(),
            P(),
            P(),
        ),
        out_specs=P("view", "tile", None),
        check_vma=False,
    )
```

```python
import functools

import jax
import jax.numpy as jnp
from jax import lax
from jax.sharding import PartitionSpec as P
from jax.experimental import pallas as pl
from jax.experimental.pallas import tpu as pltpu

BR = 8
BW = 128
TAPS = 17


def passed_along(x, axis, by):
    count = lax.axis_size(axis)
    return lax.ppermute(x, axis, [(i, (i + by) % count) for i in range(count)])


def to_blocks(values_in):
    rows, plane_width = values_in.shape
    shaped = values_in.reshape(rows // BR, BR, plane_width // BW, BW)
    return shaped.transpose(0, 2, 1, 3).reshape(-1, BR * BW)


def from_blocks(pieces, rows, plane_width):
    shaped = pieces.reshape(rows // BR, plane_width // BW, BR, BW)
    return shaped.transpose(0, 2, 1, 3).reshape(rows, plane_width)


def banded(taps_in, diff):
    result = jnp.zeros(diff.shape, jnp.float32)
    for tap_index in range(TAPS):
        result = result + jnp.where(diff == tap_index, taps_in[tap_index].astype(jnp.float32), 0.0)
    return result.astype(jnp.bfloat16)


def column_mats(taps_in, flipped):
    radius = (TAPS - 1) // 2
    source_lane = jnp.arange(BW, dtype=jnp.int32)[:, None]
    target_lane = jnp.arange(BW, dtype=jnp.int32)[None, :]
    mats = []
    for offset in (-1, 0, 1):
        if flipped:
            diff = target_lane - source_lane - offset * BW + radius
        else:
            diff = source_lane + offset * BW - target_lane + radius
        mats.append(banded(taps_in, diff))
    return mats


def row_mat(taps_in, rows):
    radius = (TAPS - 1) // 2
    out_row = jnp.arange(rows, dtype=jnp.int32)[:, None]
    src_row = jnp.arange(rows, dtype=jnp.int32)[None, :]
    return banded(taps_in, src_row - out_row + radius)


def column_pass(values_in, mats):
    rows, plane_width = values_in.shape
    col_count = plane_width // BW
    grid_cells = values_in.reshape(rows, col_count, BW)
    padded = jnp.pad(grid_cells, ((0, 0), (1, 1), (0, 0)))
    result_sum = jnp.zeros(grid_cells.shape, jnp.float32)
    for position in range(3):
        result_sum = result_sum + jnp.einsum(
            "rcj,jk->rck",
            padded[:, position : position + col_count],
            mats[position],
            preferred_element_type=jnp.float32,
        )
    return result_sum.reshape(rows, plane_width)


def update_plane(estimate, raw_plane, matrix, landing, row_taps, col_taps, level):
    rows, plane_width = estimate.shape
    blocks = (rows // BR) * (plane_width // BW)
    block_iota = jnp.arange(blocks, dtype=jnp.int32)
    rounded = estimate.astype(jnp.bfloat16).reshape(rows, plane_width // BW, BW)
    moved = jnp.einsum("rcj,jk->rck", rounded, matrix, preferred_element_type=jnp.float32)
    moved = moved.astype(jnp.bfloat16).reshape(rows, plane_width)
    gather_mat = landing[None, :] == block_iota[:, None]
    land_count = jnp.sum(gather_mat.astype(jnp.float32), axis=1)
    summed = jnp.dot(
        gather_mat.astype(jnp.bfloat16), to_blocks(moved), preferred_element_type=jnp.float32
    )
    summed = (summed / jnp.maximum(land_count, 1.0)[:, None]).astype(jnp.bfloat16)
    joined = from_blocks(summed, rows, plane_width)
    across = column_pass(joined, column_mats(col_taps, False)).astype(jnp.bfloat16)
    band = row_mat(row_taps, rows)
    blurred = jnp.dot(band, across, preferred_element_type=jnp.float32) + level
    ratio = (raw_plane.astype(jnp.float32) / blurred).astype(jnp.bfloat16)
    rows_back = jnp.dot(band.T, ratio, preferred_element_type=jnp.float32).astype(jnp.bfloat16)
    spread = column_pass(rows_back, column_mats(col_taps, True)).astype(jnp.bfloat16)
    returned = jnp.einsum(
        "rcj,kj->rck",
        spread.reshape(rows, plane_width // BW, BW),
        matrix,
        preferred_element_type=jnp.float32,
    ).astype(jnp.bfloat16)
    correction = jnp.take(to_blocks(returned.reshape(rows, plane_width)), landing, axis=0)
    return estimate * from_blocks(correction, rows, plane_width).astype(jnp.float32)


def plane_kernel(est_count, raw_index, offs_ref, bg_ref, m_ref, mt_ref, raw_hbm, s_hbm, cnt_hbm,
                 g_hbm, bf_hbm, bb_hbm, a_hbm, at_hbm, *rest):
    *est_hbm, out_ref, est_ref, raw_ref, s_ref, cnt_ref, g_ref, bf_ref, bb_ref, a_ref, at_ref = rest[:-5]
    work, joined, across, ratio, sems = rest[-5:]
    rows, plane_width = out_ref.shape
    nt = rows // BR
    nc = plane_width // BW
    f32 = jnp.float32
    bf16 = jnp.bfloat16

    def cols(c):
        return slice(c * BW, (c + 1) * BW)

    est_copies = []
    if est_count == 1:
        est_ref = est_hbm[0]
    else:
        for k, piece in enumerate(est_hbm):
            target = est_ref.at[pl.ds(pl.multiple_of(offs_ref[k], BR), piece.shape[0])]
            est_copies.append(pltpu.make_async_copy(piece, target, sems.at[k]))
    sources = [raw_hbm.at[raw_index], s_hbm, cnt_hbm, g_hbm, bf_hbm, bb_hbm, a_hbm, at_hbm]
    targets = [raw_ref, s_ref, cnt_ref, g_ref, bf_ref, bb_ref, a_ref, at_ref]
    copies = [
        pltpu.make_async_copy(src, dst, sems.at[est_count + i])
        for i, (src, dst) in enumerate(zip(sources, targets))
    ]
    raw_copy, s_copy, cnt_copy, g_copy, bf_copy, bb_copy, a_copy, at_copy = copies
    for copy in est_copies + copies:
        copy.start()
    for copy in est_copies:
        copy.wait()

    for c in range(nc):
        blk = est_ref[:, cols(c)].astype(bf16)
        moved = jnp.dot(blk, m_ref[...], preferred_element_type=f32)
        work[c] = moved.astype(bf16).astype(f32)

    def regroup(src, mat_ref, dst, post):
        for r in range(BR):
            stacked = jnp.concatenate(
                [src[c, pl.ds(r, nt, stride=BR), :] for c in range(nc)], axis=0
            )
            result = jnp.dot(mat_ref[...], stacked.astype(bf16), preferred_element_type=f32)
            result = post(result)
            for c in range(nc):
                dst[c, pl.ds(r, nt, stride=BR), :] = result[c * nt:(c + 1) * nt, :]

    s_copy.wait()
    cnt_copy.wait()
    regroup(work, s_ref, joined,
            lambda v: (v / cnt_ref[...]).astype(bf16).astype(f32))

    def column_blur(take, mats_ref, c):
        total = None
        for offset in (-1, 0, 1):
            if 0 <= c + offset < nc:
                part = jnp.dot(take(c + offset).astype(bf16), mats_ref[offset + 1],
                               preferred_element_type=f32)
                total = part if total is None else total + part
        return total

    bf_copy.wait()
    for c in range(nc):
        across[:, cols(c)] = column_blur(lambda i: joined[i], bf_ref, c).astype(bf16)
    level = bg_ref[0]
    a_copy.wait()
    at_copy.wait()
    raw_copy.wait()
    for c in range(nc):
        blurred = jnp.dot(a_ref[...], across[:, cols(c)], preferred_element_type=f32) + level
        quotient = (raw_ref[:, cols(c)].astype(f32) / blurred).astype(bf16)
        ratio[:, cols(c)] = jnp.dot(at_ref[...], quotient, preferred_element_type=f32).astype(bf16)
    bb_copy.wait()
    for c in range(nc):
        spread = column_blur(lambda i: ratio[:, cols(i)], bb_ref, c).astype(bf16)
        back = jnp.dot(spread, mt_ref[...], preferred_element_type=f32)
        work[c] = back.astype(bf16).astype(f32)
    g_copy.wait()
    regroup(work, g_ref, joined, lambda v: v)
    for c in range(nc):
        out_ref[:, cols(c)] = est_ref[:, cols(c)] * joined[c]


def band_kernel(row_ref, col_ref, a_ref, at_ref, bf_ref, bb_ref):
    count, rows, _ = a_ref.shape
    radius = (TAPS - 1) // 2
    out_row = lax.broadcasted_iota(jnp.int32, (rows, rows), 0)
    src_row = lax.broadcasted_iota(jnp.int32, (rows, rows), 1)
    source_lane = lax.broadcasted_iota(jnp.int32, (BW, BW), 0)
    target_lane = lax.broadcasted_iota(jnp.int32, (BW, BW), 1)

    def build(diff, taps_ref, base):
        result = jnp.zeros(diff.shape, jnp.float32)
        for tap_index in range(TAPS):
            result = jnp.where(diff == tap_index, taps_ref[base + tap_index], result)
        return result.astype(jnp.bfloat16)

    for i in range(count):
        base = i * TAPS
        a_ref[i] = build(src_row - out_row + radius, row_ref, base)
        at_ref[i] = build(out_row - src_row + radius, row_ref, base)
        for offset in (-1, 0, 1):
            forward = source_lane + offset * BW - target_lane + radius
            bf_ref[i, offset + 1] = build(forward, col_ref, base)
            backward = target_lane - source_lane - offset * BW + radius
            bb_ref[i, offset + 1] = build(backward, col_ref, base)


def all_bands(row_taps, col_taps, rows):
    count = row_taps.shape[0]
    smem = pl.BlockSpec(memory_space=pltpu.SMEM)
    vmem = pl.BlockSpec(memory_space=pltpu.VMEM)
    return pl.pallas_call(
        band_kernel,
        out_shape=(
            jax.ShapeDtypeStruct((count, rows, rows), jnp.bfloat16),
            jax.ShapeDtypeStruct((count, rows, rows), jnp.bfloat16),
            jax.ShapeDtypeStruct((count, 3, BW, BW), jnp.bfloat16),
            jax.ShapeDtypeStruct((count, 3, BW, BW), jnp.bfloat16),
        ),
        in_specs=[smem, smem],
        out_specs=(vmem, vmem, vmem, vmem),
    )(row_taps.astype(jnp.float32).reshape(-1), col_taps.astype(jnp.float32).reshape(-1))


def kernel_update(est_pieces, offsets, raw_all, raw_index, matrix, landing, bands, level):
    rows, plane_width = raw_all.shape[-2:]
    nt = rows // BR
    nc = plane_width // BW
    blocks = nt * nc
    order = landing.reshape(nt, nc).T.reshape(-1)
    place = (order % nc) * nt + order // nc
    spots = jnp.arange(blocks, dtype=jnp.int32)
    sum_mat = place[None, :] == spots[:, None]
    pick_mat = place[:, None] == spots[None, :]
    count = jnp.sum(sum_mat.astype(jnp.float32), axis=1)
    count = jnp.broadcast_to(jnp.maximum(count, 1.0)[:, None], (blocks, BW))
    smem = pl.BlockSpec(memory_space=pltpu.SMEM)
    vmem = pl.BlockSpec(memory_space=pltpu.VMEM)
    hbm = pl.BlockSpec(memory_space=pl.ANY)
    operands = [
        raw_all,
        sum_mat.astype(jnp.bfloat16),
        count,
        pick_mat.astype(jnp.bfloat16),
        bands[2],
        bands[3],
        bands[0],
        bands[1],
        *est_pieces,
    ]
    return pl.pallas_call(
        functools.partial(plane_kernel, len(est_pieces), raw_index),
        out_shape=jax.ShapeDtypeStruct((rows, plane_width), jnp.float32),
        in_specs=[smem, smem, vmem, vmem] + [hbm] * 8 + [vmem if len(est_pieces) == 1 else hbm] * len(est_pieces),
        out_specs=vmem,
        scratch_shapes=[
            pltpu.VMEM((rows, plane_width), jnp.float32),
            pltpu.VMEM((rows, plane_width), jnp.bfloat16),
            pltpu.VMEM((blocks, blocks), jnp.bfloat16),
            pltpu.VMEM((blocks, BW), jnp.float32),
            pltpu.VMEM((blocks, blocks), jnp.bfloat16),
            pltpu.VMEM((3, BW, BW), jnp.bfloat16),
            pltpu.VMEM((3, BW, BW), jnp.bfloat16),
            pltpu.VMEM((rows, rows), jnp.bfloat16),
            pltpu.VMEM((rows, rows), jnp.bfloat16),
            pltpu.VMEM((nc, rows, BW), jnp.float32),
            pltpu.VMEM((nc, rows, BW), jnp.float32),
            pltpu.VMEM((rows, plane_width), jnp.bfloat16),
            pltpu.VMEM((rows, plane_width), jnp.bfloat16),
            pltpu.SemaphoreType.DMA((len(est_pieces) + 8,)),
        ],
        cost_estimate=pl.CostEstimate(
            flops=2 * rows * plane_width * (4 * BW + 2 * rows + 2 * blocks // BR * BR),
            bytes_accessed=rows * plane_width * 10,
            transcendentals=0,
        ),
    )(offsets, jnp.reshape(level, (1,)).astype(jnp.float32), matrix, matrix.T, *operands)


def with_halo(cells, sides, width):
    for axis, dim in sides:
        count = lax.axis_size(axis)
        ends = count - 1
        head = lax.slice_in_dim(cells, 0, width, axis=dim)
        tail = lax.slice_in_dim(cells, cells.shape[dim] - width, cells.shape[dim], axis=dim)
        cells = jnp.concatenate(
            [
                lax.ppermute(tail, axis, [(i, (i + 1) % count) for i in range(ends)]),
                cells,
                lax.ppermute(head, axis, [((i + 1) % count, i) for i in range(ends)]),
            ],
            axis=dim,
        )
    return cells


def sharded_to_blocks(values_in):
    planes, tile_rows, plane_width = values_in.shape
    shaped = values_in.reshape(planes, tile_rows // BR, BR, plane_width // BW, BW)
    return shaped.transpose(1, 3, 0, 2, 4).reshape(-1, planes, BR, BW)


def sharded_from_blocks(pieces, tile_rows, plane_width):
    planes = pieces.shape[1]
    shaped = pieces.reshape(tile_rows // BR, plane_width // BW, planes, BR, BW)
    return shaped.transpose(2, 0, 3, 1, 4).reshape(planes, tile_rows, plane_width)


def sharded_column_pass(values_in, taps_in, flipped):
    planes, tile_rows, plane_width = values_in.shape
    radius = (taps_in.shape[1] - 1) // 2
    lane_iota = jnp.arange(BW, dtype=jnp.int32)
    source_lane = lane_iota[:, None]
    target_lane = lane_iota[None, :]
    zero_bf = jnp.zeros((), jnp.bfloat16)
    band_mats = []
    for offset in (-1, 0, 1):
        if flipped:
            tap_index = target_lane - source_lane - offset * BW + radius
        else:
            tap_index = source_lane + offset * BW - target_lane + radius
        inside = (tap_index >= 0) & (tap_index <= 2 * radius)
        picked = taps_in[:, jnp.clip(tap_index, 0, 2 * radius)]
        band_mats.append(jnp.where(inside[None, :, :], picked, zero_bf))
    col_count = plane_width // BW
    grid_cells = values_in.reshape(planes, tile_rows, col_count, BW)
    padded = jnp.pad(grid_cells, ((0, 0), (0, 0), (1, 1), (0, 0)))
    result_sum = jnp.zeros(grid_cells.shape, jnp.float32)
    for position in range(3):
        result_sum = result_sum + jnp.einsum(
            "prcj,pjk->prck",
            padded[:, :, position : position + col_count],
            band_mats[position],
            preferred_element_type=jnp.float32,
        )
    return result_sum.reshape(planes, tile_rows, plane_width)


def row_pass(padded, taps_in, flipped):
    planes, extended, plane_width = padded.shape
    radius = (taps_in.shape[1] - 1) // 2
    tile_rows = extended - 2 * radius
    row_iota = jnp.arange(tile_rows, dtype=jnp.int32)[:, None]
    src_iota = jnp.arange(extended, dtype=jnp.int32)[None, :]
    if flipped:
        tap_index = row_iota + 2 * radius - src_iota
    else:
        tap_index = src_iota - row_iota
    inside = (tap_index >= 0) & (tap_index <= 2 * radius)
    band_rows = jnp.where(
        inside[None, :, :],
        taps_in[:, jnp.clip(tap_index, 0, 2 * radius)],
        jnp.zeros((), jnp.bfloat16),
    )
    return jnp.einsum("prs,psw->prw", band_rows, padded, preferred_element_type=jnp.float32)


def sharded_update(
    estimate,
    raw_piece,
    view_index,
    slab_index,
    route_tile,
    route_block,
    interp,
    row_psf,
    col_psf,
    psf_band,
    background,
):
    tile_count = lax.axis_size("tile")
    my_tile = lax.axis_index("tile")
    planes, tile_rows, plane_width = estimate.shape
    blocks = tile_rows // BR * (plane_width // BW)
    capacity = max(2, 2 * blocks // tile_count)
    radius = (TAPS - 1) // 2
    matrix = interp[view_index]
    dest_tile = route_tile[view_index, :, 0].reshape(tile_count, blocks)
    dest_block = route_block[view_index].reshape(tile_count, blocks)
    tiles_iota = jnp.arange(tile_count, dtype=jnp.int32)
    one_hot = (dest_tile[:, :, None] == tiles_iota[None, None, :]).astype(jnp.int32)
    slot_rank = jnp.sum((jnp.cumsum(one_hot, axis=1) - one_hot) * one_hot, axis=2)
    slot_index = dest_tile * capacity + slot_rank
    my_slots = slot_index[my_tile]
    slots_iota = jnp.arange(tile_count * capacity, dtype=jnp.int32)
    block_iota = jnp.arange(blocks, dtype=jnp.int32)
    match_send = my_slots[None, :] == slots_iota[:, None]
    send_ok = jnp.any(match_send, axis=1)
    send_src = jnp.sum(jnp.where(match_send, block_iota[None, :], 0), axis=1)
    match_recv = (dest_tile == my_tile)[:, None, :] & (
        slot_rank[:, None, :] == jnp.arange(capacity, dtype=jnp.int32)[None, :, None]
    )
    recv_ok = jnp.any(match_recv, axis=2).reshape(-1)
    recv_off = jnp.sum(jnp.where(match_recv, dest_block[:, None, :], 0), axis=2).reshape(-1)
    zero_bf = jnp.zeros((), jnp.bfloat16)
    rounded_estimate = estimate.astype(jnp.bfloat16)
    interpolated = jnp.einsum(
        "bprj,jk->bprk", sharded_to_blocks(rounded_estimate), matrix, preferred_element_type=jnp.float32
    ).astype(jnp.bfloat16)
    outgoing = jnp.where(send_ok[:, None, None, None], interpolated[send_src], zero_bf)
    outgoing = outgoing.reshape(tile_count, capacity, planes, BR, BW)
    incoming = lax.all_to_all(outgoing, "tile", split_axis=0, concat_axis=0, tiled=True)
    incoming = incoming.reshape(tile_count * capacity, planes * BR * BW)
    landing = (recv_off[None, :] == block_iota[:, None]) & recv_ok[None, :]
    land_count = jnp.sum(landing.astype(jnp.float32), axis=1)
    summed = jnp.dot(landing.astype(jnp.bfloat16), incoming, preferred_element_type=jnp.float32)
    summed = (summed / jnp.maximum(land_count, 1.0)[:, None]).astype(jnp.bfloat16)
    joined_field = sharded_from_blocks(summed.reshape(blocks, planes, BR, BW), tile_rows, plane_width)
    plane_bands = lax.dynamic_slice_in_dim(psf_band, slab_index * planes, planes, 0)
    row_taps = row_psf[view_index][plane_bands]
    col_taps = col_psf[view_index][plane_bands]
    across = sharded_column_pass(joined_field, col_taps, False).astype(jnp.bfloat16)
    padded = with_halo(across, (("tile", 1),), radius)
    blurred = row_pass(padded, row_taps, False) + background[view_index]
    ratio_field = (raw_piece.astype(jnp.float32) / blurred).astype(jnp.bfloat16)
    padded_ratio = with_halo(ratio_field, (("tile", 1),), radius)
    rows_back = row_pass(padded_ratio, row_taps, True).astype(jnp.bfloat16)
    spread = sharded_column_pass(rows_back, col_taps, True).astype(jnp.bfloat16)
    returned_blocks = jnp.einsum(
        "bprj,kj->bprk", sharded_to_blocks(spread), matrix, preferred_element_type=jnp.float32
    ).astype(jnp.bfloat16)
    returning = jnp.where(recv_ok[:, None, None, None], returned_blocks[recv_off], zero_bf)
    returning = returning.reshape(tile_count, capacity, planes, BR, BW)
    arrived = lax.all_to_all(returning, "tile", split_axis=0, concat_axis=0, tiled=True)
    arrived = arrived.reshape(tile_count * capacity, planes, BR, BW)
    correction = arrived[my_slots]
    return estimate * sharded_from_blocks(correction.astype(jnp.float32), tile_rows, plane_width)


def local(
    initial_estimate,
    raw_views,
    route_tile,
    route_block,
    interp,
    row_kernel,
    col_kernel,
    psf_band,
    background,
):
    view_count = lax.axis_size("view")
    my_group = lax.axis_index("view")
    my_tile = lax.axis_index("tile")
    planes, tile_rows, plane_width = initial_estimate.shape
    tile_blocks = (tile_rows // BR) * (plane_width // BW)
    row_psf = (row_kernel / jnp.sum(row_kernel, axis=2, keepdims=True)).astype(jnp.bfloat16)
    col_psf = (col_kernel / jnp.sum(col_kernel, axis=2, keepdims=True)).astype(jnp.bfloat16)
    if view_count * tile_rows * plane_width * lax.axis_size("tile") > (1 << 22):
        estimate = initial_estimate
        for update_index in range(view_count):
            view_index = (my_group + update_index) % view_count
            own_piece = lax.dynamic_slice_in_dim(
                raw_views[0], (my_group - update_index) % view_count * planes, planes, 0
            )
            raw_piece = (
                own_piece if update_index == 0 else passed_along(own_piece, "view", -update_index)
            )
            estimate = sharded_update(
                estimate, raw_piece, view_index, my_group, route_tile, route_block,
                interp, row_psf, col_psf, psf_band, background,
            )
        return estimate
    pieces = []
    for update_index in range(view_count):
        own_piece = lax.dynamic_slice_in_dim(
            raw_views[0], (my_group - update_index) % view_count * planes, planes, 0
        )
        piece = own_piece if update_index == 0 else passed_along(own_piece, "view", -update_index)
        pieces.append(piece)
    first_raw = lax.all_gather(jnp.stack(pieces[:1]), "tile", axis=2, tiled=True)
    later_raw = lax.all_gather(jnp.stack(pieces[1:]), "tile", axis=2, tiled=True)
    tile_count = lax.axis_size("tile")
    along = [initial_estimate] + [
        passed_along(initial_estimate, "tile", shift) for shift in range(2, tile_count, 2)
    ]
    partner = [(i, i ^ 1) for i in range(tile_count)]
    arrived = along + [lax.ppermute(piece, "tile", partner) for piece in along]
    sources = [(my_tile - shift) % tile_count for shift in range(0, tile_count, 2)]
    sources = sources + [(source ^ 1) for source in sources]
    offsets = jnp.stack(sources).astype(jnp.int32) * tile_rows
    whole_plane = jnp.zeros((1,), jnp.int32)
    plane_bands = lax.dynamic_slice_in_dim(psf_band, my_group * planes, planes, 0)
    views_in_order = (my_group + jnp.arange(view_count, dtype=jnp.int32)) % view_count
    bands = all_bands(
        row_psf[views_in_order][:, plane_bands].reshape(view_count * planes, TAPS),
        col_psf[views_in_order][:, plane_bands].reshape(view_count * planes, TAPS),
        tile_rows * lax.axis_size("tile"),
    )
    for update_index in range(view_count):
        view_index = (my_group + update_index) % view_count
        matrix = interp[view_index]
        landing = route_tile[view_index, :, 0] * tile_blocks + route_block[view_index]
        level = background[view_index]
        estimate = jnp.stack(
            [
                kernel_update(
                    [piece[p] for piece in arrived] if update_index == 0 else [estimate[p]],
                    offsets if update_index == 0 else whole_plane,
                    first_raw if update_index == 0 else later_raw,
                    (0 if update_index == 0 else update_index - 1, p),
                    matrix,
                    landing,
                    [b[update_index * planes + p] for b in bands],
                    level,
                )
                for p in range(planes)
            ]
        )
    return lax.dynamic_slice_in_dim(estimate, my_tile * tile_rows, tile_rows, 1)


def solution(mesh):
    return jax.shard_map(
        local,
        mesh=mesh,
        in_specs=(
            P("view", "tile", None),
            P("view", None, "tile", None),
            P(),
            P(),
            P(),
            P(),
            P(),
            P(),
            P(),
        ),
        out_specs=P("view", "tile", None),
        check_vma=False,
    )
```

```python
import jax
import jax.numpy as jnp
from jax import lax
from jax.sharding import PartitionSpec as P
from jax.experimental import pallas as pl
from jax.experimental.pallas import tpu as pltpu

BR = 8
BW = 128
TAPS = 17


def passed_along(x, axis, by):
    count = lax.axis_size(axis)
    return lax.ppermute(x, axis, [(i, (i + by) % count) for i in range(count)])


def to_blocks(values_in):
    rows, plane_width = values_in.shape
    shaped = values_in.reshape(rows // BR, BR, plane_width // BW, BW)
    return shaped.transpose(0, 2, 1, 3).reshape(-1, BR * BW)


def from_blocks(pieces, rows, plane_width):
    shaped = pieces.reshape(rows // BR, plane_width // BW, BR, BW)
    return shaped.transpose(0, 2, 1, 3).reshape(rows, plane_width)


def banded(taps_in, diff):
    result = jnp.zeros(diff.shape, jnp.float32)
    for tap_index in range(TAPS):
        result = result + jnp.where(diff == tap_index, taps_in[tap_index].astype(jnp.float32), 0.0)
    return result.astype(jnp.bfloat16)


def column_mats(taps_in, flipped):
    radius = (TAPS - 1) // 2
    source_lane = jnp.arange(BW, dtype=jnp.int32)[:, None]
    target_lane = jnp.arange(BW, dtype=jnp.int32)[None, :]
    mats = []
    for offset in (-1, 0, 1):
        if flipped:
            diff = target_lane - source_lane - offset * BW + radius
        else:
            diff = source_lane + offset * BW - target_lane + radius
        mats.append(banded(taps_in, diff))
    return mats


def row_mat(taps_in, rows):
    radius = (TAPS - 1) // 2
    out_row = jnp.arange(rows, dtype=jnp.int32)[:, None]
    src_row = jnp.arange(rows, dtype=jnp.int32)[None, :]
    return banded(taps_in, src_row - out_row + radius)


def column_pass(values_in, mats):
    rows, plane_width = values_in.shape
    col_count = plane_width // BW
    grid_cells = values_in.reshape(rows, col_count, BW)
    padded = jnp.pad(grid_cells, ((0, 0), (1, 1), (0, 0)))
    result_sum = jnp.zeros(grid_cells.shape, jnp.float32)
    for position in range(3):
        result_sum = result_sum + jnp.einsum(
            "rcj,jk->rck",
            padded[:, position : position + col_count],
            mats[position],
            preferred_element_type=jnp.float32,
        )
    return result_sum.reshape(rows, plane_width)


def update_plane(estimate, raw_plane, matrix, landing, row_taps, col_taps, level):
    rows, plane_width = estimate.shape
    blocks = (rows // BR) * (plane_width // BW)
    block_iota = jnp.arange(blocks, dtype=jnp.int32)
    rounded = estimate.astype(jnp.bfloat16).reshape(rows, plane_width // BW, BW)
    moved = jnp.einsum("rcj,jk->rck", rounded, matrix, preferred_element_type=jnp.float32)
    moved = moved.astype(jnp.bfloat16).reshape(rows, plane_width)
    gather_mat = landing[None, :] == block_iota[:, None]
    land_count = jnp.sum(gather_mat.astype(jnp.float32), axis=1)
    summed = jnp.dot(
        gather_mat.astype(jnp.bfloat16), to_blocks(moved), preferred_element_type=jnp.float32
    )
    summed = (summed / jnp.maximum(land_count, 1.0)[:, None]).astype(jnp.bfloat16)
    joined = from_blocks(summed, rows, plane_width)
    across = column_pass(joined, column_mats(col_taps, False)).astype(jnp.bfloat16)
    band = row_mat(row_taps, rows)
    blurred = jnp.dot(band, across, preferred_element_type=jnp.float32) + level
    ratio = (raw_plane.astype(jnp.float32) / blurred).astype(jnp.bfloat16)
    rows_back = jnp.dot(band.T, ratio, preferred_element_type=jnp.float32).astype(jnp.bfloat16)
    spread = column_pass(rows_back, column_mats(col_taps, True)).astype(jnp.bfloat16)
    returned = jnp.einsum(
        "rcj,kj->rck",
        spread.reshape(rows, plane_width // BW, BW),
        matrix,
        preferred_element_type=jnp.float32,
    ).astype(jnp.bfloat16)
    correction = jnp.take(to_blocks(returned.reshape(rows, plane_width)), landing, axis=0)
    return estimate * from_blocks(correction, rows, plane_width).astype(jnp.float32)


def plane_kernel(offs_ref, bg_ref, raw_ref, m_ref, mt_ref, s_ref, cnt_ref, g_ref, bf_ref, bb_ref,
                 a_ref, at_ref, *rest):
    *piece_refs, out_ref, est_whole, work, joined, across, ratio = rest
    rows, plane_width = out_ref.shape
    if len(piece_refs) == 1:
        est_ref = piece_refs[0]
    else:
        est_ref = est_whole
        for k, piece in enumerate(piece_refs):
            piece_rows = piece.shape[0]
            est_ref[pl.ds(pl.multiple_of(offs_ref[k], BR), piece_rows), :] = piece[...]
    nt = rows // BR
    nc = plane_width // BW
    f32 = jnp.float32
    bf16 = jnp.bfloat16

    def cols(c):
        return slice(c * BW, (c + 1) * BW)

    def lanes(c):
        return pl.ds(pl.multiple_of(c * BW, BW), BW)

    @pl.loop(0, nc)
    def _(c):
        blk = est_ref[:, lanes(c)].astype(bf16)
        moved = jnp.dot(blk, m_ref[...], preferred_element_type=f32)
        work[c] = moved.astype(bf16).astype(f32)

    def regroup(src, mat_ref, dst, post):
        for r in range(BR):
            stacked = jnp.concatenate(
                [src[c, pl.ds(r, nt, stride=BR), :] for c in range(nc)], axis=0
            )
            result = jnp.dot(mat_ref[...], stacked.astype(bf16), preferred_element_type=f32)
            result = post(result)
            for c in range(nc):
                dst[c, pl.ds(r, nt, stride=BR), :] = result[c * nt:(c + 1) * nt, :]

    regroup(work, s_ref, joined,
            lambda v: (v / cnt_ref[...]).astype(bf16).astype(f32))

    def column_blur(take, mats_ref, c):
        total = None
        for offset in (-1, 0, 1):
            if 0 <= c + offset < nc:
                part = jnp.dot(take(c + offset).astype(bf16), mats_ref[offset + 1],
                               preferred_element_type=f32)
                total = part if total is None else total + part
        return total

    for c in range(nc):
        across[:, cols(c)] = column_blur(lambda i: joined[i], bf_ref, c).astype(bf16)
    level = bg_ref[0]
    @pl.loop(0, nc)
    def _(c):
        blurred = jnp.dot(a_ref[...], across[:, lanes(c)], preferred_element_type=f32) + level
        quotient = (raw_ref[:, lanes(c)].astype(f32) / blurred).astype(bf16)
        ratio[:, lanes(c)] = jnp.dot(at_ref[...], quotient, preferred_element_type=f32).astype(bf16)
    for c in range(nc):
        spread = column_blur(lambda i: ratio[:, cols(i)], bb_ref, c).astype(bf16)
        back = jnp.dot(spread, mt_ref[...], preferred_element_type=f32)
        work[c] = back.astype(bf16).astype(f32)
    regroup(work, g_ref, joined, lambda v: v)
    @pl.loop(0, nc)
    def _(c):
        out_ref[:, lanes(c)] = est_ref[:, lanes(c)] * joined[c]


def band_kernel(row_ref, col_ref, a_ref, at_ref, bf_ref, bb_ref):
    count, rows, _ = a_ref.shape
    radius = (TAPS - 1) // 2
    out_row = lax.broadcasted_iota(jnp.int32, (rows, rows), 0)
    src_row = lax.broadcasted_iota(jnp.int32, (rows, rows), 1)
    source_lane = lax.broadcasted_iota(jnp.int32, (BW, BW), 0)
    target_lane = lax.broadcasted_iota(jnp.int32, (BW, BW), 1)

    def build(diff, taps_ref, base):
        result = jnp.zeros(diff.shape, jnp.float32)
        for tap_index in range(TAPS):
            result = jnp.where(diff == tap_index, taps_ref[base + tap_index], result)
        return result.astype(jnp.bfloat16)

    for i in range(count):
        base = i * TAPS
        a_ref[i] = build(src_row - out_row + radius, row_ref, base)
        at_ref[i] = build(out_row - src_row + radius, row_ref, base)
        for offset in (-1, 0, 1):
            forward = source_lane + offset * BW - target_lane + radius
            bf_ref[i, offset + 1] = build(forward, col_ref, base)
            backward = target_lane - source_lane - offset * BW + radius
            bb_ref[i, offset + 1] = build(backward, col_ref, base)


def all_bands(row_taps, col_taps, rows):
    count = row_taps.shape[0]
    smem = pl.BlockSpec(memory_space=pltpu.SMEM)
    vmem = pl.BlockSpec(memory_space=pltpu.VMEM)
    return pl.pallas_call(
        band_kernel,
        out_shape=(
            jax.ShapeDtypeStruct((count, rows, rows), jnp.bfloat16),
            jax.ShapeDtypeStruct((count, rows, rows), jnp.bfloat16),
            jax.ShapeDtypeStruct((count, 3, BW, BW), jnp.bfloat16),
            jax.ShapeDtypeStruct((count, 3, BW, BW), jnp.bfloat16),
        ),
        in_specs=[smem, smem],
        out_specs=(vmem, vmem, vmem, vmem),
    )(row_taps.astype(jnp.float32).reshape(-1), col_taps.astype(jnp.float32).reshape(-1))


def kernel_update(est_pieces, offsets, raw_all, raw_index, matrix, landing, bands, level):
    rows, plane_width = raw_all.shape[-2:]
    nt = rows // BR
    nc = plane_width // BW
    blocks = nt * nc
    order = landing.reshape(nt, nc).T.reshape(-1)
    place = (order % nc) * nt + order // nc
    spots = jnp.arange(blocks, dtype=jnp.int32)
    sum_mat = place[None, :] == spots[:, None]
    pick_mat = place[:, None] == spots[None, :]
    count = jnp.sum(sum_mat.astype(jnp.float32), axis=1)
    count = jnp.broadcast_to(jnp.maximum(count, 1.0)[:, None], (blocks, BW))
    vmem = pl.BlockSpec(memory_space=pltpu.VMEM)
    smem = pl.BlockSpec(memory_space=pltpu.SMEM)
    raw_spec = pl.BlockSpec((None, None, rows, plane_width), lambda i: raw_index + (0, 0))
    return pl.pallas_call(
        plane_kernel,
        grid=(1,),
        out_shape=jax.ShapeDtypeStruct((rows, plane_width), jnp.float32),
        in_specs=[smem, smem, raw_spec] + [vmem] * (9 + len(est_pieces)),
        out_specs=vmem,
        scratch_shapes=[
            pltpu.VMEM((rows, plane_width), jnp.float32),
            pltpu.VMEM((nc, rows, BW), jnp.float32),
            pltpu.VMEM((nc, rows, BW), jnp.float32),
            pltpu.VMEM((rows, plane_width), jnp.bfloat16),
            pltpu.VMEM((rows, plane_width), jnp.bfloat16),
        ],
        compiler_params=pltpu.CompilerParams(vmem_limit_bytes=48 * 1024 * 1024),
        cost_estimate=pl.CostEstimate(
            flops=2 * rows * plane_width * (4 * BW + 2 * rows + 2 * blocks // BR * BR),
            bytes_accessed=rows * plane_width * 10,
            transcendentals=0,
        ),
    )(
        offsets,
        jnp.reshape(level, (1,)).astype(jnp.float32),
        raw_all,
        matrix,
        matrix.T,
        sum_mat.astype(jnp.bfloat16),
        count,
        pick_mat.astype(jnp.bfloat16),
        bands[2],
        bands[3],
        bands[0],
        bands[1],
        *est_pieces,
    )


def with_halo(cells, sides, width):
    for axis, dim in sides:
        count = lax.axis_size(axis)
        ends = count - 1
        head = lax.slice_in_dim(cells, 0, width, axis=dim)
        tail = lax.slice_in_dim(cells, cells.shape[dim] - width, cells.shape[dim], axis=dim)
        cells = jnp.concatenate(
            [
                lax.ppermute(tail, axis, [(i, (i + 1) % count) for i in range(ends)]),
                cells,
                lax.ppermute(head, axis, [((i + 1) % count, i) for i in range(ends)]),
            ],
            axis=dim,
        )
    return cells


def sharded_to_blocks(values_in):
    planes, tile_rows, plane_width = values_in.shape
    shaped = values_in.reshape(planes, tile_rows // BR, BR, plane_width // BW, BW)
    return shaped.transpose(1, 3, 0, 2, 4).reshape(-1, planes, BR, BW)


def sharded_from_blocks(pieces, tile_rows, plane_width):
    planes = pieces.shape[1]
    shaped = pieces.reshape(tile_rows // BR, plane_width // BW, planes, BR, BW)
    return shaped.transpose(2, 0, 3, 1, 4).reshape(planes, tile_rows, plane_width)


def sharded_column_pass(values_in, taps_in, flipped):
    planes, tile_rows, plane_width = values_in.shape
    radius = (taps_in.shape[1] - 1) // 2
    lane_iota = jnp.arange(BW, dtype=jnp.int32)
    source_lane = lane_iota[:, None]
    target_lane = lane_iota[None, :]
    zero_bf = jnp.zeros((), jnp.bfloat16)
    band_mats = []
    for offset in (-1, 0, 1):
        if flipped:
            tap_index = target_lane - source_lane - offset * BW + radius
        else:
            tap_index = source_lane + offset * BW - target_lane + radius
        inside = (tap_index >= 0) & (tap_index <= 2 * radius)
        picked = taps_in[:, jnp.clip(tap_index, 0, 2 * radius)]
        band_mats.append(jnp.where(inside[None, :, :], picked, zero_bf))
    col_count = plane_width // BW
    grid_cells = values_in.reshape(planes, tile_rows, col_count, BW)
    padded = jnp.pad(grid_cells, ((0, 0), (0, 0), (1, 1), (0, 0)))
    result_sum = jnp.zeros(grid_cells.shape, jnp.float32)
    for position in range(3):
        result_sum = result_sum + jnp.einsum(
            "prcj,pjk->prck",
            padded[:, :, position : position + col_count],
            band_mats[position],
            preferred_element_type=jnp.float32,
        )
    return result_sum.reshape(planes, tile_rows, plane_width)


def row_pass(padded, taps_in, flipped):
    planes, extended, plane_width = padded.shape
    radius = (taps_in.shape[1] - 1) // 2
    tile_rows = extended - 2 * radius
    row_iota = jnp.arange(tile_rows, dtype=jnp.int32)[:, None]
    src_iota = jnp.arange(extended, dtype=jnp.int32)[None, :]
    if flipped:
        tap_index = row_iota + 2 * radius - src_iota
    else:
        tap_index = src_iota - row_iota
    inside = (tap_index >= 0) & (tap_index <= 2 * radius)
    band_rows = jnp.where(
        inside[None, :, :],
        taps_in[:, jnp.clip(tap_index, 0, 2 * radius)],
        jnp.zeros((), jnp.bfloat16),
    )
    return jnp.einsum("prs,psw->prw", band_rows, padded, preferred_element_type=jnp.float32)


def sharded_update(
    estimate,
    raw_piece,
    view_index,
    slab_index,
    route_tile,
    route_block,
    interp,
    row_psf,
    col_psf,
    psf_band,
    background,
):
    tile_count = lax.axis_size("tile")
    my_tile = lax.axis_index("tile")
    planes, tile_rows, plane_width = estimate.shape
    blocks = tile_rows // BR * (plane_width // BW)
    capacity = max(2, 2 * blocks // tile_count)
    radius = (TAPS - 1) // 2
    matrix = interp[view_index]
    dest_tile = route_tile[view_index, :, 0].reshape(tile_count, blocks)
    dest_block = route_block[view_index].reshape(tile_count, blocks)
    tiles_iota = jnp.arange(tile_count, dtype=jnp.int32)
    one_hot = (dest_tile[:, :, None] == tiles_iota[None, None, :]).astype(jnp.int32)
    slot_rank = jnp.sum((jnp.cumsum(one_hot, axis=1) - one_hot) * one_hot, axis=2)
    slot_index = dest_tile * capacity + slot_rank
    my_slots = slot_index[my_tile]
    slots_iota = jnp.arange(tile_count * capacity, dtype=jnp.int32)
    block_iota = jnp.arange(blocks, dtype=jnp.int32)
    match_send = my_slots[None, :] == slots_iota[:, None]
    send_ok = jnp.any(match_send, axis=1)
    send_src = jnp.sum(jnp.where(match_send, block_iota[None, :], 0), axis=1)
    match_recv = (dest_tile == my_tile)[:, None, :] & (
        slot_rank[:, None, :] == jnp.arange(capacity, dtype=jnp.int32)[None, :, None]
    )
    recv_ok = jnp.any(match_recv, axis=2).reshape(-1)
    recv_off = jnp.sum(jnp.where(match_recv, dest_block[:, None, :], 0), axis=2).reshape(-1)
    zero_bf = jnp.zeros((), jnp.bfloat16)
    rounded_estimate = estimate.astype(jnp.bfloat16)
    interpolated = jnp.einsum(
        "bprj,jk->bprk", sharded_to_blocks(rounded_estimate), matrix, preferred_element_type=jnp.float32
    ).astype(jnp.bfloat16)
    outgoing = jnp.where(send_ok[:, None, None, None], interpolated[send_src], zero_bf)
    outgoing = outgoing.reshape(tile_count, capacity, planes, BR, BW)
    incoming = lax.all_to_all(outgoing, "tile", split_axis=0, concat_axis=0, tiled=True)
    incoming = incoming.reshape(tile_count * capacity, planes * BR * BW)
    landing = (recv_off[None, :] == block_iota[:, None]) & recv_ok[None, :]
    land_count = jnp.sum(landing.astype(jnp.float32), axis=1)
    summed = jnp.dot(landing.astype(jnp.bfloat16), incoming, preferred_element_type=jnp.float32)
    summed = (summed / jnp.maximum(land_count, 1.0)[:, None]).astype(jnp.bfloat16)
    joined_field = sharded_from_blocks(summed.reshape(blocks, planes, BR, BW), tile_rows, plane_width)
    plane_bands = lax.dynamic_slice_in_dim(psf_band, slab_index * planes, planes, 0)
    row_taps = row_psf[view_index][plane_bands]
    col_taps = col_psf[view_index][plane_bands]
    across = sharded_column_pass(joined_field, col_taps, False).astype(jnp.bfloat16)
    padded = with_halo(across, (("tile", 1),), radius)
    blurred = row_pass(padded, row_taps, False) + background[view_index]
    ratio_field = (raw_piece.astype(jnp.float32) / blurred).astype(jnp.bfloat16)
    padded_ratio = with_halo(ratio_field, (("tile", 1),), radius)
    rows_back = row_pass(padded_ratio, row_taps, True).astype(jnp.bfloat16)
    spread = sharded_column_pass(rows_back, col_taps, True).astype(jnp.bfloat16)
    returned_blocks = jnp.einsum(
        "bprj,kj->bprk", sharded_to_blocks(spread), matrix, preferred_element_type=jnp.float32
    ).astype(jnp.bfloat16)
    returning = jnp.where(recv_ok[:, None, None, None], returned_blocks[recv_off], zero_bf)
    returning = returning.reshape(tile_count, capacity, planes, BR, BW)
    arrived = lax.all_to_all(returning, "tile", split_axis=0, concat_axis=0, tiled=True)
    arrived = arrived.reshape(tile_count * capacity, planes, BR, BW)
    correction = arrived[my_slots]
    return estimate * sharded_from_blocks(correction.astype(jnp.float32), tile_rows, plane_width)


def local(
    initial_estimate,
    raw_views,
    route_tile,
    route_block,
    interp,
    row_kernel,
    col_kernel,
    psf_band,
    background,
):
    view_count = lax.axis_size("view")
    my_group = lax.axis_index("view")
    my_tile = lax.axis_index("tile")
    planes, tile_rows, plane_width = initial_estimate.shape
    tile_blocks = (tile_rows // BR) * (plane_width // BW)
    row_psf = (row_kernel / jnp.sum(row_kernel, axis=2, keepdims=True)).astype(jnp.bfloat16)
    col_psf = (col_kernel / jnp.sum(col_kernel, axis=2, keepdims=True)).astype(jnp.bfloat16)
    if view_count * tile_rows * plane_width * lax.axis_size("tile") > (1 << 22):
        estimate = initial_estimate
        for update_index in range(view_count):
            view_index = (my_group + update_index) % view_count
            own_piece = lax.dynamic_slice_in_dim(
                raw_views[0], (my_group - update_index) % view_count * planes, planes, 0
            )
            raw_piece = (
                own_piece if update_index == 0 else passed_along(own_piece, "view", -update_index)
            )
            estimate = sharded_update(
                estimate, raw_piece, view_index, my_group, route_tile, route_block,
                interp, row_psf, col_psf, psf_band, background,
            )
        return estimate
    pieces = []
    for update_index in range(view_count):
        own_piece = lax.dynamic_slice_in_dim(
            raw_views[0], (my_group - update_index) % view_count * planes, planes, 0
        )
        piece = own_piece if update_index == 0 else passed_along(own_piece, "view", -update_index)
        pieces.append(piece)
    first_raw = lax.all_gather(jnp.stack(pieces[:1]), "tile", axis=2, tiled=True)
    later_raw = lax.all_gather(jnp.stack(pieces[1:]), "tile", axis=2, tiled=True)
    tile_count = lax.axis_size("tile")
    along = [initial_estimate] + [
        passed_along(initial_estimate, "tile", shift) for shift in range(2, tile_count, 2)
    ]
    partner = [(i, i ^ 1) for i in range(tile_count)]
    arrived = along + [lax.ppermute(piece, "tile", partner) for piece in along]
    sources = [(my_tile - shift) % tile_count for shift in range(0, tile_count, 2)]
    sources = sources + [(source ^ 1) for source in sources]
    offsets = jnp.stack(sources).astype(jnp.int32) * tile_rows
    whole_plane = jnp.zeros((1,), jnp.int32)
    plane_bands = lax.dynamic_slice_in_dim(psf_band, my_group * planes, planes, 0)
    views_in_order = (my_group + jnp.arange(view_count, dtype=jnp.int32)) % view_count
    bands = all_bands(
        row_psf[views_in_order][:, plane_bands].reshape(view_count * planes, TAPS),
        col_psf[views_in_order][:, plane_bands].reshape(view_count * planes, TAPS),
        tile_rows * lax.axis_size("tile"),
    )
    for update_index in range(view_count):
        view_index = (my_group + update_index) % view_count
        matrix = interp[view_index]
        landing = route_tile[view_index, :, 0] * tile_blocks + route_block[view_index]
        level = background[view_index]
        estimate = jnp.stack(
            [
                kernel_update(
                    [piece[p] for piece in arrived] if update_index == 0 else [estimate[p]],
                    offsets if update_index == 0 else whole_plane,
                    first_raw if update_index == 0 else later_raw,
                    (0 if update_index == 0 else update_index - 1, p),
                    matrix,
                    landing,
                    [b[update_index * planes + p] for b in bands],
                    level,
                )
                for p in range(planes)
            ]
        )
    return lax.dynamic_slice_in_dim(estimate, my_tile * tile_rows, tile_rows, 1)


def solution(mesh):
    return jax.shard_map(
        local,
        mesh=mesh,
        in_specs=(
            P("view", "tile", None),
            P("view", None, "tile", None),
            P(),
            P(),
            P(),
            P(),
            P(),
            P(),
            P(),
        ),
        out_specs=P("view", "tile", None),
        check_vma=False,
    )
```

```python
import jax
import jax.numpy as jnp
from jax import lax
from jax.sharding import PartitionSpec as P
from jax.experimental import pallas as pl
from jax.experimental.pallas import tpu as pltpu

BR = 8
BW = 128
TAPS = 17


def passed_along(x, axis, by):
    count = lax.axis_size(axis)
    return lax.ppermute(x, axis, [(i, (i + by) % count) for i in range(count)])


def to_blocks(values_in):
    rows, plane_width = values_in.shape
    shaped = values_in.reshape(rows // BR, BR, plane_width // BW, BW)
    return shaped.transpose(0, 2, 1, 3).reshape(-1, BR * BW)


def from_blocks(pieces, rows, plane_width):
    shaped = pieces.reshape(rows // BR, plane_width // BW, BR, BW)
    return shaped.transpose(0, 2, 1, 3).reshape(rows, plane_width)


def banded(taps_in, diff):
    result = jnp.zeros(diff.shape, jnp.float32)
    for tap_index in range(TAPS):
        result = result + jnp.where(diff == tap_index, taps_in[tap_index].astype(jnp.float32), 0.0)
    return result.astype(jnp.bfloat16)


def column_mats(taps_in, flipped):
    radius = (TAPS - 1) // 2
    source_lane = jnp.arange(BW, dtype=jnp.int32)[:, None]
    target_lane = jnp.arange(BW, dtype=jnp.int32)[None, :]
    mats = []
    for offset in (-1, 0, 1):
        if flipped:
            diff = target_lane - source_lane - offset * BW + radius
        else:
            diff = source_lane + offset * BW - target_lane + radius
        mats.append(banded(taps_in, diff))
    return mats


def row_mat(taps_in, rows):
    radius = (TAPS - 1) // 2
    out_row = jnp.arange(rows, dtype=jnp.int32)[:, None]
    src_row = jnp.arange(rows, dtype=jnp.int32)[None, :]
    return banded(taps_in, src_row - out_row + radius)


def column_pass(values_in, mats):
    rows, plane_width = values_in.shape
    col_count = plane_width // BW
    grid_cells = values_in.reshape(rows, col_count, BW)
    padded = jnp.pad(grid_cells, ((0, 0), (1, 1), (0, 0)))
    result_sum = jnp.zeros(grid_cells.shape, jnp.float32)
    for position in range(3):
        result_sum = result_sum + jnp.einsum(
            "rcj,jk->rck",
            padded[:, position : position + col_count],
            mats[position],
            preferred_element_type=jnp.float32,
        )
    return result_sum.reshape(rows, plane_width)


def update_plane(estimate, raw_plane, matrix, landing, row_taps, col_taps, level):
    rows, plane_width = estimate.shape
    blocks = (rows // BR) * (plane_width // BW)
    block_iota = jnp.arange(blocks, dtype=jnp.int32)
    rounded = estimate.astype(jnp.bfloat16).reshape(rows, plane_width // BW, BW)
    moved = jnp.einsum("rcj,jk->rck", rounded, matrix, preferred_element_type=jnp.float32)
    moved = moved.astype(jnp.bfloat16).reshape(rows, plane_width)
    gather_mat = landing[None, :] == block_iota[:, None]
    land_count = jnp.sum(gather_mat.astype(jnp.float32), axis=1)
    summed = jnp.dot(
        gather_mat.astype(jnp.bfloat16), to_blocks(moved), preferred_element_type=jnp.float32
    )
    summed = (summed / jnp.maximum(land_count, 1.0)[:, None]).astype(jnp.bfloat16)
    joined = from_blocks(summed, rows, plane_width)
    across = column_pass(joined, column_mats(col_taps, False)).astype(jnp.bfloat16)
    band = row_mat(row_taps, rows)
    blurred = jnp.dot(band, across, preferred_element_type=jnp.float32) + level
    ratio = (raw_plane.astype(jnp.float32) / blurred).astype(jnp.bfloat16)
    rows_back = jnp.dot(band.T, ratio, preferred_element_type=jnp.float32).astype(jnp.bfloat16)
    spread = column_pass(rows_back, column_mats(col_taps, True)).astype(jnp.bfloat16)
    returned = jnp.einsum(
        "rcj,kj->rck",
        spread.reshape(rows, plane_width // BW, BW),
        matrix,
        preferred_element_type=jnp.float32,
    ).astype(jnp.bfloat16)
    correction = jnp.take(to_blocks(returned.reshape(rows, plane_width)), landing, axis=0)
    return estimate * from_blocks(correction, rows, plane_width).astype(jnp.float32)


def plane_kernel(offs_ref, bg_ref, raw_ref, m_ref, mt_ref, s_ref, cnt_ref, g_ref, bf_ref, bb_ref,
                 a_ref, at_ref, *rest):
    *piece_refs, out_ref, est_whole, work, joined, across, ratio = rest
    rows, plane_width = out_ref.shape
    if len(piece_refs) == 1:
        est_ref = piece_refs[0]
    else:
        est_ref = est_whole
        for k, piece in enumerate(piece_refs):
            piece_rows = piece.shape[0]
            est_ref[pl.ds(pl.multiple_of(offs_ref[k], BR), piece_rows), :] = piece[...]
    nt = rows // BR
    nc = plane_width // BW
    f32 = jnp.float32
    bf16 = jnp.bfloat16

    def cols(c):
        return slice(c * BW, (c + 1) * BW)

    def lanes(c):
        return pl.ds(pl.multiple_of(c * BW, BW), BW)

    @pl.loop(0, nc)
    def _(c):
        blk = est_ref[:, lanes(c)].astype(bf16)
        moved = jnp.dot(blk, m_ref[...], preferred_element_type=f32)
        work[c] = moved.astype(bf16).astype(f32)

    def regroup(src, mat_ref, dst, post):
        for r in range(BR):
            stacked = jnp.concatenate(
                [src[c, pl.ds(r, nt, stride=BR), :] for c in range(nc)], axis=0
            )
            result = jnp.dot(mat_ref[...], stacked.astype(bf16), preferred_element_type=f32)
            result = post(result)
            for c in range(nc):
                dst[c, pl.ds(r, nt, stride=BR), :] = result[c * nt:(c + 1) * nt, :]

    regroup(work, s_ref, joined,
            lambda v: (v / cnt_ref[...]).astype(bf16).astype(f32))

    def column_blur(take, mats_ref, c):
        total = None
        for offset in (-1, 0, 1):
            if 0 <= c + offset < nc:
                part = jnp.dot(take(c + offset).astype(bf16), mats_ref[offset + 1],
                               preferred_element_type=f32)
                total = part if total is None else total + part
        return total

    for c in range(nc):
        across[:, cols(c)] = column_blur(lambda i: joined[i], bf_ref, c).astype(bf16)
    level = bg_ref[0]
    for c in range(nc):
        blurred = jnp.dot(a_ref[...], across[:, cols(c)], preferred_element_type=f32) + level
        quotient = (raw_ref[:, cols(c)].astype(f32) / blurred).astype(bf16)
        ratio[:, cols(c)] = jnp.dot(at_ref[...], quotient, preferred_element_type=f32).astype(bf16)
    for c in range(nc):
        spread = column_blur(lambda i: ratio[:, cols(i)], bb_ref, c).astype(bf16)
        back = jnp.dot(spread, mt_ref[...], preferred_element_type=f32)
        work[c] = back.astype(bf16).astype(f32)
    regroup(work, g_ref, joined, lambda v: v)
    @pl.loop(0, nc)
    def _(c):
        out_ref[:, lanes(c)] = est_ref[:, lanes(c)] * joined[c]


def band_kernel(row_ref, col_ref, a_ref, at_ref, bf_ref, bb_ref):
    count, rows, _ = a_ref.shape
    radius = (TAPS - 1) // 2
    out_row = lax.broadcasted_iota(jnp.int32, (rows, rows), 0)
    src_row = lax.broadcasted_iota(jnp.int32, (rows, rows), 1)
    source_lane = lax.broadcasted_iota(jnp.int32, (BW, BW), 0)
    target_lane = lax.broadcasted_iota(jnp.int32, (BW, BW), 1)

    def build(diff, taps_ref, base):
        result = jnp.zeros(diff.shape, jnp.float32)
        for tap_index in range(TAPS):
            result = jnp.where(diff == tap_index, taps_ref[base + tap_index], result)
        return result.astype(jnp.bfloat16)

    @pl.loop(0, count)
    def _(i):
        base = i * TAPS
        a_ref[i] = build(src_row - out_row + radius, row_ref, base)
        at_ref[i] = build(out_row - src_row + radius, row_ref, base)
        for offset in (-1, 0, 1):
            forward = source_lane + offset * BW - target_lane + radius
            bf_ref[i, offset + 1] = build(forward, col_ref, base)
            backward = target_lane - source_lane - offset * BW + radius
            bb_ref[i, offset + 1] = build(backward, col_ref, base)


def all_bands(row_taps, col_taps, rows):
    count = row_taps.shape[0]
    smem = pl.BlockSpec(memory_space=pltpu.SMEM)
    vmem = pl.BlockSpec(memory_space=pltpu.VMEM)
    return pl.pallas_call(
        band_kernel,
        out_shape=(
            jax.ShapeDtypeStruct((count, rows, rows), jnp.bfloat16),
            jax.ShapeDtypeStruct((count, rows, rows), jnp.bfloat16),
            jax.ShapeDtypeStruct((count, 3, BW, BW), jnp.bfloat16),
            jax.ShapeDtypeStruct((count, 3, BW, BW), jnp.bfloat16),
        ),
        in_specs=[smem, smem],
        out_specs=(vmem, vmem, vmem, vmem),
    )(row_taps.astype(jnp.float32).reshape(-1), col_taps.astype(jnp.float32).reshape(-1))


def kernel_update(est_pieces, offsets, raw_all, raw_index, matrix, landing, bands, level):
    rows, plane_width = raw_all.shape[-2:]
    nt = rows // BR
    nc = plane_width // BW
    blocks = nt * nc
    order = landing.reshape(nt, nc).T.reshape(-1)
    place = (order % nc) * nt + order // nc
    spots = jnp.arange(blocks, dtype=jnp.int32)
    sum_mat = place[None, :] == spots[:, None]
    pick_mat = place[:, None] == spots[None, :]
    count = jnp.sum(sum_mat.astype(jnp.float32), axis=1)
    count = jnp.broadcast_to(jnp.maximum(count, 1.0)[:, None], (blocks, BW))
    vmem = pl.BlockSpec(memory_space=pltpu.VMEM)
    smem = pl.BlockSpec(memory_space=pltpu.SMEM)
    raw_spec = pl.BlockSpec((None, None, rows, plane_width), lambda i: raw_index + (0, 0))
    return pl.pallas_call(
        plane_kernel,
        grid=(1,),
        out_shape=jax.ShapeDtypeStruct((rows, plane_width), jnp.float32),
        in_specs=[smem, smem, raw_spec] + [vmem] * (9 + len(est_pieces)),
        out_specs=vmem,
        scratch_shapes=[
            pltpu.VMEM((rows, plane_width), jnp.float32),
            pltpu.VMEM((nc, rows, BW), jnp.float32),
            pltpu.VMEM((nc, rows, BW), jnp.float32),
            pltpu.VMEM((rows, plane_width), jnp.bfloat16),
            pltpu.VMEM((rows, plane_width), jnp.bfloat16),
        ],
        compiler_params=pltpu.CompilerParams(vmem_limit_bytes=48 * 1024 * 1024),
        cost_estimate=pl.CostEstimate(
            flops=2 * rows * plane_width * (4 * BW + 2 * rows + 2 * blocks // BR * BR),
            bytes_accessed=rows * plane_width * 10,
            transcendentals=0,
        ),
    )(
        offsets,
        jnp.reshape(level, (1,)).astype(jnp.float32),
        raw_all,
        matrix,
        matrix.T,
        sum_mat.astype(jnp.bfloat16),
        count,
        pick_mat.astype(jnp.bfloat16),
        bands[2],
        bands[3],
        bands[0],
        bands[1],
        *est_pieces,
    )


def with_halo(cells, sides, width):
    for axis, dim in sides:
        count = lax.axis_size(axis)
        ends = count - 1
        head = lax.slice_in_dim(cells, 0, width, axis=dim)
        tail = lax.slice_in_dim(cells, cells.shape[dim] - width, cells.shape[dim], axis=dim)
        cells = jnp.concatenate(
            [
                lax.ppermute(tail, axis, [(i, (i + 1) % count) for i in range(ends)]),
                cells,
                lax.ppermute(head, axis, [((i + 1) % count, i) for i in range(ends)]),
            ],
            axis=dim,
        )
    return cells


def sharded_to_blocks(values_in):
    planes, tile_rows, plane_width = values_in.shape
    shaped = values_in.reshape(planes, tile_rows // BR, BR, plane_width // BW, BW)
    return shaped.transpose(1, 3, 0, 2, 4).reshape(-1, planes, BR, BW)


def sharded_from_blocks(pieces, tile_rows, plane_width):
    planes = pieces.shape[1]
    shaped = pieces.reshape(tile_rows // BR, plane_width // BW, planes, BR, BW)
    return shaped.transpose(2, 0, 3, 1, 4).reshape(planes, tile_rows, plane_width)


def sharded_column_pass(values_in, taps_in, flipped):
    planes, tile_rows, plane_width = values_in.shape
    radius = (taps_in.shape[1] - 1) // 2
    lane_iota = jnp.arange(BW, dtype=jnp.int32)
    source_lane = lane_iota[:, None]
    target_lane = lane_iota[None, :]
    zero_bf = jnp.zeros((), jnp.bfloat16)
    band_mats = []
    for offset in (-1, 0, 1):
        if flipped:
            tap_index = target_lane - source_lane - offset * BW + radius
        else:
            tap_index = source_lane + offset * BW - target_lane + radius
        inside = (tap_index >= 0) & (tap_index <= 2 * radius)
        picked = taps_in[:, jnp.clip(tap_index, 0, 2 * radius)]
        band_mats.append(jnp.where(inside[None, :, :], picked, zero_bf))
    col_count = plane_width // BW
    grid_cells = values_in.reshape(planes, tile_rows, col_count, BW)
    padded = jnp.pad(grid_cells, ((0, 0), (0, 0), (1, 1), (0, 0)))
    result_sum = jnp.zeros(grid_cells.shape, jnp.float32)
    for position in range(3):
        result_sum = result_sum + jnp.einsum(
            "prcj,pjk->prck",
            padded[:, :, position : position + col_count],
            band_mats[position],
            preferred_element_type=jnp.float32,
        )
    return result_sum.reshape(planes, tile_rows, plane_width)


def row_pass(padded, taps_in, flipped):
    planes, extended, plane_width = padded.shape
    radius = (taps_in.shape[1] - 1) // 2
    tile_rows = extended - 2 * radius
    row_iota = jnp.arange(tile_rows, dtype=jnp.int32)[:, None]
    src_iota = jnp.arange(extended, dtype=jnp.int32)[None, :]
    if flipped:
        tap_index = row_iota + 2 * radius - src_iota
    else:
        tap_index = src_iota - row_iota
    inside = (tap_index >= 0) & (tap_index <= 2 * radius)
    band_rows = jnp.where(
        inside[None, :, :],
        taps_in[:, jnp.clip(tap_index, 0, 2 * radius)],
        jnp.zeros((), jnp.bfloat16),
    )
    return jnp.einsum("prs,psw->prw", band_rows, padded, preferred_element_type=jnp.float32)


def sharded_update(
    estimate,
    raw_piece,
    view_index,
    slab_index,
    route_tile,
    route_block,
    interp,
    row_psf,
    col_psf,
    psf_band,
    background,
):
    tile_count = lax.axis_size("tile")
    my_tile = lax.axis_index("tile")
    planes, tile_rows, plane_width = estimate.shape
    blocks = tile_rows // BR * (plane_width // BW)
    capacity = max(2, 2 * blocks // tile_count)
    radius = (TAPS - 1) // 2
    matrix = interp[view_index]
    dest_tile = route_tile[view_index, :, 0].reshape(tile_count, blocks)
    dest_block = route_block[view_index].reshape(tile_count, blocks)
    tiles_iota = jnp.arange(tile_count, dtype=jnp.int32)
    one_hot = (dest_tile[:, :, None] == tiles_iota[None, None, :]).astype(jnp.int32)
    slot_rank = jnp.sum((jnp.cumsum(one_hot, axis=1) - one_hot) * one_hot, axis=2)
    slot_index = dest_tile * capacity + slot_rank
    my_slots = slot_index[my_tile]
    slots_iota = jnp.arange(tile_count * capacity, dtype=jnp.int32)
    block_iota = jnp.arange(blocks, dtype=jnp.int32)
    match_send = my_slots[None, :] == slots_iota[:, None]
    send_ok = jnp.any(match_send, axis=1)
    send_src = jnp.sum(jnp.where(match_send, block_iota[None, :], 0), axis=1)
    match_recv = (dest_tile == my_tile)[:, None, :] & (
        slot_rank[:, None, :] == jnp.arange(capacity, dtype=jnp.int32)[None, :, None]
    )
    recv_ok = jnp.any(match_recv, axis=2).reshape(-1)
    recv_off = jnp.sum(jnp.where(match_recv, dest_block[:, None, :], 0), axis=2).reshape(-1)
    zero_bf = jnp.zeros((), jnp.bfloat16)
    rounded_estimate = estimate.astype(jnp.bfloat16)
    interpolated = jnp.einsum(
        "bprj,jk->bprk", sharded_to_blocks(rounded_estimate), matrix, preferred_element_type=jnp.float32
    ).astype(jnp.bfloat16)
    outgoing = jnp.where(send_ok[:, None, None, None], interpolated[send_src], zero_bf)
    outgoing = outgoing.reshape(tile_count, capacity, planes, BR, BW)
    incoming = lax.all_to_all(outgoing, "tile", split_axis=0, concat_axis=0, tiled=True)
    incoming = incoming.reshape(tile_count * capacity, planes * BR * BW)
    landing = (recv_off[None, :] == block_iota[:, None]) & recv_ok[None, :]
    land_count = jnp.sum(landing.astype(jnp.float32), axis=1)
    summed = jnp.dot(landing.astype(jnp.bfloat16), incoming, preferred_element_type=jnp.float32)
    summed = (summed / jnp.maximum(land_count, 1.0)[:, None]).astype(jnp.bfloat16)
    joined_field = sharded_from_blocks(summed.reshape(blocks, planes, BR, BW), tile_rows, plane_width)
    plane_bands = lax.dynamic_slice_in_dim(psf_band, slab_index * planes, planes, 0)
    row_taps = row_psf[view_index][plane_bands]
    col_taps = col_psf[view_index][plane_bands]
    across = sharded_column_pass(joined_field, col_taps, False).astype(jnp.bfloat16)
    padded = with_halo(across, (("tile", 1),), radius)
    blurred = row_pass(padded, row_taps, False) + background[view_index]
    ratio_field = (raw_piece.astype(jnp.float32) / blurred).astype(jnp.bfloat16)
    padded_ratio = with_halo(ratio_field, (("tile", 1),), radius)
    rows_back = row_pass(padded_ratio, row_taps, True).astype(jnp.bfloat16)
    spread = sharded_column_pass(rows_back, col_taps, True).astype(jnp.bfloat16)
    returned_blocks = jnp.einsum(
        "bprj,kj->bprk", sharded_to_blocks(spread), matrix, preferred_element_type=jnp.float32
    ).astype(jnp.bfloat16)
    returning = jnp.where(recv_ok[:, None, None, None], returned_blocks[recv_off], zero_bf)
    returning = returning.reshape(tile_count, capacity, planes, BR, BW)
    arrived = lax.all_to_all(returning, "tile", split_axis=0, concat_axis=0, tiled=True)
    arrived = arrived.reshape(tile_count * capacity, planes, BR, BW)
    correction = arrived[my_slots]
    return estimate * sharded_from_blocks(correction.astype(jnp.float32), tile_rows, plane_width)


def local(
    initial_estimate,
    raw_views,
    route_tile,
    route_block,
    interp,
    row_kernel,
    col_kernel,
    psf_band,
    background,
):
    view_count = lax.axis_size("view")
    my_group = lax.axis_index("view")
    my_tile = lax.axis_index("tile")
    planes, tile_rows, plane_width = initial_estimate.shape
    tile_blocks = (tile_rows // BR) * (plane_width // BW)
    row_psf = (row_kernel / jnp.sum(row_kernel, axis=2, keepdims=True)).astype(jnp.bfloat16)
    col_psf = (col_kernel / jnp.sum(col_kernel, axis=2, keepdims=True)).astype(jnp.bfloat16)
    if view_count * tile_rows * plane_width * lax.axis_size("tile") > (1 << 22):
        estimate = initial_estimate
        for update_index in range(view_count):
            view_index = (my_group + update_index) % view_count
            own_piece = lax.dynamic_slice_in_dim(
                raw_views[0], (my_group - update_index) % view_count * planes, planes, 0
            )
            raw_piece = (
                own_piece if update_index == 0 else passed_along(own_piece, "view", -update_index)
            )
            estimate = sharded_update(
                estimate, raw_piece, view_index, my_group, route_tile, route_block,
                interp, row_psf, col_psf, psf_band, background,
            )
        return estimate
    pieces = []
    for update_index in range(view_count):
        own_piece = lax.dynamic_slice_in_dim(
            raw_views[0], (my_group - update_index) % view_count * planes, planes, 0
        )
        piece = own_piece if update_index == 0 else passed_along(own_piece, "view", -update_index)
        pieces.append(piece)
    first_raw = lax.all_gather(jnp.stack(pieces[:1]), "tile", axis=2, tiled=True)
    later_raw = lax.all_gather(jnp.stack(pieces[1:]), "tile", axis=2, tiled=True)
    tile_count = lax.axis_size("tile")
    along = [initial_estimate] + [
        passed_along(initial_estimate, "tile", shift) for shift in range(2, tile_count, 2)
    ]
    partner = [(i, i ^ 1) for i in range(tile_count)]
    arrived = along + [lax.ppermute(piece, "tile", partner) for piece in along]
    sources = [(my_tile - shift) % tile_count for shift in range(0, tile_count, 2)]
    sources = sources + [(source ^ 1) for source in sources]
    offsets = jnp.stack(sources).astype(jnp.int32) * tile_rows
    whole_plane = jnp.zeros((1,), jnp.int32)
    plane_bands = lax.dynamic_slice_in_dim(psf_band, my_group * planes, planes, 0)
    views_in_order = (my_group + jnp.arange(view_count, dtype=jnp.int32)) % view_count
    bands = all_bands(
        row_psf[views_in_order][:, plane_bands].reshape(view_count * planes, TAPS),
        col_psf[views_in_order][:, plane_bands].reshape(view_count * planes, TAPS),
        tile_rows * lax.axis_size("tile"),
    )
    for update_index in range(view_count):
        view_index = (my_group + update_index) % view_count
        matrix = interp[view_index]
        landing = route_tile[view_index, :, 0] * tile_blocks + route_block[view_index]
        level = background[view_index]
        estimate = jnp.stack(
            [
                kernel_update(
                    [piece[p] for piece in arrived] if update_index == 0 else [estimate[p]],
                    offsets if update_index == 0 else whole_plane,
                    first_raw if update_index == 0 else later_raw,
                    (0 if update_index == 0 else update_index - 1, p),
                    matrix,
                    landing,
                    [b[update_index * planes + p] for b in bands],
                    level,
                )
                for p in range(planes)
            ]
        )
    return lax.dynamic_slice_in_dim(estimate, my_tile * tile_rows, tile_rows, 1)


def solution(mesh):
    return jax.shard_map(
        local,
        mesh=mesh,
        in_specs=(
            P("view", "tile", None),
            P("view", None, "tile", None),
            P(),
            P(),
            P(),
            P(),
            P(),
            P(),
            P(),
        ),
        out_specs=P("view", "tile", None),
        check_vma=False,
    )
```
